32 devices in a mesh: ctx: 8 (over z, core), head: 4 (over y, x).
Axes of the slice: x: 2, y: 2, z: 4, core: 2. Of those that a mesh axis runs over, the one named last changes fastest.
Arguments:
- lin_query: bfloat16 [2048, 8192], P('ctx', 'head'), may hold values from -6 to 6
- lin_key: bfloat16 [2048, 8192], P('ctx', 'head'), may hold values from -6 to 6
- lin_value: bfloat16 [2048, 8192], P('ctx', 'head'), may hold values from -6 to 6
- norm_gain: float32 [8192], P('head'), may hold values from 0.1 to 1.9
- soft_query: bfloat16 [2048, 8192], P(('ctx', 'head')), may hold values from -180 to 180
- soft_key: bfloat16 [2048, 1024], P(('ctx', 'head')), may hold values from -6.2 to 6.2
- soft_value: bfloat16 [2048, 1024], P(('ctx', 'head')), may hold values from -6 to 6
- doc_lengths: int32 [4], replicated, may hold values from 1 to 768, 2048 in all
Outputs:
- lightning_out: bfloat16 [2048, 8192], P('ctx', 'head')
- attended: bfloat16 [2048, 8192], P('ctx', 'head')
The draws below stay inside these ranges and needn't reach their ends.
Inputs may be any that keep to these rules, and one draw needn't show every extreme that they name: `doc_lengths`: 4 documents whose lengths sum to 2048.
All inputs are finite; a program needn't handle non-finite values.
Results may differ from the reference program's by a relative error of at most 0.0037.
Values may be sent and summed in bfloat16 or wider, within the bound.
No kernel may reach another device: no remote copies, remote signals or barrier semaphores. Data moves between devices by JAX's collectives and lax.ppermute only.
A program may use at most 64 MiB of HBM per device.

```python
import math
import jax
import jax.numpy as jnp
import numpy as np
from jax import lax

HEADS = 64
HD = 128
KV_HEADS = 8
TOK_DEV = 256
SPAN = 3
GROUP = 8
TOKENS = 2048
NDOCS = 4


def paired_fields(key):
    query_seed = jax.random.fold_in(key, 11)
    key_seed = jax.random.fold_in(key, 12)
    keys_drawn = jax.random.truncated_normal(key_seed, -6.0, 6.0, (TOKENS, KV_HEADS * HD), jnp.float32)
    queries_drawn = jax.random.truncated_normal(query_seed, -6.0, 6.0, (TOKENS, HEADS * HD), jnp.float32)
    return (queries_drawn, keys_drawn)


def draw_soft_query(key, part):
    return paired_fields(key)[0].astype(jnp.bfloat16)


def draw_soft_key(key, part):
    return paired_fields(key)[1].astype(jnp.bfloat16)


def level_of(stream_key, dims, cuts, smallest, high):
    loudness = 1.0
    for axis_at, blocks in cuts:
        steps = jax.random.uniform(jax.random.fold_in(jax.random.fold_in(stream_key, 6), axis_at), (blocks,), jnp.float32, smallest / len(cuts), high / len(cuts))
        loudness = loudness * jnp.repeat(jnp.exp(steps), dims[axis_at] // blocks).reshape((-1,) + (1,) * (len(dims) - 1 - axis_at))
    return loudness


def length_profile(number_of, total, bound, slope):
    weights = [(1 << 20) // math.isqrt(rank ** slope) + 1 for rank in range(2, number_of + 1)]
    spare, holding = total - bound - (number_of - 1), [1] * (number_of - 1)
    while spare > 0:
        free = [i for i in range(number_of - 1) if holding[i] < bound]
        pool, left = sum([weights[i] for i in free]), spare
        for i in free:
            addition = min(bound - holding[i], max(1, left * weights[i] // pool), spare)
            holding[i] = holding[i] + addition
            spare = spare - addition
    return np.array([bound] + holding)


def uneven(rng, amount, total, most, skew):
    if amount == 2:
        one = jax.random.randint(rng, (), max(1, total - most), min(most, total - 1) + 1)
        return jnp.stack([one, total - one])
    tallies = jnp.asarray(length_profile(amount, total, most, skew), jnp.int32)
    twos = (amount - 1) // 2
    donor, taker = tallies[1:1 + 2 * twos:2], tallies[2:2 + 2 * twos:2]
    slack = jnp.minimum(donor - 1, most - taker)
    passed = jax.random.randint(jax.random.fold_in(rng, 1), (twos,), 0, 1 << 20) % (slack + 1)
    tallies = tallies.at[1:1 + 2 * twos:2].set(donor - passed).at[2:2 + 2 * twos:2].set(taker + passed)
    return tallies[jax.random.permutation(jax.random.fold_in(rng, 2), amount)]


def centred(stream_key, extent, scale, limit, shards=(), held_as=jnp.bfloat16):
    entries = jax.random.normal(stream_key, extent, jnp.float32) * scale
    if len(shards) > 0:
        entries = level_of(stream_key, extent, shards, -0.22, 0.18) * entries
    return jnp.clip(entries, min=-limit, max=limit).astype(held_as)


def setup_inputs(seed: int = 0) -> dict:
    streams_of = jax.random.split(jax.random.key(seed), 9)
    return {
        "lin_query": centred(streams_of[0], (TOKENS, HEADS * HD), 1.0, 6.0, ((0, 8), (1, 4))),
        "lin_key": centred(streams_of[1], (TOKENS, HEADS * HD), 1.0, 6.0, ((0, 8), (1, 4))),
        "lin_value": centred(streams_of[2], (TOKENS, HEADS * HD), 1.0, 6.0, ((0, 8), (1, 4))),
        "norm_gain": jnp.clip(1.0 + 0.18 * jax.random.normal(streams_of[3], (HEADS * HD,), jnp.float32), 0.1, 1.9),
        "soft_query": draw_soft_query(jax.random.fold_in(streams_of[8], 71), 0),
        "soft_key": draw_soft_key(jax.random.fold_in(streams_of[8], 71), 0),
        "soft_value": centred(streams_of[6], (TOKENS, KV_HEADS * HD), 1.0, 6.0, ((0, 32),)),
        "doc_lengths": uneven(streams_of[7], NDOCS, TOKENS, SPAN * TOK_DEV, 1).astype(jnp.int32),
    }


def document_index(doc_lengths, positions):
    doc_ends = jnp.cumsum(doc_lengths).astype(jnp.int32)
    counted = lax.optimization_barrier(jnp.sum((positions[:, None] >= doc_ends[None, :]).astype(jnp.int32), axis=1)).astype(jnp.int32)
    return jnp.where(positions < 0, -1, counted).astype(jnp.int32)

def reference(lin_query, lin_key, lin_value, norm_gain, soft_query, soft_key, soft_value, doc_lengths):
    positions = jnp.arange(TOKENS, dtype=jnp.int32)
    documents = document_index(doc_lengths, positions)
    margin = SPAN * TOK_DEV
    window = margin + TOK_DEV
    padded_docs = jnp.concatenate([jnp.full((margin,), -1, jnp.int32), documents])
    scale = 1.0 / math.sqrt(HD)
    highest = lax.Precision.HIGHEST

    def heads_of(field):
        return field.reshape(TOKENS, HEADS, HD)

    def padded3(field3):
        return jnp.concatenate([jnp.zeros((margin, field3.shape[1], HD), field3.dtype), field3])
    lin_q3 = heads_of(lin_query)
    lin_k3 = padded3(heads_of(lin_key))
    lin_v3 = padded3(heads_of(lin_value))
    soft_q3 = heads_of(soft_query)
    soft_k3 = padded3(soft_key.reshape(TOKENS, KV_HEADS, HD))
    soft_v3 = padded3(soft_value.reshape(TOKENS, KV_HEADS, HD))
    gain_table = norm_gain.reshape(HEADS, HD)

    def block(index):
        start = (index * TOK_DEV).astype(jnp.int32)
        query_docs = lax.dynamic_slice_in_dim(documents, start, TOK_DEV)
        key_docs = lax.dynamic_slice_in_dim(padded_docs, start, window)
        query_pos = start + jnp.arange(TOK_DEV, dtype=jnp.int32)
        key_pos = start - margin + jnp.arange(window, dtype=jnp.int32)
        visible = (query_docs[:, None] == key_docs[None, :]) & (key_pos[None, :] <= query_pos[:, None])
        lin_qb = lax.dynamic_slice_in_dim(lin_q3, start, TOK_DEV, 0).astype(jnp.float32)
        lin_kb = lax.dynamic_slice_in_dim(lin_k3, start, window, 0).astype(jnp.float32)
        lin_vb = lax.dynamic_slice_in_dim(lin_v3, start, window, 0).astype(jnp.float32)
        lin_scores = jnp.einsum('qhd,khd->hqk', lin_qb, lin_kb, precision=highest)
        lin_scores = jnp.where(visible[None], lin_scores, 0.0)
        lin = jnp.einsum('hqk,khd->qhd', lin_scores, lin_vb, precision=highest)
        normed = lin * lax.rsqrt(lax.optimization_barrier(jnp.mean(lin * lin, axis=-1, keepdims=True)) + 1e-06) * gain_table
        soft_qb = lax.dynamic_slice_in_dim(soft_q3, start, TOK_DEV, 0).astype(jnp.float32)
        soft_kb = jnp.repeat(lax.dynamic_slice_in_dim(soft_k3, start, window, 0).astype(jnp.float32), GROUP, axis=1)
        soft_vb = jnp.repeat(lax.dynamic_slice_in_dim(soft_v3, start, window, 0).astype(jnp.float32), GROUP, axis=1)
        scores = jnp.einsum('qhd,khd->hqk', soft_qb, soft_kb, precision=highest) * scale
        scores = jnp.where(visible[None], scores, -1e+30)
        largest = lax.optimization_barrier(jnp.max(scores, axis=-1, keepdims=True))
        weights = jnp.exp(scores - largest)
        total = lax.optimization_barrier(jnp.sum(weights, axis=-1, keepdims=True))
        probs = weights.astype(jnp.bfloat16).astype(jnp.float32)
        summed = jnp.einsum('hqk,khd->qhd', probs, soft_vb, precision=highest)
        result = summed / jnp.transpose(total, (1, 0, 2))
        return (normed.astype(jnp.bfloat16), result.astype(jnp.bfloat16))
    normed_all, attended_all = lax.map(block, jnp.arange(TOKENS // TOK_DEV, dtype=jnp.int32))
    return (normed_all.reshape(TOKENS, HEADS * HD), attended_all.reshape(TOKENS, HEADS * HD))
```

```python
import math

import jax
import jax.numpy as jnp
import numpy as np
from jax import lax
from jax.experimental import pallas as pl
from jax.experimental.pallas import tpu as pltpu
from jax.sharding import PartitionSpec as P

HEADS = 64
HD = 128
KV_HEADS = 8
SPAN = 3

F32 = jnp.float32
BF16 = jnp.bfloat16


def document_index(doc_lengths, positions):
    doc_ends = jnp.cumsum(doc_lengths)
    counted = jnp.sum((positions[:, None] >= doc_ends[None, :]).astype(jnp.int32), axis=1)
    return jnp.where(positions < 0, -1, counted).astype(jnp.int32)


def from_behind(value, axis, steps):
    count = lax.axis_size(axis)
    pairs = [(source, source + steps) for source in range(0, count - steps)]
    if not pairs:
        return jnp.zeros_like(value)
    return lax.ppermute(value, axis, pairs)


def split_bf16(x):
    hi = x.astype(BF16)
    lo = (x - hi.astype(F32)).astype(BF16)
    return hi, lo


def dot_nt(a, b):
    return lax.dot_general(a, b, (((1,), (1,)), ((), ())), preferred_element_type=F32)


def tail_kernel(mask_ref, k_ref, v_ref, t_ref):
    masked = v_ref[...] * mask_ref[...]
    t_ref[0] = lax.dot_general(
        k_ref[...], masked, (((0,), (0,)), ((), ())), preferred_element_type=F32
    )


def lin_local_kernel(dq_ref, dk_ref, q_ref, k_ref, v_ref, lin_ref):
    rows = q_ref.shape[0]
    scores = dot_nt(q_ref[...], k_ref[...])
    row = lax.broadcasted_iota(jnp.int32, (rows, rows), 0)
    col = lax.broadcasted_iota(jnp.int32, (rows, rows), 1)
    visible = (dq_ref[...] == dk_ref[...]) & (col <= row)
    scores = jnp.where(visible, scores, 0.0)
    hi, lo = split_bf16(scores)
    v = v_ref[...]
    lin_ref[...] = jnp.dot(hi, v, preferred_element_type=F32) + jnp.dot(
        lo, v, preferred_element_type=F32
    )


def lin_finish_kernel(sees_ref, q_ref, c_ref, lin_ref, g_ref, o_ref):
    hi, lo = split_bf16(c_ref[0])
    q = q_ref[...]
    carried = jnp.dot(q, hi, preferred_element_type=F32) + jnp.dot(
        q, lo, preferred_element_type=F32
    )
    lin = lin_ref[...] + carried * sees_ref[...]
    mean_sq = jnp.mean(lin * lin, axis=-1, keepdims=True)
    o_ref[...] = (lin * lax.rsqrt(mean_sq + 1e-06) * g_ref[...]).astype(o_ref.dtype)


def col_spec(rows):
    return pl.BlockSpec((rows, HD), lambda h: (0, h))


def full_spec(shape):
    return pl.BlockSpec(shape, lambda h: (0,) * len(shape))


def params():
    return pltpu.CompilerParams(dimension_semantics=("arbitrary",))


def soft_kernel(blocks, dq_ref, dk_ref, q_ref, *rest):
    key_refs = rest[0:blocks]
    value_refs = rest[blocks : 2 * blocks]
    o_ref = rest[2 * blocks]
    q = q_ref[...]
    rows = q.shape[0]
    scale = 1.0 / math.sqrt(HD)
    dq = dq_ref[...]
    row = lax.broadcasted_iota(jnp.int32, (rows, rows), 0)
    col = lax.broadcasted_iota(jnp.int32, (rows, rows), 1)
    scores = []
    for m in range(blocks):
        s = dot_nt(q, key_refs[m][...]) * scale
        visible = dq == dk_ref[m : m + 1, :]
        if m == 0:
            visible = visible & (col <= row)
        scores.append(jnp.where(visible, s, -1e30))
    largest = jnp.max(scores[0], axis=-1, keepdims=True)
    for s in scores[1:]:
        largest = jnp.maximum(largest, jnp.max(s, axis=-1, keepdims=True))
    total = None
    summed = None
    for m in range(blocks):
        weights = jnp.exp(scores[m] - largest)
        part = jnp.sum(weights, axis=-1, keepdims=True)
        term = jnp.dot(weights.astype(BF16), value_refs[m][...], preferred_element_type=F32)
        total = part if total is None else total + part
        summed = term if summed is None else summed + term
    o_ref[...] = (summed / total).astype(o_ref.dtype)


def body(lin_query, lin_key, lin_value, norm_gain, soft_query, soft_key, soft_value, doc_lengths):
    rows, width = lin_query.shape
    local_heads = width // HD
    shard_index = lax.axis_index("ctx")
    shard_start = shard_index * rows
    offsets = jnp.arange(rows, dtype=jnp.int32)
    own_docs = document_index(doc_lengths, shard_start + offsets)
    edges = document_index(
        doc_lengths,
        jnp.stack(
            [
                shard_start - 1,
                shard_start + rows - 1,
                shard_start - rows - 1,
                shard_start - 2 * rows - 1,
            ]
        ),
    )
    before_doc, last_doc, before1, before2 = edges[0], edges[1], edges[2], edges[3]

    head_devices = lax.axis_size("head")
    group_size = HEADS // KV_HEADS
    per_device = HEADS // head_devices
    kv_local = max(1, per_device // group_size)
    kv_table = (
        np.arange(head_devices)[:, None] * per_device // group_size + np.arange(kv_local)[None, :]
    ).reshape(-1)
    short_rows = soft_key.shape[0]

    def spread(field):
        if np.array_equal(kv_table, np.arange(KV_HEADS)):
            return field.reshape(short_rows, head_devices, kv_local * HD)
        taken = jnp.take(field.reshape(short_rows, KV_HEADS, HD), kv_table, axis=1)
        return taken.reshape(short_rows, head_devices, kv_local * HD)

    packed = jnp.concatenate(
        [
            soft_query.reshape(short_rows, head_devices, per_device * HD),
            spread(soft_key),
            spread(soft_value),
        ],
        axis=2,
    )
    per_dest = packed.shape[2]
    packed = packed.reshape(short_rows, head_devices * per_dest)
    mixed = lax.all_to_all(packed, "head", split_axis=1, concat_axis=0, tiled=True)
    own_kv = mixed[:, per_device * HD :]
    older = [from_behind(own_kv, "ctx", step) for step in range(1, SPAN + 1)]

    tail_mask = (own_docs == last_doc).astype(BF16)[:, None]
    tail = pl.pallas_call(
        tail_kernel,
        out_shape=jax.ShapeDtypeStruct((local_heads, HD, HD), F32),
        grid=(local_heads,),
        in_specs=[full_spec((rows, 1)), col_spec(rows), col_spec(rows)],
        out_specs=pl.BlockSpec((1, HD, HD), lambda h: (h, 0, 0)),
        compiler_params=params(),
        cost_estimate=pl.CostEstimate(
            flops=2 * rows * HD * HD * local_heads,
            transcendentals=0,
            bytes_accessed=2 * rows * width * 2 + local_heads * HD * HD * 4,
        ),
    )(tail_mask, lin_key, lin_value)
    tails = [from_behind(tail, "ctx", step) for step in range(1, SPAN + 1)]

    lin_local = pl.pallas_call(
        lin_local_kernel,
        out_shape=jax.ShapeDtypeStruct((rows, width), F32),
        grid=(local_heads,),
        in_specs=[
            full_spec((rows, 1)),
            full_spec((1, rows)),
            col_spec(rows),
            col_spec(rows),
            col_spec(rows),
        ],
        out_specs=col_spec(rows),
        compiler_params=params(),
        cost_estimate=pl.CostEstimate(
            flops=6 * rows * rows * HD * local_heads,
            transcendentals=0,
            bytes_accessed=3 * rows * width * 2 + rows * width * 4,
        ),
    )(own_docs[:, None], own_docs[None, :], lin_query, lin_key, lin_value)

    key_docs = jnp.stack(
        [
            document_index(doc_lengths, (shard_index - step) * rows + offsets)
            for step in range(SPAN + 1)
        ]
    )
    kv_index = lambda h: (h * kv_local) // per_device
    own_k_spec = pl.BlockSpec((rows, HD), lambda h: (0, per_device + kv_index(h)))
    own_v_spec = pl.BlockSpec((rows, HD), lambda h: (0, per_device + kv_local + kv_index(h)))
    old_k_spec = pl.BlockSpec((rows, HD), lambda h: (0, kv_index(h)))
    old_v_spec = pl.BlockSpec((rows, HD), lambda h: (0, kv_local + kv_index(h)))
    blocks = SPAN + 1
    attended = pl.pallas_call(
        lambda *refs: soft_kernel(blocks, *refs),
        out_shape=jax.ShapeDtypeStruct((rows, per_device * HD), BF16),
        grid=(per_device,),
        in_specs=[full_spec((rows, 1)), full_spec((blocks, rows)), col_spec(rows)]
        + [own_k_spec]
        + [old_k_spec] * SPAN
        + [own_v_spec]
        + [old_v_spec] * SPAN,
        out_specs=col_spec(rows),
        compiler_params=params(),
        cost_estimate=pl.CostEstimate(
            flops=4 * rows * rows * blocks * HD * per_device,
            transcendentals=rows * rows * blocks * per_device,
            bytes_accessed=rows * per_device * HD * 4 + 2 * blocks * rows * HD * 2 * per_device,
        ),
    )(own_docs[:, None], key_docs, mixed, mixed, *older, mixed, *older)

    through1 = (before1 == before_doc).astype(F32)
    through2 = (before2 == before1).astype(F32)
    carried = tails[0] + through1 * (tails[1] + through2 * tails[2])
    sees_carry = (own_docs == before_doc).astype(F32)[:, None]
    lightning_out = pl.pallas_call(
        lin_finish_kernel,
        out_shape=jax.ShapeDtypeStruct((rows, width), BF16),
        grid=(local_heads,),
        in_specs=[
            full_spec((rows, 1)),
            col_spec(rows),
            pl.BlockSpec((1, HD, HD), lambda h: (h, 0, 0)),
            col_spec(rows),
            pl.BlockSpec((1, HD), lambda h: (0, h)),
        ],
        out_specs=col_spec(rows),
        compiler_params=params(),
        cost_estimate=pl.CostEstimate(
            flops=4 * rows * HD * HD * local_heads,
            transcendentals=rows * local_heads,
            bytes_accessed=rows * width * (2 + 4 + 2) + local_heads * HD * HD * 4,
        ),
    )(sees_carry, lin_query, carried, lin_local, norm_gain.reshape(1, width))
    return (lightning_out, attended)


def solution(mesh):
    placed = (
        P("ctx", "head"),
        P("ctx", "head"),
        P("ctx", "head"),
        P("head"),
        P(("ctx", "head"), None),
        P(("ctx", "head"), None),
        P(("ctx", "head"), None),
        P(),
    )
    return jax.shard_map(
        body,
        mesh=mesh,
        in_specs=placed,
        out_specs=(P("ctx", "head"), P("ctx", "head")),
        check_vma=False,
    )
```

```python
import math

import jax
import jax.numpy as jnp
import numpy as np
from jax import lax
from jax.experimental import pallas as pl
from jax.experimental.pallas import tpu as pltpu
from jax.sharding import PartitionSpec as P

HEADS = 64
HD = 128
KV_HEADS = 8
SPAN = 3

F32 = jnp.float32
BF16 = jnp.bfloat16


def document_index(doc_lengths, positions):
    doc_ends = jnp.cumsum(doc_lengths)
    counted = jnp.sum((positions[:, None] >= doc_ends[None, :]).astype(jnp.int32), axis=1)
    return jnp.where(positions < 0, -1, counted).astype(jnp.int32)


def from_behind(value, axis, steps):
    count = lax.axis_size(axis)
    pairs = [(source, source + steps) for source in range(0, count - steps)]
    if not pairs:
        return jnp.zeros_like(value)
    return lax.ppermute(value, axis, pairs)


def split_bf16(x):
    hi = x.astype(BF16)
    lo = (x - hi.astype(F32)).astype(BF16)
    return hi, lo


def dot_nt(a, b):
    return lax.dot_general(a, b, (((1,), (1,)), ((), ())), preferred_element_type=F32)


def head_cols(j):
    return slice(j * HD, (j + 1) * HD)


def tail_kernel(hpb, mask_ref, k_ref, v_ref, t_ref):
    mask = mask_ref[...]
    for j in range(hpb):
        masked = v_ref[:, head_cols(j)] * mask
        t_ref[j] = lax.dot_general(
            k_ref[:, head_cols(j)], masked, (((0,), (0,)), ((), ())), preferred_element_type=F32
        )


def lin_local_kernel(hpb, dq_ref, dk_ref, q_ref, k_ref, v_ref, lin_ref):
    rows = q_ref.shape[0]
    row = lax.broadcasted_iota(jnp.int32, (rows, rows), 0)
    col = lax.broadcasted_iota(jnp.int32, (rows, rows), 1)
    visible = (dq_ref[...] == dk_ref[...]) & (col <= row)
    for j in range(hpb):
        scores = dot_nt(q_ref[:, head_cols(j)], k_ref[:, head_cols(j)])
        scores = jnp.where(visible, scores, 0.0)
        hi, lo = split_bf16(scores)
        v = v_ref[:, head_cols(j)]
        lin_ref[:, head_cols(j)] = jnp.dot(hi, v, preferred_element_type=F32) + jnp.dot(
            lo, v, preferred_element_type=F32
        )


def lin_finish_kernel(hpb, sees_ref, q_ref, c_ref, lin_ref, g_ref, o_ref):
    sees = sees_ref[...]
    for j in range(hpb):
        hi, lo = split_bf16(c_ref[j])
        q = q_ref[:, head_cols(j)]
        carried = jnp.dot(q, hi, preferred_element_type=F32) + jnp.dot(
            q, lo, preferred_element_type=F32
        )
        lin = lin_ref[:, head_cols(j)] + carried * sees
        mean_sq = jnp.mean(lin * lin, axis=-1, keepdims=True)
        normed = lin * lax.rsqrt(mean_sq + 1e-06) * g_ref[:, head_cols(j)]
        o_ref[:, head_cols(j)] = normed.astype(o_ref.dtype)


def col_spec(rows, width=HD):
    return pl.BlockSpec((rows, width), lambda h: (0, h))


def full_spec(shape):
    return pl.BlockSpec(shape, lambda h: (0,) * len(shape))


def params():
    return pltpu.CompilerParams(dimension_semantics=("arbitrary",))


def soft_kernel(blocks, hpb, need_ref, bias_ref, q_ref, *rest):
    key_refs = rest[0:blocks]
    value_refs = rest[blocks : 2 * blocks]
    o_ref = rest[2 * blocks]
    s_ref, mx_ref, tot_ref, acc_ref = rest[2 * blocks + 1 :]
    scale = 1.0 / math.sqrt(HD)
    for j in range(hpb):
        q = q_ref[:, head_cols(j)]
        first = dot_nt(q, key_refs[0][...]) * scale + bias_ref[0]
        s_ref[0] = first
        mx_ref[...] = jnp.max(first, axis=-1, keepdims=True)
        for m in range(1, blocks):

            @pl.when(need_ref[m] > 0)
            def _():
                s = dot_nt(q, key_refs[m][...]) * scale + bias_ref[m]
                s_ref[m] = s
                mx_ref[...] = jnp.maximum(mx_ref[...], jnp.max(s, axis=-1, keepdims=True))

        weights = jnp.exp(s_ref[0] - mx_ref[...])
        tot_ref[...] = jnp.sum(weights, axis=-1, keepdims=True)
        acc_ref[...] = jnp.dot(
            weights.astype(BF16), value_refs[0][...], preferred_element_type=F32
        )
        for m in range(1, blocks):

            @pl.when(need_ref[m] > 0)
            def _():
                w = jnp.exp(s_ref[m] - mx_ref[...])
                tot_ref[...] += jnp.sum(w, axis=-1, keepdims=True)
                acc_ref[...] += jnp.dot(
                    w.astype(BF16), value_refs[m][...], preferred_element_type=F32
                )

        o_ref[:, head_cols(j)] = (acc_ref[...] / tot_ref[...]).astype(o_ref.dtype)


def body(lin_query, lin_key, lin_value, norm_gain, soft_query, soft_key, soft_value, doc_lengths):
    rows, width = lin_query.shape
    local_heads = width // HD
    shard_index = lax.axis_index("ctx")
    shard_start = shard_index * rows
    offsets = jnp.arange(rows, dtype=jnp.int32)
    own_docs = document_index(doc_lengths, shard_start + offsets)
    edges = document_index(
        doc_lengths,
        jnp.stack(
            [
                shard_start - 1,
                shard_start + rows - 1,
                shard_start - rows - 1,
                shard_start - 2 * rows - 1,
            ]
        ),
    )
    before_doc, last_doc, before1, before2 = edges[0], edges[1], edges[2], edges[3]

    head_devices = lax.axis_size("head")
    group_size = HEADS // KV_HEADS
    per_device = HEADS // head_devices
    kv_local = max(1, per_device // group_size)
    kv_table = (
        np.arange(head_devices)[:, None] * per_device // group_size + np.arange(kv_local)[None, :]
    ).reshape(-1)
    short_rows = soft_key.shape[0]

    def spread(field):
        if np.array_equal(kv_table, np.arange(KV_HEADS)):
            return field.reshape(short_rows, head_devices, kv_local * HD)
        taken = jnp.take(field.reshape(short_rows, KV_HEADS, HD), kv_table, axis=1)
        return taken.reshape(short_rows, head_devices, kv_local * HD)

    packed = jnp.concatenate(
        [
            soft_query.reshape(short_rows, head_devices, per_device * HD),
            spread(soft_key),
            spread(soft_value),
        ],
        axis=2,
    )
    per_dest = packed.shape[2]
    packed = packed.reshape(short_rows, head_devices * per_dest)
    mixed = lax.all_to_all(packed, "head", split_axis=1, concat_axis=0, tiled=True)
    own_kv = mixed[:, per_device * HD :]
    older = [from_behind(own_kv, "ctx", step) for step in range(1, SPAN + 1)]

    lhpb = min(local_heads, group_size)
    lsteps = local_heads // lhpb
    lwide = lhpb * HD
    tail_mask = (own_docs == last_doc).astype(BF16)[:, None]
    tail = pl.pallas_call(
        lambda *refs: tail_kernel(lhpb, *refs),
        out_shape=jax.ShapeDtypeStruct((local_heads, HD, HD), F32),
        grid=(lsteps,),
        in_specs=[full_spec((rows, 1)), col_spec(rows, lwide), col_spec(rows, lwide)],
        out_specs=pl.BlockSpec((lhpb, HD, HD), lambda h: (h, 0, 0)),
        compiler_params=params(),
        cost_estimate=pl.CostEstimate(
            flops=2 * rows * HD * HD * local_heads,
            transcendentals=0,
            bytes_accessed=2 * rows * width * 2 + local_heads * HD * HD * 4,
        ),
    )(tail_mask, lin_key, lin_value)
    tails = [from_behind(tail, "ctx", step) for step in range(1, SPAN + 1)]

    lin_local = pl.pallas_call(
        lambda *refs: lin_local_kernel(lhpb, *refs),
        out_shape=jax.ShapeDtypeStruct((rows, width), F32),
        grid=(lsteps,),
        in_specs=[
            full_spec((rows, 1)),
            full_spec((1, rows)),
            col_spec(rows, lwide),
            col_spec(rows, lwide),
            col_spec(rows, lwide),
        ],
        out_specs=col_spec(rows, lwide),
        compiler_params=params(),
        cost_estimate=pl.CostEstimate(
            flops=6 * rows * rows * HD * local_heads,
            transcendentals=0,
            bytes_accessed=3 * rows * width * 2 + rows * width * 4,
        ),
    )(own_docs[:, None], own_docs[None, :], lin_query, lin_key, lin_value)

    blocks = SPAN + 1
    key_docs = jnp.stack(
        [
            document_index(doc_lengths, (shard_index - step) * rows + offsets)
            for step in range(blocks)
        ]
    )
    causal = offsets[None, :] <= offsets[:, None]
    visible = own_docs[None, :, None] == key_docs[:, None, :]
    visible = visible & jnp.concatenate(
        [causal[None], jnp.ones((SPAN, rows, rows), jnp.bool_)], axis=0
    )
    bias = jnp.where(visible, 0.0, -1e30).astype(F32)
    need = (key_docs[:, rows - 1] == own_docs[0]).astype(jnp.int32)
    shpb = min(per_device, group_size)
    ssteps = per_device // shpb
    kv_index = lambda i: (i * shpb * kv_local) // per_device
    own_k_spec = pl.BlockSpec((rows, HD), lambda i: (0, per_device + kv_index(i)))
    own_v_spec = pl.BlockSpec((rows, HD), lambda i: (0, per_device + kv_local + kv_index(i)))
    old_k_spec = pl.BlockSpec((rows, HD), lambda i: (0, kv_index(i)))
    old_v_spec = pl.BlockSpec((rows, HD), lambda i: (0, kv_local + kv_index(i)))
    attended = pl.pallas_call(
        lambda *refs: soft_kernel(blocks, shpb, *refs),
        out_shape=jax.ShapeDtypeStruct((rows, per_device * HD), BF16),
        grid=(ssteps,),
        in_specs=[
            pl.BlockSpec(memory_space=pltpu.SMEM),
            full_spec((blocks, rows, rows)),
            col_spec(rows, shpb * HD),
        ]
        + [own_k_spec]
        + [old_k_spec] * SPAN
        + [own_v_spec]
        + [old_v_spec] * SPAN,
        out_specs=col_spec(rows, shpb * HD),
        scratch_shapes=[
            pltpu.VMEM((blocks, rows, rows), F32),
            pltpu.VMEM((rows, 1), F32),
            pltpu.VMEM((rows, 1), F32),
            pltpu.VMEM((rows, HD), F32),
        ],
        compiler_params=params(),
        cost_estimate=pl.CostEstimate(
            flops=4 * rows * rows * blocks * HD * per_device,
            transcendentals=rows * rows * blocks * per_device,
            bytes_accessed=rows * per_device * HD * 4 + 2 * blocks * rows * HD * 2 * per_device,
        ),
    )(need, bias, mixed, mixed, *older, mixed, *older)

    through1 = (before1 == before_doc).astype(F32)
    through2 = (before2 == before1).astype(F32)
    carried = tails[0] + through1 * (tails[1] + through2 * tails[2])
    sees_carry = (own_docs == before_doc).astype(F32)[:, None]
    lightning_out = pl.pallas_call(
        lambda *refs: lin_finish_kernel(lhpb, *refs),
        out_shape=jax.ShapeDtypeStruct((rows, width), BF16),
        grid=(lsteps,),
        in_specs=[
            full_spec((rows, 1)),
            col_spec(rows, lwide),
            pl.BlockSpec((lhpb, HD, HD), lambda h: (h, 0, 0)),
            col_spec(rows, lwide),
            pl.BlockSpec((1, lwide), lambda h: (0, h)),
        ],
        out_specs=col_spec(rows, lwide),
        compiler_params=params(),
        cost_estimate=pl.CostEstimate(
            flops=4 * rows * HD * HD * local_heads,
            transcendentals=rows * local_heads,
            bytes_accessed=rows * width * (2 + 4 + 2) + local_heads * HD * HD * 4,
        ),
    )(sees_carry, lin_query, carried, lin_local, norm_gain.reshape(1, width))
    return (lightning_out, attended)


def solution(mesh):
    placed = (
        P("ctx", "head"),
        P("ctx", "head"),
        P("ctx", "head"),
        P("head"),
        P(("ctx", "head"), None),
        P(("ctx", "head"), None),
        P(("ctx", "head"), None),
        P(),
    )
    return jax.shard_map(
        body,
        mesh=mesh,
        in_specs=placed,
        out_specs=(P("ctx", "head"), P("ctx", "head")),
        check_vma=False,
    )
```

```python
import math

import jax
import jax.numpy as jnp
import numpy as np
from jax import lax
from jax.experimental import pallas as pl
from jax.experimental.pallas import tpu as pltpu
from jax.sharding import PartitionSpec as P

HEADS = 64
HD = 128
KV_HEADS = 8
SPAN = 3

F32 = jnp.float32
BF16 = jnp.bfloat16


def document_index(doc_lengths, positions):
    doc_ends = jnp.cumsum(doc_lengths)
    counted = jnp.sum((positions[:, None] >= doc_ends[None, :]).astype(jnp.int32), axis=1)
    return jnp.where(positions < 0, -1, counted).astype(jnp.int32)


def from_behind(value, axis, steps):
    count = lax.axis_size(axis)
    pairs = [(source, source + steps) for source in range(0, count - steps)]
    if not pairs:
        return jnp.zeros_like(value)
    return lax.ppermute(value, axis, pairs)


def split_bf16(x):
    hi = x.astype(BF16)
    lo = (x - hi.astype(F32)).astype(BF16)
    return hi, lo


def dot_nt(a, b):
    return lax.dot_general(a, b, (((1,), (1,)), ((), ())), preferred_element_type=F32)


def head_cols(j):
    return slice(j * HD, (j + 1) * HD)


def tail_kernel(hpb, mask_ref, k_ref, v_ref, t_ref):
    mask = mask_ref[...]
    for j in range(hpb):
        masked = v_ref[:, head_cols(j)] * mask
        t_ref[j] = lax.dot_general(
            k_ref[:, head_cols(j)], masked, (((0,), (0,)), ((), ())), preferred_element_type=F32
        )


def lin_local_kernel(hpb, dq_ref, dk_ref, q_ref, k_ref, v_ref, lin_ref):
    rows = q_ref.shape[0]
    row = lax.broadcasted_iota(jnp.int32, (rows, rows), 0)
    col = lax.broadcasted_iota(jnp.int32, (rows, rows), 1)
    visible = (dq_ref[...] == dk_ref[...]) & (col <= row)
    for j in range(hpb):
        scores = dot_nt(q_ref[:, head_cols(j)], k_ref[:, head_cols(j)])
        scores = jnp.where(visible, scores, 0.0)
        hi, lo = split_bf16(scores)
        v = v_ref[:, head_cols(j)]
        lin_ref[:, head_cols(j)] = jnp.dot(hi, v, preferred_element_type=F32) + jnp.dot(
            lo, v, preferred_element_type=F32
        )


def lin_finish_kernel(hpb, sees_ref, q_ref, c_ref, lin_ref, g_ref, o_ref):
    sees = sees_ref[...]
    for j in range(hpb):
        hi, lo = split_bf16(c_ref[j])
        q = q_ref[:, head_cols(j)]
        carried = jnp.dot(q, hi, preferred_element_type=F32) + jnp.dot(
            q, lo, preferred_element_type=F32
        )
        lin = lin_ref[:, head_cols(j)] + carried * sees
        mean_sq = jnp.mean(lin * lin, axis=-1, keepdims=True)
        normed = lin * lax.rsqrt(mean_sq + 1e-06) * g_ref[:, head_cols(j)]
        o_ref[:, head_cols(j)] = normed.astype(o_ref.dtype)


def col_spec(rows, width=HD):
    return pl.BlockSpec((rows, width), lambda h: (0, h))


def full_spec(shape):
    return pl.BlockSpec(shape, lambda h: (0,) * len(shape))


def params():
    return pltpu.CompilerParams(dimension_semantics=("arbitrary",))


def soft_kernel(blocks, hpb, need_ref, bias_ref, q_ref, *rest):
    key_refs = rest[0:blocks]
    value_refs = rest[blocks : 2 * blocks]
    o_ref = rest[2 * blocks]
    s_ref, mx_ref, tot_ref, acc_ref = rest[2 * blocks + 1 :]
    scale = 1.0 / math.sqrt(HD)
    for j in range(hpb):
        q = q_ref[:, head_cols(j)]
        first = dot_nt(q, key_refs[0][...]) * scale + bias_ref[0]
        s_ref[0] = first
        mx_ref[...] = jnp.max(first, axis=-1, keepdims=True)
        for m in range(1, blocks):

            @pl.when(need_ref[m] > 0)
            def _():
                s = dot_nt(q, key_refs[m][...]) * scale + bias_ref[m]
                s_ref[m] = s
                mx_ref[...] = jnp.maximum(mx_ref[...], jnp.max(s, axis=-1, keepdims=True))

        weights = jnp.exp(s_ref[0] - mx_ref[...])
        tot_ref[...] = jnp.sum(weights, axis=-1, keepdims=True)
        acc_ref[...] = jnp.dot(
            weights.astype(BF16), value_refs[0][...], preferred_element_type=F32
        )
        for m in range(1, blocks):

            @pl.when(need_ref[m] > 0)
            def _():
                w = jnp.exp(s_ref[m] - mx_ref[...])
                tot_ref[...] += jnp.sum(w, axis=-1, keepdims=True)
                acc_ref[...] += jnp.dot(
                    w.astype(BF16), value_refs[m][...], preferred_element_type=F32
                )

        o_ref[:, head_cols(j)] = (acc_ref[...] / tot_ref[...]).astype(o_ref.dtype)


def body(lin_query, lin_key, lin_value, norm_gain, soft_query, soft_key, soft_value, doc_lengths):
    rows, width = lin_query.shape
    local_heads = width // HD
    shard_index = lax.axis_index("ctx")
    shard_start = shard_index * rows
    offsets = jnp.arange(rows, dtype=jnp.int32)
    own_docs = document_index(doc_lengths, shard_start + offsets)
    edges = document_index(
        doc_lengths,
        jnp.stack(
            [
                shard_start - 1,
                shard_start + rows - 1,
                shard_start - rows - 1,
                shard_start - 2 * rows - 1,
            ]
        ),
    )
    before_doc, last_doc, before1, before2 = edges[0], edges[1], edges[2], edges[3]

    head_devices = lax.axis_size("head")
    group_size = HEADS // KV_HEADS
    per_device = HEADS // head_devices
    kv_local = max(1, per_device // group_size)
    kv_table = (
        np.arange(head_devices)[:, None] * per_device // group_size + np.arange(kv_local)[None, :]
    ).reshape(-1)
    short_rows = soft_key.shape[0]

    def spread(field):
        if np.array_equal(kv_table, np.arange(KV_HEADS)):
            return field.reshape(short_rows, head_devices, kv_local * HD)
        taken = jnp.take(field.reshape(short_rows, KV_HEADS, HD), kv_table, axis=1)
        return taken.reshape(short_rows, head_devices, kv_local * HD)

    packed = jnp.concatenate(
        [
            soft_query.reshape(short_rows, head_devices, per_device * HD),
            spread(soft_key),
            spread(soft_value),
        ],
        axis=2,
    )
    per_dest = packed.shape[2]
    packed = packed.reshape(short_rows, head_devices * per_dest)
    mixed = lax.all_to_all(packed, "head", split_axis=1, concat_axis=0, tiled=True)
    own_kv = mixed[:, per_device * HD :]
    older = []
    moving = own_kv
    for _ in range(SPAN):
        moving = from_behind(moving, "ctx", 1)
        older.append(moving)

    lhpb = min(local_heads, group_size)
    lsteps = local_heads // lhpb
    lwide = lhpb * HD
    tail_mask = (own_docs == last_doc).astype(BF16)[:, None]
    tail = pl.pallas_call(
        lambda *refs: tail_kernel(lhpb, *refs),
        out_shape=jax.ShapeDtypeStruct((local_heads, HD, HD), F32),
        grid=(lsteps,),
        in_specs=[full_spec((rows, 1)), col_spec(rows, lwide), col_spec(rows, lwide)],
        out_specs=pl.BlockSpec((lhpb, HD, HD), lambda h: (h, 0, 0)),
        compiler_params=params(),
        cost_estimate=pl.CostEstimate(
            flops=2 * rows * HD * HD * local_heads,
            transcendentals=0,
            bytes_accessed=2 * rows * width * 2 + local_heads * HD * HD * 4,
        ),
    )(tail_mask, lin_key, lin_value)
    through_own = (before_doc == last_doc).astype(F32)
    received = from_behind(tail, "ctx", 1)
    for _ in range(SPAN - 1):
        received = from_behind(tail + through_own * received, "ctx", 1)
    carried = received

    lin_local = pl.pallas_call(
        lambda *refs: lin_local_kernel(lhpb, *refs),
        out_shape=jax.ShapeDtypeStruct((rows, width), F32),
        grid=(lsteps,),
        in_specs=[
            full_spec((rows, 1)),
            full_spec((1, rows)),
            col_spec(rows, lwide),
            col_spec(rows, lwide),
            col_spec(rows, lwide),
        ],
        out_specs=col_spec(rows, lwide),
        compiler_params=params(),
        cost_estimate=pl.CostEstimate(
            flops=6 * rows * rows * HD * local_heads,
            transcendentals=0,
            bytes_accessed=3 * rows * width * 2 + rows * width * 4,
        ),
    )(own_docs[:, None], own_docs[None, :], lin_query, lin_key, lin_value)

    blocks = SPAN + 1
    key_docs = jnp.stack(
        [
            document_index(doc_lengths, (shard_index - step) * rows + offsets)
            for step in range(blocks)
        ]
    )
    causal = offsets[None, :] <= offsets[:, None]
    visible = own_docs[None, :, None] == key_docs[:, None, :]
    visible = visible & jnp.concatenate(
        [causal[None], jnp.ones((SPAN, rows, rows), jnp.bool_)], axis=0
    )
    bias = jnp.where(visible, 0.0, -1e30).astype(F32)
    need = (key_docs[:, rows - 1] == own_docs[0]).astype(jnp.int32)
    shpb = min(per_device, group_size)
    ssteps = per_device // shpb
    kv_index = lambda i: (i * shpb * kv_local) // per_device
    own_k_spec = pl.BlockSpec((rows, HD), lambda i: (0, per_device + kv_index(i)))
    own_v_spec = pl.BlockSpec((rows, HD), lambda i: (0, per_device + kv_local + kv_index(i)))
    old_k_spec = pl.BlockSpec((rows, HD), lambda i: (0, kv_index(i)))
    old_v_spec = pl.BlockSpec((rows, HD), lambda i: (0, kv_local + kv_index(i)))
    attended = pl.pallas_call(
        lambda *refs: soft_kernel(blocks, shpb, *refs),
        out_shape=jax.ShapeDtypeStruct((rows, per_device * HD), BF16),
        grid=(ssteps,),
        in_specs=[
            pl.BlockSpec(memory_space=pltpu.SMEM),
            full_spec((blocks, rows, rows)),
            col_spec(rows, shpb * HD),
        ]
        + [own_k_spec]
        + [old_k_spec] * SPAN
        + [own_v_spec]
        + [old_v_spec] * SPAN,
        out_specs=col_spec(rows, shpb * HD),
        scratch_shapes=[
            pltpu.VMEM((blocks, rows, rows), F32),
            pltpu.VMEM((rows, 1), F32),
            pltpu.VMEM((rows, 1), F32),
            pltpu.VMEM((rows, HD), F32),
        ],
        compiler_params=params(),
        cost_estimate=pl.CostEstimate(
            flops=4 * rows * rows * blocks * HD * per_device,
            transcendentals=rows * rows * blocks * per_device,
            bytes_accessed=rows * per_device * HD * 4 + 2 * blocks * rows * HD * 2 * per_device,
        ),
    )(need, bias, mixed, mixed, *older, mixed, *older)

    sees_carry = (own_docs == before_doc).astype(F32)[:, None]
    lightning_out = pl.pallas_call(
        lambda *refs: lin_finish_kernel(lhpb, *refs),
        out_shape=jax.ShapeDtypeStruct((rows, width), BF16),
        grid=(lsteps,),
        in_specs=[
            full_spec((rows, 1)),
            col_spec(rows, lwide),
            pl.BlockSpec((lhpb, HD, HD), lambda h: (h, 0, 0)),
            col_spec(rows, lwide),
            pl.BlockSpec((1, lwide), lambda h: (0, h)),
        ],
        out_specs=col_spec(rows, lwide),
        compiler_params=params(),
        cost_estimate=pl.CostEstimate(
            flops=4 * rows * HD * HD * local_heads,
            transcendentals=rows * local_heads,
            bytes_accessed=rows * width * (2 + 4 + 2) + local_heads * HD * HD * 4,
        ),
    )(sees_carry, lin_query, carried, lin_local, norm_gain.reshape(1, width))
    return (lightning_out, attended)


def solution(mesh):
    placed = (
        P("ctx", "head"),
        P("ctx", "head"),
        P("ctx", "head"),
        P("head"),
        P(("ctx", "head"), None),
        P(("ctx", "head"), None),
        P(("ctx", "head"), None),
        P(),
    )
    return jax.shard_map(
        body,
        mesh=mesh,
        in_specs=placed,
        out_specs=(P("ctx", "head"), P("ctx", "head")),
        check_vma=False,
    )
```

```python
import math

import jax
import jax.numpy as jnp
import numpy as np
from jax import lax
from jax.experimental import pallas as pl
from jax.experimental.pallas import tpu as pltpu
from jax.sharding import PartitionSpec as P

HEADS = 64
HD = 128
KV_HEADS = 8
SPAN = 3

F32 = jnp.float32
BF16 = jnp.bfloat16


def document_index(doc_lengths, positions):
    doc_ends = jnp.cumsum(doc_lengths)
    counted = jnp.sum((positions[:, None] >= doc_ends[None, :]).astype(jnp.int32), axis=1)
    return jnp.where(positions < 0, -1, counted).astype(jnp.int32)


def from_behind(value, axis, steps):
    count = lax.axis_size(axis)
    pairs = [(source, source + steps) for source in range(0, count - steps)]
    if not pairs:
        return jnp.zeros_like(value)
    return lax.ppermute(value, axis, pairs)


def split_bf16(x):
    hi = x.astype(BF16)
    lo = (x - hi.astype(F32)).astype(BF16)
    return hi, lo


def dot_nt(a, b):
    return lax.dot_general(a, b, (((1,), (1,)), ((), ())), preferred_element_type=F32)


def head_cols(j):
    return slice(j * HD, (j + 1) * HD)


def doc_ends(len_ref, ndocs):
    ends = []
    total = jnp.int32(0)
    for i in range(ndocs):
        total = total + len_ref[i]
        ends.append(total)
    return ends


def doc_of(ends, pos):
    counted = jnp.zeros_like(pos)
    for e in ends:
        counted = counted + (pos >= e).astype(jnp.int32)
    return jnp.where(pos < 0, -1, counted)


def tail_kernel(hpb, ndocs, len_ref, start_ref, k_ref, v_ref, t_ref):
    rows = k_ref.shape[0]
    ends = doc_ends(len_ref, ndocs)
    start = start_ref[0]
    pos = start + lax.broadcasted_iota(jnp.int32, (rows, 1), 0)
    last = doc_of(ends, start + rows - 1)
    mask = (doc_of(ends, pos) == last).astype(BF16)
    for j in range(hpb):
        masked = v_ref[:, head_cols(j)] * mask
        t_ref[j] = lax.dot_general(
            k_ref[:, head_cols(j)], masked, (((0,), (0,)), ((), ())), preferred_element_type=F32
        )


def lin_local_kernel(hpb, ndocs, len_ref, start_ref, q_ref, k_ref, v_ref, lin_ref):
    rows = q_ref.shape[0]
    ends = doc_ends(len_ref, ndocs)
    start = start_ref[0]
    qpos = start + lax.broadcasted_iota(jnp.int32, (rows, 1), 0)
    kpos = start + lax.broadcasted_iota(jnp.int32, (1, rows), 1)
    visible = (doc_of(ends, qpos) == doc_of(ends, kpos)) & (kpos <= qpos)
    for j in range(hpb):
        scores = dot_nt(q_ref[:, head_cols(j)], k_ref[:, head_cols(j)])
        scores = jnp.where(visible, scores, 0.0)
        hi, lo = split_bf16(scores)
        v = v_ref[:, head_cols(j)]
        lin_ref[:, head_cols(j)] = jnp.dot(hi, v, preferred_element_type=F32) + jnp.dot(
            lo, v, preferred_element_type=F32
        )


def lin_finish_kernel(hpb, ndocs, len_ref, start_ref, q_ref, c_ref, lin_ref, g_ref, o_ref):
    rows = q_ref.shape[0]
    ends = doc_ends(len_ref, ndocs)
    start = start_ref[0]
    pos = start + lax.broadcasted_iota(jnp.int32, (rows, 1), 0)
    sees = (doc_of(ends, pos) == doc_of(ends, start - 1)).astype(F32)
    for j in range(hpb):
        hi, lo = split_bf16(c_ref[j])
        q = q_ref[:, head_cols(j)]
        carried = jnp.dot(q, hi, preferred_element_type=F32) + jnp.dot(
            q, lo, preferred_element_type=F32
        )
        lin = lin_ref[:, head_cols(j)] + carried * sees
        mean_sq = jnp.mean(lin * lin, axis=-1, keepdims=True)
        normed = lin * lax.rsqrt(mean_sq + 1e-06) * g_ref[:, head_cols(j)]
        o_ref[:, head_cols(j)] = normed.astype(o_ref.dtype)


def col_spec(rows, width=HD):
    return pl.BlockSpec((rows, width), lambda h: (0, h))


def full_spec(shape):
    return pl.BlockSpec(shape, lambda h: (0,) * len(shape))


def params():
    return pltpu.CompilerParams(dimension_semantics=("arbitrary",))


def soft_kernel(blocks, hpb, ndocs, len_ref, start_ref, q_ref, *rest):
    key_refs = rest[0:blocks]
    value_refs = rest[blocks : 2 * blocks]
    o_ref = rest[2 * blocks]
    s_ref, mx_ref, tot_ref, acc_ref = rest[2 * blocks + 1 :]
    rows = q_ref.shape[0]
    scale = 1.0 / math.sqrt(HD)
    ends = doc_ends(len_ref, ndocs)
    start = start_ref[0]
    qpos = start + lax.broadcasted_iota(jnp.int32, (rows, 1), 0)
    kpos = start + lax.broadcasted_iota(jnp.int32, (1, rows), 1)
    dq = doc_of(ends, qpos)
    first_doc = doc_of(ends, start)
    q = jnp.concatenate([q_ref[:, head_cols(j)] for j in range(hpb)], axis=0)

    def block_scores(m):
        shifted = kpos - m * rows
        visible = dq == doc_of(ends, shifted)
        if m == 0:
            visible = visible & (shifted <= qpos)
        s = dot_nt(q, key_refs[m][...]).reshape(hpb, rows, rows) * scale
        return jnp.where(visible[None], s, -1e30)

    def needed(m):
        return doc_of(ends, start - (m - 1) * rows - 1) == first_doc

    s0 = block_scores(0)
    s_ref[0] = s0
    mx_ref[...] = jnp.max(s0, axis=-1, keepdims=True)
    for m in range(1, blocks):

        @pl.when(needed(m))
        def _():
            s = block_scores(m)
            s_ref[m] = s
            mx_ref[...] = jnp.maximum(mx_ref[...], jnp.max(s, axis=-1, keepdims=True))

    def weighted(m):
        w = jnp.exp(s_ref[m] - mx_ref[...])
        part = jnp.sum(w, axis=-1, keepdims=True)
        term = jnp.dot(
            w.reshape(hpb * rows, rows).astype(BF16),
            value_refs[m][...],
            preferred_element_type=F32,
        ).reshape(hpb, rows, HD)
        return part, term

    part, term = weighted(0)
    tot_ref[...] = part
    acc_ref[...] = term
    for m in range(1, blocks):

        @pl.when(needed(m))
        def _():
            part, term = weighted(m)
            tot_ref[...] += part
            acc_ref[...] += term

    out = acc_ref[...] / tot_ref[...]
    for j in range(hpb):
        o_ref[:, head_cols(j)] = out[j].astype(o_ref.dtype)


def smem_spec():
    return pl.BlockSpec(memory_space=pltpu.SMEM)


def body(lin_query, lin_key, lin_value, norm_gain, soft_query, soft_key, soft_value, doc_lengths):
    rows, width = lin_query.shape
    local_heads = width // HD
    ndocs = doc_lengths.shape[0]
    lengths = doc_lengths.astype(jnp.int32)
    shard_start = (lax.axis_index("ctx") * rows).astype(jnp.int32).reshape(1)
    ends = jnp.cumsum(lengths)

    def doc_at(pos):
        return jnp.where(pos < 0, -1, jnp.sum((pos >= ends).astype(jnp.int32)))

    through_own = (doc_at(shard_start[0] - 1) == doc_at(shard_start[0] + rows - 1)).astype(F32)

    head_devices = lax.axis_size("head")
    group_size = HEADS // KV_HEADS
    per_device = HEADS // head_devices
    kv_local = max(1, per_device // group_size)
    kv_table = (
        np.arange(head_devices)[:, None] * per_device // group_size + np.arange(kv_local)[None, :]
    ).reshape(-1)
    short_rows = soft_key.shape[0]

    def spread(field):
        if np.array_equal(kv_table, np.arange(KV_HEADS)):
            return field.reshape(short_rows, head_devices, kv_local * HD)
        taken = jnp.take(field.reshape(short_rows, KV_HEADS, HD), kv_table, axis=1)
        return taken.reshape(short_rows, head_devices, kv_local * HD)

    packed = jnp.concatenate(
        [
            soft_query.reshape(short_rows, head_devices, per_device * HD),
            spread(soft_key),
            spread(soft_value),
        ],
        axis=2,
    )
    per_dest = packed.shape[2]
    packed = packed.reshape(short_rows, head_devices * per_dest)
    mixed = lax.all_to_all(packed, "head", split_axis=1, concat_axis=0, tiled=True)
    own_kv = mixed[:, per_device * HD :]
    older = []
    moving = own_kv
    for _ in range(SPAN):
        moving = from_behind(moving, "ctx", 1)
        older.append(moving)

    lhpb = min(local_heads, group_size)
    lsteps = local_heads // lhpb
    lwide = lhpb * HD
    tail = pl.pallas_call(
        lambda *refs: tail_kernel(lhpb, ndocs, *refs),
        out_shape=jax.ShapeDtypeStruct((local_heads, HD, HD), F32),
        grid=(lsteps,),
        in_specs=[smem_spec(), smem_spec(), col_spec(rows, lwide), col_spec(rows, lwide)],
        out_specs=pl.BlockSpec((lhpb, HD, HD), lambda h: (h, 0, 0)),
        compiler_params=params(),
        cost_estimate=pl.CostEstimate(
            flops=2 * rows * HD * HD * local_heads,
            transcendentals=0,
            bytes_accessed=2 * rows * width * 2 + local_heads * HD * HD * 4,
        ),
    )(lengths, shard_start, lin_key, lin_value)
    received = from_behind(tail, "ctx", 1)

    lin_local = pl.pallas_call(
        lambda *refs: lin_local_kernel(lhpb, ndocs, *refs),
        out_shape=jax.ShapeDtypeStruct((rows, width), F32),
        grid=(lsteps,),
        in_specs=[
            smem_spec(),
            smem_spec(),
            col_spec(rows, lwide),
            col_spec(rows, lwide),
            col_spec(rows, lwide),
        ],
        out_specs=col_spec(rows, lwide),
        compiler_params=params(),
        cost_estimate=pl.CostEstimate(
            flops=6 * rows * rows * HD * local_heads,
            transcendentals=0,
            bytes_accessed=3 * rows * width * 2 + rows * width * 4,
        ),
    )(lengths, shard_start, lin_query, lin_key, lin_value)

    onward = tail + through_own * received
    lin_local, onward = lax.optimization_barrier((lin_local, onward))
    received = from_behind(onward, "ctx", 1)
    for _ in range(SPAN - 2):
        received = from_behind(tail + through_own * received, "ctx", 1)
    carried = received

    blocks = SPAN + 1
    shpb = min(per_device, group_size)
    ssteps = per_device // shpb
    kv_index = lambda i: (i * shpb * kv_local) // per_device
    own_k_spec = pl.BlockSpec((rows, HD), lambda i: (0, per_device + kv_index(i)))
    own_v_spec = pl.BlockSpec((rows, HD), lambda i: (0, per_device + kv_local + kv_index(i)))
    old_k_spec = pl.BlockSpec((rows, HD), lambda i: (0, kv_index(i)))
    old_v_spec = pl.BlockSpec((rows, HD), lambda i: (0, kv_local + kv_index(i)))
    attended = pl.pallas_call(
        lambda *refs: soft_kernel(blocks, shpb, ndocs, *refs),
        out_shape=jax.ShapeDtypeStruct((rows, per_device * HD), BF16),
        grid=(ssteps,),
        in_specs=[smem_spec(), smem_spec(), col_spec(rows, shpb * HD)]
        + [own_k_spec]
        + [old_k_spec] * SPAN
        + [own_v_spec]
        + [old_v_spec] * SPAN,
        out_specs=col_spec(rows, shpb * HD),
        scratch_shapes=[
            pltpu.VMEM((blocks, shpb, rows, rows), F32),
            pltpu.VMEM((shpb, rows, 1), F32),
            pltpu.VMEM((shpb, rows, 1), F32),
            pltpu.VMEM((shpb, rows, HD), F32),
        ],
        compiler_params=pltpu.CompilerParams(
            dimension_semantics=("arbitrary",), vmem_limit_bytes=48 * 1024 * 1024
        ),
        cost_estimate=pl.CostEstimate(
            flops=4 * rows * rows * blocks * HD * per_device,
            transcendentals=rows * rows * blocks * per_device,
            bytes_accessed=rows * per_device * HD * 4 + 2 * blocks * rows * HD * 2 * per_device,
        ),
    )(lengths, shard_start, mixed, mixed, *older, mixed, *older)

    lightning_out = pl.pallas_call(
        lambda *refs: lin_finish_kernel(lhpb, ndocs, *refs),
        out_shape=jax.ShapeDtypeStruct((rows, width), BF16),
        grid=(lsteps,),
        in_specs=[
            smem_spec(),
            smem_spec(),
            col_spec(rows, lwide),
            pl.BlockSpec((lhpb, HD, HD), lambda h: (h, 0, 0)),
            col_spec(rows, lwide),
            pl.BlockSpec((1, lwide), lambda h: (0, h)),
        ],
        out_specs=col_spec(rows, lwide),
        compiler_params=params(),
        cost_estimate=pl.CostEstimate(
            flops=4 * rows * HD * HD * local_heads,
            transcendentals=rows * local_heads,
            bytes_accessed=rows * width * (2 + 4 + 2) + local_heads * HD * HD * 4,
        ),
    )(lengths, shard_start, lin_query, carried, lin_local, norm_gain.reshape(1, width))
    return (lightning_out, attended)


def solution(mesh):
    placed = (
        P("ctx", "head"),
        P("ctx", "head"),
        P("ctx", "head"),
        P("head"),
        P(("ctx", "head"), None),
        P(("ctx", "head"), None),
        P(("ctx", "head"), None),
        P(),
    )
    return jax.shard_map(
        body,
        mesh=mesh,
        in_specs=placed,
        out_specs=(P("ctx", "head"), P("ctx", "head")),
        check_vma=False,
    )
```

```python
import math

import jax
import jax.numpy as jnp
import numpy as np
from jax import lax
from jax.experimental import pallas as pl
from jax.experimental.pallas import tpu as pltpu
from jax.sharding import PartitionSpec as P

HEADS = 64
HD = 128
KV_HEADS = 8
SPAN = 3

F32 = jnp.float32
BF16 = jnp.bfloat16


def document_index(doc_lengths, positions):
    doc_ends = jnp.cumsum(doc_lengths)
    counted = jnp.sum((positions[:, None] >= doc_ends[None, :]).astype(jnp.int32), axis=1)
    return jnp.where(positions < 0, -1, counted).astype(jnp.int32)


def from_behind(value, axis, steps):
    count = lax.axis_size(axis)
    pairs = [(source, source + steps) for source in range(0, count - steps)]
    if not pairs:
        return jnp.zeros_like(value)
    return lax.ppermute(value, axis, pairs)


def split_bf16(x):
    hi = x.astype(BF16)
    lo = (x - hi.astype(F32)).astype(BF16)
    return hi, lo


def dot_nt(a, b):
    return lax.dot_general(a, b, (((1,), (1,)), ((), ())), preferred_element_type=F32)


def head_cols(j):
    return slice(j * HD, (j + 1) * HD)


def doc_ends(len_ref, ndocs):
    ends = []
    total = jnp.int32(0)
    for i in range(ndocs):
        total = total + len_ref[i]
        ends.append(total)
    return ends


def doc_of(ends, pos):
    counted = jnp.zeros_like(pos)
    for e in ends:
        counted = counted + (pos >= e).astype(jnp.int32)
    return jnp.where(pos < 0, -1, counted)


def tail_kernel(hpb, ndocs, len_ref, start_ref, k_ref, v_ref, t_ref):
    rows = k_ref.shape[0]
    ends = doc_ends(len_ref, ndocs)
    start = start_ref[0]
    pos = start + lax.broadcasted_iota(jnp.int32, (rows, 1), 0)
    last = doc_of(ends, start + rows - 1)
    mask = (doc_of(ends, pos) == last).astype(BF16)
    for j in range(hpb):
        masked = v_ref[:, head_cols(j)] * mask
        t_ref[j] = lax.dot_general(
            k_ref[:, head_cols(j)], masked, (((0,), (0,)), ((), ())), preferred_element_type=F32
        )


def lin_local_kernel(hpb, ndocs, len_ref, start_ref, q_ref, k_ref, v_ref, lin_ref):
    rows = q_ref.shape[0]
    ends = doc_ends(len_ref, ndocs)
    start = start_ref[0]
    qpos = start + lax.broadcasted_iota(jnp.int32, (rows, 1), 0)
    kpos = start + lax.broadcasted_iota(jnp.int32, (1, rows), 1)
    visible = (doc_of(ends, qpos) == doc_of(ends, kpos)) & (kpos <= qpos)
    for j in range(hpb):
        scores = dot_nt(q_ref[:, head_cols(j)], k_ref[:, head_cols(j)])
        scores = jnp.where(visible, scores, 0.0)
        hi, lo = split_bf16(scores)
        v = v_ref[:, head_cols(j)]
        lin_ref[:, head_cols(j)] = jnp.dot(hi, v, preferred_element_type=F32) + jnp.dot(
            lo, v, preferred_element_type=F32
        )


def lin_finish_kernel(hpb, ndocs, len_ref, start_ref, q_ref, hi_ref, lo_ref, lin_ref, g_ref, o_ref):
    rows = q_ref.shape[0]
    ends = doc_ends(len_ref, ndocs)
    start = start_ref[0]
    pos = start + lax.broadcasted_iota(jnp.int32, (rows, 1), 0)
    sees = (doc_of(ends, pos) == doc_of(ends, start - 1)).astype(F32)
    for j in range(hpb):
        hi, lo = hi_ref[j], lo_ref[j]
        q = q_ref[:, head_cols(j)]
        carried = jnp.dot(q, hi, preferred_element_type=F32) + jnp.dot(
            q, lo, preferred_element_type=F32
        )
        lin = lin_ref[:, head_cols(j)] + carried * sees
        mean_sq = jnp.mean(lin * lin, axis=-1, keepdims=True)
        normed = lin * lax.rsqrt(mean_sq + 1e-06) * g_ref[:, head_cols(j)]
        o_ref[:, head_cols(j)] = normed.astype(o_ref.dtype)


def col_spec(rows, width=HD):
    return pl.BlockSpec((rows, width), lambda h: (0, h))


def full_spec(shape):
    return pl.BlockSpec(shape, lambda h: (0,) * len(shape))


def params():
    return pltpu.CompilerParams(dimension_semantics=("arbitrary",))


def soft_kernel(blocks, hpb, ndocs, len_ref, start_ref, q_ref, *rest):
    key_refs = rest[0:blocks]
    value_refs = rest[blocks : 2 * blocks]
    o_ref = rest[2 * blocks]
    s_ref, mx_ref, tot_ref, acc_ref = rest[2 * blocks + 1 :]
    rows = q_ref.shape[0]
    scale = 1.0 / math.sqrt(HD)
    ends = doc_ends(len_ref, ndocs)
    start = start_ref[0]
    qpos = start + lax.broadcasted_iota(jnp.int32, (rows, 1), 0)
    kpos = start + lax.broadcasted_iota(jnp.int32, (1, rows), 1)
    dq = doc_of(ends, qpos)
    first_doc = doc_of(ends, start)
    q = jnp.concatenate([q_ref[:, head_cols(j)] for j in range(hpb)], axis=0)

    def block_scores(m):
        shifted = kpos - m * rows
        visible = dq == doc_of(ends, shifted)
        if m == 0:
            visible = visible & (shifted <= qpos)
        s = dot_nt(q, key_refs[m][...].reshape(rows, HD)).reshape(hpb, rows, rows) * scale
        return jnp.where(visible[None], s, -1e30)

    def needed(m):
        return doc_of(ends, start - (m - 1) * rows - 1) == first_doc

    s0 = block_scores(0)
    s_ref[0] = s0
    mx_ref[...] = jnp.max(s0, axis=-1, keepdims=True)
    for m in range(1, blocks):

        @pl.when(needed(m))
        def _():
            s = block_scores(m)
            s_ref[m] = s
            mx_ref[...] = jnp.maximum(mx_ref[...], jnp.max(s, axis=-1, keepdims=True))

    def weighted(m):
        w = jnp.exp(s_ref[m] - mx_ref[...])
        part = jnp.sum(w, axis=-1, keepdims=True)
        term = jnp.dot(
            w.reshape(hpb * rows, rows).astype(BF16),
            value_refs[m][...].reshape(rows, HD),
            preferred_element_type=F32,
        ).reshape(hpb, rows, HD)
        return part, term

    part, term = weighted(0)
    tot_ref[...] = part
    acc_ref[...] = term
    for m in range(1, blocks):

        @pl.when(needed(m))
        def _():
            part, term = weighted(m)
            tot_ref[...] += part
            acc_ref[...] += term

    out = acc_ref[...] / tot_ref[...]
    for j in range(hpb):
        o_ref[:, head_cols(j)] = out[j].astype(o_ref.dtype)


def smem_spec():
    return pl.BlockSpec(memory_space=pltpu.SMEM)


def body(lin_query, lin_key, lin_value, norm_gain, soft_query, soft_key, soft_value, doc_lengths):
    rows, width = lin_query.shape
    local_heads = width // HD
    ndocs = doc_lengths.shape[0]
    lengths = doc_lengths.astype(jnp.int32)
    shard_start = (lax.axis_index("ctx") * rows).astype(jnp.int32).reshape(1)
    ends = jnp.cumsum(lengths)

    def doc_at(pos):
        return jnp.where(pos < 0, -1, jnp.sum((pos >= ends).astype(jnp.int32)))

    through_own = (doc_at(shard_start[0] - 1) == doc_at(shard_start[0] + rows - 1)).astype(F32)

    head_devices = lax.axis_size("head")
    group_size = HEADS // KV_HEADS
    per_device = HEADS // head_devices
    kv_local = max(1, per_device // group_size)
    kv_table = (
        np.arange(head_devices)[:, None] * per_device // group_size + np.arange(kv_local)[None, :]
    ).reshape(-1)
    short_rows = soft_key.shape[0]

    def spread(field):
        if np.array_equal(kv_table, np.arange(KV_HEADS)):
            return field.reshape(short_rows, head_devices, kv_local * HD)
        taken = jnp.take(field.reshape(short_rows, KV_HEADS, HD), kv_table, axis=1)
        return taken.reshape(short_rows, head_devices, kv_local * HD)

    packed = jnp.concatenate(
        [
            soft_query.reshape(short_rows, head_devices, per_device * HD),
            spread(soft_key),
            spread(soft_value),
        ],
        axis=2,
    )
    per_dest = packed.shape[2]
    packed = packed.reshape(short_rows, head_devices * per_dest)
    mixed = lax.all_to_all(packed, "head", split_axis=1, concat_axis=0, tiled=True)
    own_kv = mixed[:, per_device * HD :]
    kv_planes = own_kv.reshape(rows, 2 * kv_local, HD).transpose(1, 0, 2)
    kv_planes = kv_planes.reshape(2 * kv_local * rows // HD, HD, HD)

    lhpb = min(local_heads, group_size)
    lsteps = local_heads // lhpb
    lwide = lhpb * HD
    tail = pl.pallas_call(
        lambda *refs: tail_kernel(lhpb, ndocs, *refs),
        out_shape=jax.ShapeDtypeStruct((local_heads, HD, HD), F32),
        grid=(lsteps,),
        in_specs=[smem_spec(), smem_spec(), col_spec(rows, lwide), col_spec(rows, lwide)],
        out_specs=pl.BlockSpec((lhpb, HD, HD), lambda h: (h, 0, 0)),
        compiler_params=params(),
        cost_estimate=pl.CostEstimate(
            flops=2 * rows * HD * HD * local_heads,
            transcendentals=0,
            bytes_accessed=2 * rows * width * 2 + local_heads * HD * HD * 4,
        ),
    )(lengths, shard_start, lin_key, lin_value)

    lin_local = pl.pallas_call(
        lambda *refs: lin_local_kernel(lhpb, ndocs, *refs),
        out_shape=jax.ShapeDtypeStruct((rows, width), F32),
        grid=(lsteps,),
        in_specs=[
            smem_spec(),
            smem_spec(),
            col_spec(rows, lwide),
            col_spec(rows, lwide),
            col_spec(rows, lwide),
        ],
        out_specs=col_spec(rows, lwide),
        compiler_params=params(),
        cost_estimate=pl.CostEstimate(
            flops=6 * rows * rows * HD * local_heads,
            transcendentals=0,
            bytes_accessed=3 * rows * width * 2 + rows * width * 4,
        ),
    )(lengths, shard_start, lin_query, lin_key, lin_value)

    def pack(state, planes):
        hi, lo = split_bf16(state)
        return jnp.concatenate([hi, lo, planes], axis=0)

    payloads = []
    payload = from_behind(pack(tail, kv_planes), "ctx", 1)
    payloads.append(payload)
    for step in range(SPAN - 1):
        state = payload[:local_heads].astype(F32) + payload[local_heads : 2 * local_heads].astype(F32)
        outgoing = pack(tail + through_own * state, payload[2 * local_heads :])
        if step == 0:
            lin_local, outgoing = lax.optimization_barrier((lin_local, outgoing))
        payload = from_behind(outgoing, "ctx", 1)
        payloads.append(payload)
    older = [p.reshape(p.shape[0] // 2, rows, HD) for p in payloads]

    blocks = SPAN + 1
    shpb = min(per_device, group_size)
    ssteps = per_device // shpb
    kv_index = lambda i: (i * shpb * kv_local) // per_device
    own_k_spec = pl.BlockSpec((rows, HD), lambda i: (0, per_device + kv_index(i)))
    own_v_spec = pl.BlockSpec((rows, HD), lambda i: (0, per_device + kv_local + kv_index(i)))
    old_k_spec = pl.BlockSpec((1, rows, HD), lambda i: (local_heads + kv_index(i), 0, 0))
    old_v_spec = pl.BlockSpec(
        (1, rows, HD), lambda i: (local_heads + kv_local + kv_index(i), 0, 0)
    )
    attended = pl.pallas_call(
        lambda *refs: soft_kernel(blocks, shpb, ndocs, *refs),
        out_shape=jax.ShapeDtypeStruct((rows, per_device * HD), BF16),
        grid=(ssteps,),
        in_specs=[smem_spec(), smem_spec(), col_spec(rows, shpb * HD)]
        + [own_k_spec]
        + [old_k_spec] * SPAN
        + [own_v_spec]
        + [old_v_spec] * SPAN,
        out_specs=col_spec(rows, shpb * HD),
        scratch_shapes=[
            pltpu.VMEM((blocks, shpb, rows, rows), F32),
            pltpu.VMEM((shpb, rows, 1), F32),
            pltpu.VMEM((shpb, rows, 1), F32),
            pltpu.VMEM((shpb, rows, HD), F32),
        ],
        compiler_params=pltpu.CompilerParams(
            dimension_semantics=("arbitrary",), vmem_limit_bytes=48 * 1024 * 1024
        ),
        cost_estimate=pl.CostEstimate(
            flops=4 * rows * rows * blocks * HD * per_device,
            transcendentals=rows * rows * blocks * per_device,
            bytes_accessed=rows * per_device * HD * 4 + 2 * blocks * rows * HD * 2 * per_device,
        ),
    )(lengths, shard_start, mixed, mixed, *older, mixed, *older)

    lightning_out = pl.pallas_call(
        lambda *refs: lin_finish_kernel(lhpb, ndocs, *refs),
        out_shape=jax.ShapeDtypeStruct((rows, width), BF16),
        grid=(lsteps,),
        in_specs=[
            smem_spec(),
            smem_spec(),
            col_spec(rows, lwide),
            pl.BlockSpec((lhpb, HD, HD), lambda h: (h, 0, 0)),
            pl.BlockSpec((lhpb, HD, HD), lambda h: (lsteps + h, 0, 0)),
            col_spec(rows, lwide),
            pl.BlockSpec((1, lwide), lambda h: (0, h)),
        ],
        out_specs=col_spec(rows, lwide),
        compiler_params=params(),
        cost_estimate=pl.CostEstimate(
            flops=4 * rows * HD * HD * local_heads,
            transcendentals=rows * local_heads,
            bytes_accessed=rows * width * (2 + 4 + 2) + local_heads * HD * HD * 4,
        ),
    )(lengths, shard_start, lin_query, payload, payload, lin_local, norm_gain.reshape(1, width))
    return (lightning_out, attended)


def solution(mesh):
    placed = (
        P("ctx", "head"),
        P("ctx", "head"),
        P("ctx", "head"),
        P("head"),
        P(("ctx", "head"), None),
        P(("ctx", "head"), None),
        P(("ctx", "head"), None),
        P(),
    )
    return jax.shard_map(
        body,
        mesh=mesh,
        in_specs=placed,
        out_specs=(P("ctx", "head"), P("ctx", "head")),
        check_vma=False,
    )
```

```python
import math

import jax
import jax.numpy as jnp
import numpy as np
from jax import lax
from jax.experimental import pallas as pl
from jax.experimental.pallas import tpu as pltpu
from jax.sharding import PartitionSpec as P

HEADS = 64
HD = 128
KV_HEADS = 8
SPAN = 3

F32 = jnp.float32
BF16 = jnp.bfloat16


def document_index(doc_lengths, positions):
    doc_ends = jnp.cumsum(doc_lengths)
    counted = jnp.sum((positions[:, None] >= doc_ends[None, :]).astype(jnp.int32), axis=1)
    return jnp.where(positions < 0, -1, counted).astype(jnp.int32)


def from_behind(value, axis, steps):
    count = lax.axis_size(axis)
    pairs = [(source, source + steps) for source in range(0, count - steps)]
    if not pairs:
        return jnp.zeros_like(value)
    return lax.ppermute(value, axis, pairs)


def split_bf16(x):
    hi = x.astype(BF16)
    lo = (x - hi.astype(F32)).astype(BF16)
    return hi, lo


def dot_nt(a, b):
    return lax.dot_general(a, b, (((1,), (1,)), ((), ())), preferred_element_type=F32)


def head_cols(j):
    return slice(j * HD, (j + 1) * HD)


def doc_ends(len_ref, ndocs):
    ends = []
    total = jnp.int32(0)
    for i in range(ndocs):
        total = total + len_ref[i]
        ends.append(total)
    return ends


def doc_of(ends, pos):
    counted = jnp.zeros_like(pos)
    for e in ends:
        counted = counted + (pos >= e).astype(jnp.int32)
    return jnp.where(pos < 0, -1, counted)


def tail_kernel(hpb, ndocs, len_ref, start_ref, k_ref, v_ref, t_ref):
    rows = k_ref.shape[0]
    ends = doc_ends(len_ref, ndocs)
    start = start_ref[0]
    pos = start + lax.broadcasted_iota(jnp.int32, (rows, 1), 0)
    last = doc_of(ends, start + rows - 1)
    mask = (doc_of(ends, pos) == last).astype(BF16)
    for j in range(hpb):
        masked = v_ref[:, head_cols(j)] * mask
        t_ref[j] = lax.dot_general(
            k_ref[:, head_cols(j)], masked, (((0,), (0,)), ((), ())), preferred_element_type=F32
        )


def lin_local_kernel(hpb, ndocs, len_ref, start_ref, q_ref, k_ref, v_ref, lin_ref):
    rows = q_ref.shape[0]
    ends = doc_ends(len_ref, ndocs)
    start = start_ref[0]
    qpos = start + lax.broadcasted_iota(jnp.int32, (rows, 1), 0)
    kpos = start + lax.broadcasted_iota(jnp.int32, (1, rows), 1)
    visible = (doc_of(ends, qpos) == doc_of(ends, kpos)) & (kpos <= qpos)
    for j in range(hpb):
        scores = dot_nt(q_ref[:, head_cols(j)], k_ref[:, head_cols(j)])
        scores = jnp.where(visible, scores, 0.0)
        hi, lo = split_bf16(scores)
        v = v_ref[:, head_cols(j)]
        lin_ref[:, head_cols(j)] = jnp.dot(hi, v, preferred_element_type=F32) + jnp.dot(
            lo, v, preferred_element_type=F32
        )


def lin_finish_kernel(hpb, ndocs, len_ref, start_ref, q_ref, hi_ref, lo_ref, lin_ref, g_ref, o_ref):
    rows = q_ref.shape[0]
    ends = doc_ends(len_ref, ndocs)
    start = start_ref[0]
    pos = start + lax.broadcasted_iota(jnp.int32, (rows, 1), 0)
    sees = (doc_of(ends, pos) == doc_of(ends, start - 1)).astype(F32)
    for j in range(hpb):
        hi, lo = split_bf16(hi_ref[j])
        q = q_ref[:, head_cols(j)]
        carried = jnp.dot(q, hi, preferred_element_type=F32) + jnp.dot(
            q, lo, preferred_element_type=F32
        )
        lin = lin_ref[:, head_cols(j)] + carried * sees
        mean_sq = jnp.mean(lin * lin, axis=-1, keepdims=True)
        normed = lin * lax.rsqrt(mean_sq + 1e-06) * g_ref[:, head_cols(j)]
        o_ref[:, head_cols(j)] = normed.astype(o_ref.dtype)


def col_spec(rows, width=HD):
    return pl.BlockSpec((rows, width), lambda h: (0, h))


def full_spec(shape):
    return pl.BlockSpec(shape, lambda h: (0,) * len(shape))


def params():
    return pltpu.CompilerParams(dimension_semantics=("arbitrary",))


def soft_kernel(blocks, hpb, ndocs, len_ref, start_ref, q_ref, *rest):
    key_refs = rest[0:blocks]
    value_refs = rest[blocks : 2 * blocks]
    o_ref = rest[2 * blocks]
    s_ref, mx_ref, tot_ref, acc_ref = rest[2 * blocks + 1 :]
    rows = q_ref.shape[0]
    scale = 1.0 / math.sqrt(HD)
    ends = doc_ends(len_ref, ndocs)
    start = start_ref[0]
    qpos = start + lax.broadcasted_iota(jnp.int32, (rows, 1), 0)
    kpos = start + lax.broadcasted_iota(jnp.int32, (1, rows), 1)
    dq = doc_of(ends, qpos)
    first_doc = doc_of(ends, start)
    q = jnp.concatenate([q_ref[:, head_cols(j)] for j in range(hpb)], axis=0)

    def block_scores(m):
        shifted = kpos - m * rows
        visible = dq == doc_of(ends, shifted)
        if m == 0:
            visible = visible & (shifted <= qpos)
        s = dot_nt(q, key_refs[m][...].reshape(rows, HD)).reshape(hpb, rows, rows) * scale
        return jnp.where(visible[None], s, -1e30)

    def needed(m):
        return doc_of(ends, start - (m - 1) * rows - 1) == first_doc

    s0 = block_scores(0)
    s_ref[0] = s0
    mx_ref[...] = jnp.max(s0, axis=-1, keepdims=True)
    for m in range(1, blocks):

        @pl.when(needed(m))
        def _():
            s = block_scores(m)
            s_ref[m] = s
            mx_ref[...] = jnp.maximum(mx_ref[...], jnp.max(s, axis=-1, keepdims=True))

    def weighted(m):
        w = jnp.exp(s_ref[m] - mx_ref[...])
        part = jnp.sum(w, axis=-1, keepdims=True)
        term = jnp.dot(
            w.reshape(hpb * rows, rows).astype(BF16),
            value_refs[m][...].reshape(rows, HD),
            preferred_element_type=F32,
        ).reshape(hpb, rows, HD)
        return part, term

    part, term = weighted(0)
    tot_ref[...] = part
    acc_ref[...] = term
    for m in range(1, blocks):

        @pl.when(needed(m))
        def _():
            part, term = weighted(m)
            tot_ref[...] += part
            acc_ref[...] += term

    out = acc_ref[...] / tot_ref[...]
    for j in range(hpb):
        o_ref[:, head_cols(j)] = out[j].astype(o_ref.dtype)


def smem_spec():
    return pl.BlockSpec(memory_space=pltpu.SMEM)


def body(lin_query, lin_key, lin_value, norm_gain, soft_query, soft_key, soft_value, doc_lengths):
    rows, width = lin_query.shape
    local_heads = width // HD
    ndocs = doc_lengths.shape[0]
    lengths = doc_lengths.astype(jnp.int32)
    shard_start = (lax.axis_index("ctx") * rows).astype(jnp.int32).reshape(1)
    ends = jnp.cumsum(lengths)

    def doc_at(pos):
        return jnp.where(pos < 0, -1, jnp.sum((pos >= ends).astype(jnp.int32)))

    through_own = (doc_at(shard_start[0] - 1) == doc_at(shard_start[0] + rows - 1)).astype(F32)

    head_devices = lax.axis_size("head")
    group_size = HEADS // KV_HEADS
    per_device = HEADS // head_devices
    kv_local = max(1, per_device // group_size)
    kv_table = (
        np.arange(head_devices)[:, None] * per_device // group_size + np.arange(kv_local)[None, :]
    ).reshape(-1)
    short_rows = soft_key.shape[0]

    def spread(field):
        if np.array_equal(kv_table, np.arange(KV_HEADS)):
            return field.reshape(short_rows, head_devices, kv_local * HD)
        taken = jnp.take(field.reshape(short_rows, KV_HEADS, HD), kv_table, axis=1)
        return taken.reshape(short_rows, head_devices, kv_local * HD)

    raw = jnp.concatenate([soft_key, soft_value], axis=1)
    shards = [raw]
    for _ in range(SPAN):
        shards.append(from_behind(shards[-1], "ctx", 1))
    pieces = [soft_query.reshape(short_rows, head_devices, per_device * HD)]
    for shard in shards:
        pieces.append(spread(shard[:, : KV_HEADS * HD]))
        pieces.append(spread(shard[:, KV_HEADS * HD :]))
    packed = jnp.concatenate(pieces, axis=2)
    per_dest = packed.shape[2]
    packed = packed.reshape(short_rows, head_devices * per_dest)
    mixed = lax.all_to_all(packed, "head", split_axis=1, concat_axis=0, tiled=True)

    lhpb = min(local_heads, group_size)
    lsteps = local_heads // lhpb
    lwide = lhpb * HD
    tail = pl.pallas_call(
        lambda *refs: tail_kernel(lhpb, ndocs, *refs),
        out_shape=jax.ShapeDtypeStruct((local_heads, HD, HD), F32),
        grid=(lsteps,),
        in_specs=[smem_spec(), smem_spec(), col_spec(rows, lwide), col_spec(rows, lwide)],
        out_specs=pl.BlockSpec((lhpb, HD, HD), lambda h: (h, 0, 0)),
        compiler_params=params(),
        cost_estimate=pl.CostEstimate(
            flops=2 * rows * HD * HD * local_heads,
            transcendentals=0,
            bytes_accessed=2 * rows * width * 2 + local_heads * HD * HD * 4,
        ),
    )(lengths, shard_start, lin_key, lin_value)

    lin_local = pl.pallas_call(
        lambda *refs: lin_local_kernel(lhpb, ndocs, *refs),
        out_shape=jax.ShapeDtypeStruct((rows, width), F32),
        grid=(lsteps,),
        in_specs=[
            smem_spec(),
            smem_spec(),
            col_spec(rows, lwide),
            col_spec(rows, lwide),
            col_spec(rows, lwide),
        ],
        out_specs=col_spec(rows, lwide),
        compiler_params=params(),
        cost_estimate=pl.CostEstimate(
            flops=6 * rows * rows * HD * local_heads,
            transcendentals=0,
            bytes_accessed=3 * rows * width * 2 + rows * width * 4,
        ),
    )(lengths, shard_start, lin_query, lin_key, lin_value)

    received = from_behind(tail, "ctx", 1)
    onward = tail + through_own * received
    lin_local, onward = lax.optimization_barrier((lin_local, onward))
    received = from_behind(onward, "ctx", 1)
    for _ in range(SPAN - 2):
        received = from_behind(tail + through_own * received, "ctx", 1)
    hi_state, lo_state = received, received

    blocks = SPAN + 1
    shpb = min(per_device, group_size)
    ssteps = per_device // shpb
    kv_index = lambda i: (i * shpb * kv_local) // per_device
    def kv_spec(m, value):
        base = per_device + 2 * kv_local * m + (kv_local if value else 0)
        return pl.BlockSpec((rows, HD), lambda i: (0, base + kv_index(i)))

    attended = pl.pallas_call(
        lambda *refs: soft_kernel(blocks, shpb, ndocs, *refs),
        out_shape=jax.ShapeDtypeStruct((rows, per_device * HD), BF16),
        grid=(ssteps,),
        in_specs=[smem_spec(), smem_spec(), col_spec(rows, shpb * HD)]
        + [kv_spec(m, False) for m in range(blocks)]
        + [kv_spec(m, True) for m in range(blocks)],
        out_specs=col_spec(rows, shpb * HD),
        scratch_shapes=[
            pltpu.VMEM((blocks, shpb, rows, rows), F32),
            pltpu.VMEM((shpb, rows, 1), F32),
            pltpu.VMEM((shpb, rows, 1), F32),
            pltpu.VMEM((shpb, rows, HD), F32),
        ],
        compiler_params=pltpu.CompilerParams(
            dimension_semantics=("arbitrary",), vmem_limit_bytes=48 * 1024 * 1024
        ),
        cost_estimate=pl.CostEstimate(
            flops=4 * rows * rows * blocks * HD * per_device,
            transcendentals=rows * rows * blocks * per_device,
            bytes_accessed=rows * per_device * HD * 4 + 2 * blocks * rows * HD * 2 * per_device,
        ),
    )(lengths, shard_start, mixed, *([mixed] * (2 * blocks)))

    lightning_out = pl.pallas_call(
        lambda *refs: lin_finish_kernel(lhpb, ndocs, *refs),
        out_shape=jax.ShapeDtypeStruct((rows, width), BF16),
        grid=(lsteps,),
        in_specs=[
            smem_spec(),
            smem_spec(),
            col_spec(rows, lwide),
            pl.BlockSpec((lhpb, HD, HD), lambda h: (h, 0, 0)),
            pl.BlockSpec((lhpb, HD, HD), lambda h: (h, 0, 0)),
            col_spec(rows, lwide),
            pl.BlockSpec((1, lwide), lambda h: (0, h)),
        ],
        out_specs=col_spec(rows, lwide),
        compiler_params=params(),
        cost_estimate=pl.CostEstimate(
            flops=4 * rows * HD * HD * local_heads,
            transcendentals=rows * local_heads,
            bytes_accessed=rows * width * (2 + 4 + 2) + local_heads * HD * HD * 4,
        ),
    )(lengths, shard_start, lin_query, hi_state, lo_state, lin_local, norm_gain.reshape(1, width))
    return (lightning_out, attended)


def solution(mesh):
    placed = (
        P("ctx", "head"),
        P("ctx", "head"),
        P("ctx", "head"),
        P("head"),
        P(("ctx", "head"), None),
        P(("ctx", "head"), None),
        P(("ctx", "head"), None),
        P(),
    )
    return jax.shard_map(
        body,
        mesh=mesh,
        in_specs=placed,
        out_specs=(P("ctx", "head"), P("ctx", "head")),
        check_vma=False,
    )
```

```python
import math

import jax
import jax.numpy as jnp
import numpy as np
from jax import lax
from jax.experimental import pallas as pl
from jax.experimental.pallas import tpu as pltpu
from jax.sharding import PartitionSpec as P

HEADS = 64
HD = 128
KV_HEADS = 8
SPAN = 3

F32 = jnp.float32
BF16 = jnp.bfloat16


def document_index(doc_lengths, positions):
    doc_ends = jnp.cumsum(doc_lengths)
    counted = jnp.sum((positions[:, None] >= doc_ends[None, :]).astype(jnp.int32), axis=1)
    return jnp.where(positions < 0, -1, counted).astype(jnp.int32)


def from_behind(value, axis, steps):
    count = lax.axis_size(axis)
    pairs = [(source, source + steps) for source in range(0, count - steps)]
    if not pairs:
        return jnp.zeros_like(value)
    return lax.ppermute(value, axis, pairs)


def split_bf16(x):
    hi = x.astype(BF16)
    lo = (x - hi.astype(F32)).astype(BF16)
    return hi, lo


def dot_nt(a, b):
    return lax.dot_general(a, b, (((1,), (1,)), ((), ())), preferred_element_type=F32)


def head_cols(j):
    return slice(j * HD, (j + 1) * HD)


def doc_ends(len_ref, ndocs):
    ends = []
    total = jnp.int32(0)
    for i in range(ndocs):
        total = total + len_ref[i]
        ends.append(total)
    return ends


def doc_of(ends, pos):
    counted = jnp.zeros_like(pos)
    for e in ends:
        counted = counted + (pos >= e).astype(jnp.int32)
    return jnp.where(pos < 0, -1, counted)


def tail_kernel(hpb, ndocs, len_ref, start_ref, k_ref, v_ref, t_ref):
    rows = k_ref.shape[0]
    ends = doc_ends(len_ref, ndocs)
    start = start_ref[0]
    pos = start + lax.broadcasted_iota(jnp.int32, (rows, 1), 0)
    last = doc_of(ends, start + rows - 1)
    mask = (doc_of(ends, pos) == last).astype(BF16)
    for j in range(hpb):
        masked = v_ref[:, head_cols(j)] * mask
        t_ref[j] = lax.dot_general(
            k_ref[:, head_cols(j)], masked, (((0,), (0,)), ((), ())), preferred_element_type=F32
        )


def lin_local_kernel(hpb, ndocs, len_ref, start_ref, q_ref, k_ref, v_ref, lin_ref):
    rows = q_ref.shape[0]
    ends = doc_ends(len_ref, ndocs)
    start = start_ref[0]
    qpos = start + lax.broadcasted_iota(jnp.int32, (rows, 1), 0)
    kpos = start + lax.broadcasted_iota(jnp.int32, (1, rows), 1)
    visible = (doc_of(ends, qpos) == doc_of(ends, kpos)) & (kpos <= qpos)
    for j in range(hpb):
        scores = dot_nt(q_ref[:, head_cols(j)], k_ref[:, head_cols(j)])
        scores = jnp.where(visible, scores, 0.0)
        hi, lo = split_bf16(scores)
        v = v_ref[:, head_cols(j)]
        lin_ref[:, head_cols(j)] = jnp.dot(hi, v, preferred_element_type=F32) + jnp.dot(
            lo, v, preferred_element_type=F32
        )


def lin_finish_kernel(hpb, ndocs, len_ref, start_ref, q_ref, hi_ref, lo_ref, lin_ref, g_ref, o_ref):
    rows = q_ref.shape[0]
    ends = doc_ends(len_ref, ndocs)
    start = start_ref[0]
    pos = start + lax.broadcasted_iota(jnp.int32, (rows, 1), 0)
    sees = (doc_of(ends, pos) == doc_of(ends, start - 1)).astype(F32)
    for j in range(hpb):
        hi, lo = split_bf16(hi_ref[j])
        q = q_ref[:, head_cols(j)]
        carried = jnp.dot(q, hi, preferred_element_type=F32) + jnp.dot(
            q, lo, preferred_element_type=F32
        )
        lin = lin_ref[:, head_cols(j)] + carried * sees
        mean_sq = jnp.mean(lin * lin, axis=-1, keepdims=True)
        normed = lin * lax.rsqrt(mean_sq + 1e-06) * g_ref[:, head_cols(j)]
        o_ref[:, head_cols(j)] = normed.astype(o_ref.dtype)


def col_spec(rows, width=HD):
    return pl.BlockSpec((rows, width), lambda h: (0, h))


def full_spec(shape):
    return pl.BlockSpec(shape, lambda h: (0,) * len(shape))


def params():
    return pltpu.CompilerParams(dimension_semantics=("arbitrary",))


def soft_kernel(blocks, hpb, ndocs, len_ref, start_ref, q_ref, *rest):
    key_refs = rest[0:blocks]
    value_refs = rest[blocks : 2 * blocks]
    o_ref = rest[2 * blocks]
    s_ref, mx_ref, tot_ref, acc_ref = rest[2 * blocks + 1 :]
    rows = q_ref.shape[0]
    scale = 1.0 / math.sqrt(HD)
    ends = doc_ends(len_ref, ndocs)
    start = start_ref[0]
    qpos = start + lax.broadcasted_iota(jnp.int32, (rows, 1), 0)
    kpos = start + lax.broadcasted_iota(jnp.int32, (1, rows), 1)
    dq = doc_of(ends, qpos)
    first_doc = doc_of(ends, start)
    q = jnp.concatenate([q_ref[:, head_cols(j)] for j in range(hpb)], axis=0)

    def block_scores(m):
        shifted = kpos - m * rows
        visible = dq == doc_of(ends, shifted)
        if m == 0:
            visible = visible & (shifted <= qpos)
        s = dot_nt(q, key_refs[m][...].reshape(rows, HD)).reshape(hpb, rows, rows) * scale
        return jnp.where(visible[None], s, -1e30)

    def needed(m):
        return doc_of(ends, start - (m - 1) * rows - 1) == first_doc

    s0 = block_scores(0)
    s_ref[0] = s0
    mx_ref[...] = jnp.max(s0, axis=-1, keepdims=True)
    for m in range(1, blocks):

        @pl.when(needed(m))
        def _():
            s = block_scores(m)
            s_ref[m] = s
            mx_ref[...] = jnp.maximum(mx_ref[...], jnp.max(s, axis=-1, keepdims=True))

    def weighted(m):
        w = jnp.exp(s_ref[m] - mx_ref[...])
        part = jnp.sum(w, axis=-1, keepdims=True)
        term = jnp.dot(
            w.reshape(hpb * rows, rows).astype(BF16),
            value_refs[m][...].reshape(rows, HD),
            preferred_element_type=F32,
        ).reshape(hpb, rows, HD)
        return part, term

    part, term = weighted(0)
    tot_ref[...] = part
    acc_ref[...] = term
    for m in range(1, blocks):

        @pl.when(needed(m))
        def _():
            part, term = weighted(m)
            tot_ref[...] += part
            acc_ref[...] += term

    out = acc_ref[...] / tot_ref[...]
    for j in range(hpb):
        o_ref[:, head_cols(j)] = out[j].astype(o_ref.dtype)


def smem_spec():
    return pl.BlockSpec(memory_space=pltpu.SMEM)


def body(lin_query, lin_key, lin_value, norm_gain, soft_query, soft_key, soft_value, doc_lengths):
    rows, width = lin_query.shape
    local_heads = width // HD
    ndocs = doc_lengths.shape[0]
    lengths = doc_lengths.astype(jnp.int32)
    shard_start = (lax.axis_index("ctx") * rows).astype(jnp.int32).reshape(1)
    ends = jnp.cumsum(lengths)

    def doc_at(pos):
        return jnp.where(pos < 0, -1, jnp.sum((pos >= ends).astype(jnp.int32)))

    through_own = (doc_at(shard_start[0] - 1) == doc_at(shard_start[0] + rows - 1)).astype(F32)

    head_devices = lax.axis_size("head")
    group_size = HEADS // KV_HEADS
    per_device = HEADS // head_devices
    kv_local = max(1, per_device // group_size)
    kv_table = (
        np.arange(head_devices)[:, None] * per_device // group_size + np.arange(kv_local)[None, :]
    ).reshape(-1)
    short_rows = soft_key.shape[0]

    def spread(field):
        if np.array_equal(kv_table, np.arange(KV_HEADS)):
            return field.reshape(short_rows, head_devices, kv_local * HD)
        taken = jnp.take(field.reshape(short_rows, KV_HEADS, HD), kv_table, axis=1)
        return taken.reshape(short_rows, head_devices, kv_local * HD)

    packed = jnp.concatenate(
        [
            soft_query.reshape(short_rows, head_devices, per_device * HD),
            spread(soft_key),
            spread(soft_value),
        ],
        axis=2,
    )
    per_dest = packed.shape[2]
    packed = packed.reshape(short_rows, head_devices * per_dest)
    mixed = lax.all_to_all(packed, "head", split_axis=1, concat_axis=0, tiled=True)
    own_kv = mixed[:, per_device * HD :]
    kv_width = own_kv.shape[1]

    n_ctx = lax.axis_size("ctx")
    even_to_odd = [(c, c + 1) for c in range(0, n_ctx - 1, 2)]
    odd_to_next = [(c, c + 1) for c in range(1, n_ctx - 1, 2)]
    even_to_even = [(c, c + 2) for c in range(0, n_ctx - 2, 2)]
    is_odd = lax.rem(lax.axis_index("ctx"), 2) == 1

    def send(value, pairs):
        if not pairs:
            return jnp.zeros_like(value)
        return lax.ppermute(value, "ctx", pairs)

    kv_a = send(own_kv, even_to_odd)
    kv_b = send(jnp.concatenate([own_kv, kv_a], axis=1), odd_to_next)
    kv_c1 = send(kv_b[:, :kv_width], even_to_even)
    kv_c2 = send(kv_b, even_to_odd)
    older = [
        jnp.where(is_odd, kv_a, kv_b[:, :kv_width]),
        jnp.where(is_odd, kv_c2[:, :kv_width], kv_b[:, kv_width:]),
        jnp.where(is_odd, kv_c2[:, kv_width:], kv_c1),
    ]

    lhpb = min(local_heads, group_size)
    lsteps = local_heads // lhpb
    lwide = lhpb * HD
    tail = pl.pallas_call(
        lambda *refs: tail_kernel(lhpb, ndocs, *refs),
        out_shape=jax.ShapeDtypeStruct((local_heads, HD, HD), F32),
        grid=(lsteps,),
        in_specs=[smem_spec(), smem_spec(), col_spec(rows, lwide), col_spec(rows, lwide)],
        out_specs=pl.BlockSpec((lhpb, HD, HD), lambda h: (h, 0, 0)),
        compiler_params=params(),
        cost_estimate=pl.CostEstimate(
            flops=2 * rows * HD * HD * local_heads,
            transcendentals=0,
            bytes_accessed=2 * rows * width * 2 + local_heads * HD * HD * 4,
        ),
    )(lengths, shard_start, lin_key, lin_value)

    lin_local = pl.pallas_call(
        lambda *refs: lin_local_kernel(lhpb, ndocs, *refs),
        out_shape=jax.ShapeDtypeStruct((rows, width), F32),
        grid=(lsteps,),
        in_specs=[
            smem_spec(),
            smem_spec(),
            col_spec(rows, lwide),
            col_spec(rows, lwide),
            col_spec(rows, lwide),
        ],
        out_specs=col_spec(rows, lwide),
        compiler_params=params(),
        cost_estimate=pl.CostEstimate(
            flops=6 * rows * rows * HD * local_heads,
            transcendentals=0,
            bytes_accessed=3 * rows * width * 2 + rows * width * 4,
        ),
    )(lengths, shard_start, lin_query, lin_key, lin_value)

    def through(shard):
        first = shard * rows
        return (doc_at(first - 1) == doc_at(first + rows - 1)).astype(F32)

    here = lax.axis_index("ctx")
    state_a = send(tail, even_to_odd)
    state_v = tail + through_own * state_a
    lin_local, state_v = lax.optimization_barrier((lin_local, state_v))
    state_b = send(state_v, odd_to_next)
    state_c1 = send(through(here) * through(here + 1) * state_b, even_to_even)
    state_c2 = send(state_b, even_to_odd)
    carried = jnp.where(is_odd, state_a + through(here - 1) * state_c2, state_b + state_c1)
    hi_state, lo_state = carried, carried

    blocks = SPAN + 1
    shpb = min(per_device, group_size)
    ssteps = per_device // shpb
    kv_index = lambda i: (i * shpb * kv_local) // per_device
    def kv_spec(m, value):
        base = (per_device if m == 0 else 0) + (kv_local if value else 0)
        return pl.BlockSpec((rows, HD), lambda i: (0, base + kv_index(i)))

    attended = pl.pallas_call(
        lambda *refs: soft_kernel(blocks, shpb, ndocs, *refs),
        out_shape=jax.ShapeDtypeStruct((rows, per_device * HD), BF16),
        grid=(ssteps,),
        in_specs=[smem_spec(), smem_spec(), col_spec(rows, shpb * HD)]
        + [kv_spec(m, False) for m in range(blocks)]
        + [kv_spec(m, True) for m in range(blocks)],
        out_specs=col_spec(rows, shpb * HD),
        scratch_shapes=[
            pltpu.VMEM((blocks, shpb, rows, rows), F32),
            pltpu.VMEM((shpb, rows, 1), F32),
            pltpu.VMEM((shpb, rows, 1), F32),
            pltpu.VMEM((shpb, rows, HD), F32),
        ],
        compiler_params=pltpu.CompilerParams(
            dimension_semantics=("arbitrary",), vmem_limit_bytes=48 * 1024 * 1024
        ),
        cost_estimate=pl.CostEstimate(
            flops=4 * rows * rows * blocks * HD * per_device,
            transcendentals=rows * rows * blocks * per_device,
            bytes_accessed=rows * per_device * HD * 4 + 2 * blocks * rows * HD * 2 * per_device,
        ),
    )(lengths, shard_start, mixed, mixed, *older, mixed, *older)

    lightning_out = pl.pallas_call(
        lambda *refs: lin_finish_kernel(lhpb, ndocs, *refs),
        out_shape=jax.ShapeDtypeStruct((rows, width), BF16),
        grid=(lsteps,),
        in_specs=[
            smem_spec(),
            smem_spec(),
            col_spec(rows, lwide),
            pl.BlockSpec((lhpb, HD, HD), lambda h: (h, 0, 0)),
            pl.BlockSpec((lhpb, HD, HD), lambda h: (h, 0, 0)),
            col_spec(rows, lwide),
            pl.BlockSpec((1, lwide), lambda h: (0, h)),
        ],
        out_specs=col_spec(rows, lwide),
        compiler_params=params(),
        cost_estimate=pl.CostEstimate(
            flops=4 * rows * HD * HD * local_heads,
            transcendentals=rows * local_heads,
            bytes_accessed=rows * width * (2 + 4 + 2) + local_heads * HD * HD * 4,
        ),
    )(lengths, shard_start, lin_query, hi_state, lo_state, lin_local, norm_gain.reshape(1, width))
    return (lightning_out, attended)


def solution(mesh):
    placed = (
        P("ctx", "head"),
        P("ctx", "head"),
        P("ctx", "head"),
        P("head"),
        P(("ctx", "head"), None),
        P(("ctx", "head"), None),
        P(("ctx", "head"), None),
        P(),
    )
    return jax.shard_map(
        body,
        mesh=mesh,
        in_specs=placed,
        out_specs=(P("ctx", "head"), P("ctx", "head")),
        check_vma=False,
    )
```

```python
import math

import jax
import jax.numpy as jnp
import numpy as np
from jax import lax
from jax.experimental import pallas as pl
from jax.experimental.pallas import tpu as pltpu
from jax.sharding import PartitionSpec as P

HEADS = 64
HD = 128
KV_HEADS = 8
SPAN = 3

F32 = jnp.float32
BF16 = jnp.bfloat16


def document_index(doc_lengths, positions):
    doc_ends = jnp.cumsum(doc_lengths)
    counted = jnp.sum((positions[:, None] >= doc_ends[None, :]).astype(jnp.int32), axis=1)
    return jnp.where(positions < 0, -1, counted).astype(jnp.int32)


def from_behind(value, axis, steps):
    count = lax.axis_size(axis)
    pairs = [(source, source + steps) for source in range(0, count - steps)]
    if not pairs:
        return jnp.zeros_like(value)
    return lax.ppermute(value, axis, pairs)


def split_bf16(x):
    hi = x.astype(BF16)
    lo = (x - hi.astype(F32)).astype(BF16)
    return hi, lo


def dot_nt(a, b):
    return lax.dot_general(a, b, (((1,), (1,)), ((), ())), preferred_element_type=F32)


def head_cols(j):
    return slice(j * HD, (j + 1) * HD)


def doc_ends(len_ref, ndocs):
    ends = []
    total = jnp.int32(0)
    for i in range(ndocs):
        total = total + len_ref[i]
        ends.append(total)
    return ends


def doc_of(ends, pos):
    counted = jnp.zeros_like(pos)
    for e in ends:
        counted = counted + (pos >= e).astype(jnp.int32)
    return jnp.where(pos < 0, -1, counted)


def tail_kernel(hpb, ndocs, len_ref, start_ref, k_ref, v_ref, t_ref):
    rows = k_ref.shape[0]
    ends = doc_ends(len_ref, ndocs)
    start = start_ref[0]
    pos = start + lax.broadcasted_iota(jnp.int32, (rows, 1), 0)
    last = doc_of(ends, start + rows - 1)
    mask = (doc_of(ends, pos) == last).astype(BF16)
    for j in range(hpb):
        masked = v_ref[:, head_cols(j)] * mask
        t_ref[j] = lax.dot_general(
            k_ref[:, head_cols(j)], masked, (((0,), (0,)), ((), ())), preferred_element_type=F32
        )


def lin_local_kernel(hpb, ndocs, len_ref, start_ref, q_ref, k_ref, v_ref, lin_ref):
    rows = q_ref.shape[0]
    ends = doc_ends(len_ref, ndocs)
    start = start_ref[0]
    qpos = start + lax.broadcasted_iota(jnp.int32, (rows, 1), 0)
    kpos = start + lax.broadcasted_iota(jnp.int32, (1, rows), 1)
    visible = (doc_of(ends, qpos) == doc_of(ends, kpos)) & (kpos <= qpos)
    for j in range(hpb):
        scores = dot_nt(q_ref[:, head_cols(j)], k_ref[:, head_cols(j)])
        scores = jnp.where(visible, scores, 0.0)
        hi, lo = split_bf16(scores)
        v = v_ref[:, head_cols(j)]
        lin_ref[:, head_cols(j)] = jnp.dot(hi, v, preferred_element_type=F32) + jnp.dot(
            lo, v, preferred_element_type=F32
        )


def lin_finish_kernel(
    hpb, ndocs, len_ref, start_ref, q_ref, a_ref, c2_ref, b_ref, c1_ref, lin_ref, g_ref, o_ref
):
    rows = q_ref.shape[0]
    ends = doc_ends(len_ref, ndocs)
    start = start_ref[0]
    pos = start + lax.broadcasted_iota(jnp.int32, (rows, 1), 0)
    sees = (doc_of(ends, pos) == doc_of(ends, start - 1)).astype(F32)
    odd = lax.rem(start // rows, 2) == 1
    through_prev = (doc_of(ends, start - rows - 1) == doc_of(ends, start - 1)).astype(F32)
    for j in range(hpb):
        state = jnp.where(odd, a_ref[j] + through_prev * c2_ref[j], b_ref[j] + c1_ref[j])
        hi, lo = split_bf16(state)
        q = q_ref[:, head_cols(j)]
        carried = jnp.dot(q, hi, preferred_element_type=F32) + jnp.dot(
            q, lo, preferred_element_type=F32
        )
        lin = lin_ref[:, head_cols(j)] + carried * sees
        mean_sq = jnp.mean(lin * lin, axis=-1, keepdims=True)
        normed = lin * lax.rsqrt(mean_sq + 1e-06) * g_ref[:, head_cols(j)]
        o_ref[:, head_cols(j)] = normed.astype(o_ref.dtype)


def col_spec(rows, width=HD):
    return pl.BlockSpec((rows, width), lambda h: (0, h))


def full_spec(shape):
    return pl.BlockSpec(shape, lambda h: (0,) * len(shape))


def params():
    return pltpu.CompilerParams(dimension_semantics=("arbitrary",))


def soft_kernel(blocks, hpb, ndocs, len_ref, start_ref, q_ref, *rest):
    per_kind = 2 * blocks - 1
    o_ref = rest[2 * per_kind]
    s_ref, mx_ref, tot_ref, acc_ref = rest[2 * per_kind + 1 :]
    rows = q_ref.shape[0]
    odd = lax.rem(start_ref[0] // rows, 2) == 1

    def pick(refs):
        picked = [lambda: refs[0][...]]
        for m in range(1, blocks):
            picked.append(
                lambda m=m: jnp.where(odd, refs[2 * m - 1][...], refs[2 * m][...])
            )
        return picked

    key_refs = pick(rest[0:per_kind])
    value_refs = pick(rest[per_kind : 2 * per_kind])
    scale = 1.0 / math.sqrt(HD)
    ends = doc_ends(len_ref, ndocs)
    start = start_ref[0]
    qpos = start + lax.broadcasted_iota(jnp.int32, (rows, 1), 0)
    kpos = start + lax.broadcasted_iota(jnp.int32, (1, rows), 1)
    dq = doc_of(ends, qpos)
    first_doc = doc_of(ends, start)
    q = jnp.concatenate([q_ref[:, head_cols(j)] for j in range(hpb)], axis=0)

    def block_scores(m):
        shifted = kpos - m * rows
        visible = dq == doc_of(ends, shifted)
        if m == 0:
            visible = visible & (shifted <= qpos)
        s = dot_nt(q, key_refs[m]()).reshape(hpb, rows, rows) * scale
        return jnp.where(visible[None], s, -1e30)

    def needed(m):
        return doc_of(ends, start - (m - 1) * rows - 1) == first_doc

    s0 = block_scores(0)
    s_ref[0] = s0
    mx_ref[...] = jnp.max(s0, axis=-1, keepdims=True)
    for m in range(1, blocks):

        @pl.when(needed(m))
        def _():
            s = block_scores(m)
            s_ref[m] = s
            mx_ref[...] = jnp.maximum(mx_ref[...], jnp.max(s, axis=-1, keepdims=True))

    def weighted(m):
        w = jnp.exp(s_ref[m] - mx_ref[...])
        part = jnp.sum(w, axis=-1, keepdims=True)
        term = jnp.dot(
            w.reshape(hpb * rows, rows).astype(BF16),
            value_refs[m](),
            preferred_element_type=F32,
        ).reshape(hpb, rows, HD)
        return part, term

    part, term = weighted(0)
    tot_ref[...] = part
    acc_ref[...] = term
    for m in range(1, blocks):

        @pl.when(needed(m))
        def _():
            part, term = weighted(m)
            tot_ref[...] += part
            acc_ref[...] += term

    out = acc_ref[...] / tot_ref[...]
    for j in range(hpb):
        o_ref[:, head_cols(j)] = out[j].astype(o_ref.dtype)


def smem_spec():
    return pl.BlockSpec(memory_space=pltpu.SMEM)


def body(lin_query, lin_key, lin_value, norm_gain, soft_query, soft_key, soft_value, doc_lengths):
    rows, width = lin_query.shape
    local_heads = width // HD
    ndocs = doc_lengths.shape[0]
    lengths = doc_lengths.astype(jnp.int32)
    shard_start = (lax.axis_index("ctx") * rows).astype(jnp.int32).reshape(1)
    ends = jnp.cumsum(lengths)

    def doc_at(pos):
        return jnp.where(pos < 0, -1, jnp.sum((pos >= ends).astype(jnp.int32)))

    through_own = (doc_at(shard_start[0] - 1) == doc_at(shard_start[0] + rows - 1)).astype(F32)

    head_devices = lax.axis_size("head")
    group_size = HEADS // KV_HEADS
    per_device = HEADS // head_devices
    kv_local = max(1, per_device // group_size)
    kv_table = (
        np.arange(head_devices)[:, None] * per_device // group_size + np.arange(kv_local)[None, :]
    ).reshape(-1)
    short_rows = soft_key.shape[0]

    def spread(field):
        if np.array_equal(kv_table, np.arange(KV_HEADS)):
            return field.reshape(short_rows, head_devices, kv_local * HD)
        taken = jnp.take(field.reshape(short_rows, KV_HEADS, HD), kv_table, axis=1)
        return taken.reshape(short_rows, head_devices, kv_local * HD)

    kv_packed = jnp.concatenate([spread(soft_key), spread(soft_value)], axis=2)
    kv_packed = kv_packed.reshape(short_rows, head_devices * 2 * kv_local * HD)
    own_kv = lax.all_to_all(kv_packed, "head", split_axis=1, concat_axis=0, tiled=True)
    mixed = lax.all_to_all(soft_query, "head", split_axis=1, concat_axis=0, tiled=True)
    kv_width = own_kv.shape[1]

    n_ctx = lax.axis_size("ctx")
    even_to_odd = [(c, c + 1) for c in range(0, n_ctx - 1, 2)]
    odd_to_next = [(c, c + 1) for c in range(1, n_ctx - 1, 2)]
    even_to_even = [(c, c + 2) for c in range(0, n_ctx - 2, 2)]
    is_odd = lax.rem(lax.axis_index("ctx"), 2) == 1

    def send(value, pairs):
        if not pairs:
            return jnp.zeros_like(value)
        return lax.ppermute(value, "ctx", pairs)

    kv_a = send(own_kv, even_to_odd)
    kv_b = send(jnp.concatenate([own_kv, kv_a], axis=1), odd_to_next)
    kv_c1 = send(kv_b[:, :kv_width], even_to_even)
    kv_c2 = send(kv_b, even_to_odd)
    odd_src = [(own_kv, 0), (kv_a, 0), (kv_c2, 0), (kv_c2, 2 * kv_local)]
    even_src = [(own_kv, 0), (kv_b, 0), (kv_b, 2 * kv_local), (kv_c1, 0)]

    lhpb = min(local_heads, group_size)
    lsteps = local_heads // lhpb
    lwide = lhpb * HD
    tail = pl.pallas_call(
        lambda *refs: tail_kernel(lhpb, ndocs, *refs),
        out_shape=jax.ShapeDtypeStruct((local_heads, HD, HD), F32),
        grid=(lsteps,),
        in_specs=[smem_spec(), smem_spec(), col_spec(rows, lwide), col_spec(rows, lwide)],
        out_specs=pl.BlockSpec((lhpb, HD, HD), lambda h: (h, 0, 0)),
        compiler_params=params(),
        cost_estimate=pl.CostEstimate(
            flops=2 * rows * HD * HD * local_heads,
            transcendentals=0,
            bytes_accessed=2 * rows * width * 2 + local_heads * HD * HD * 4,
        ),
    )(lengths, shard_start, lin_key, lin_value)

    lin_local = pl.pallas_call(
        lambda *refs: lin_local_kernel(lhpb, ndocs, *refs),
        out_shape=jax.ShapeDtypeStruct((rows, width), F32),
        grid=(lsteps,),
        in_specs=[
            smem_spec(),
            smem_spec(),
            col_spec(rows, lwide),
            col_spec(rows, lwide),
            col_spec(rows, lwide),
        ],
        out_specs=col_spec(rows, lwide),
        compiler_params=params(),
        cost_estimate=pl.CostEstimate(
            flops=6 * rows * rows * HD * local_heads,
            transcendentals=0,
            bytes_accessed=3 * rows * width * 2 + rows * width * 4,
        ),
    )(lengths, shard_start, lin_query, lin_key, lin_value)

    def through(shard):
        first = shard * rows
        return (doc_at(first - 1) == doc_at(first + rows - 1)).astype(F32)

    here = lax.axis_index("ctx")
    state_a = send(tail, even_to_odd)
    state_v = tail + through_own * state_a
    lin_local, state_v = lax.optimization_barrier((lin_local, state_v))
    state_b = send(state_v, odd_to_next)
    state_c1 = send(through(here) * through(here + 1) * state_b, even_to_even)
    state_c2 = send(state_b, even_to_odd)

    blocks = SPAN + 1
    shpb = min(per_device, group_size)
    ssteps = per_device // shpb
    kv_index = lambda i: (i * shpb * kv_local) // per_device
    def kv_spec(offset, value):
        base = offset + (kv_local if value else 0)
        return pl.BlockSpec((rows, HD), lambda i: (0, base + kv_index(i)))

    kv_arrays, kv_specs = [], []
    for value in (False, True):
        for m in range(blocks):
            for source in ((odd_src[m],) if m == 0 else (odd_src[m], even_src[m])):
                kv_arrays.append(source[0])
                kv_specs.append(kv_spec(source[1], value))

    attended = pl.pallas_call(
        lambda *refs: soft_kernel(blocks, shpb, ndocs, *refs),
        out_shape=jax.ShapeDtypeStruct((rows, per_device * HD), BF16),
        grid=(ssteps,),
        in_specs=[smem_spec(), smem_spec(), col_spec(rows, shpb * HD)] + kv_specs,
        out_specs=col_spec(rows, shpb * HD),
        scratch_shapes=[
            pltpu.VMEM((blocks, shpb, rows, rows), F32),
            pltpu.VMEM((shpb, rows, 1), F32),
            pltpu.VMEM((shpb, rows, 1), F32),
            pltpu.VMEM((shpb, rows, HD), F32),
        ],
        compiler_params=pltpu.CompilerParams(
            dimension_semantics=("arbitrary",), vmem_limit_bytes=48 * 1024 * 1024
        ),
        cost_estimate=pl.CostEstimate(
            flops=4 * rows * rows * blocks * HD * per_device,
            transcendentals=rows * rows * blocks * per_device,
            bytes_accessed=rows * per_device * HD * 4 + 2 * blocks * rows * HD * 2 * per_device,
        ),
    )(lengths, shard_start, mixed, *kv_arrays)

    lightning_out = pl.pallas_call(
        lambda *refs: lin_finish_kernel(lhpb, ndocs, *refs),
        out_shape=jax.ShapeDtypeStruct((rows, width), BF16),
        grid=(lsteps,),
        in_specs=[
            smem_spec(),
            smem_spec(),
            col_spec(rows, lwide),
            pl.BlockSpec((lhpb, HD, HD), lambda h: (h, 0, 0)),
            pl.BlockSpec((lhpb, HD, HD), lambda h: (h, 0, 0)),
            pl.BlockSpec((lhpb, HD, HD), lambda h: (h, 0, 0)),
            pl.BlockSpec((lhpb, HD, HD), lambda h: (h, 0, 0)),
            col_spec(rows, lwide),
            pl.BlockSpec((1, lwide), lambda h: (0, h)),
        ],
        out_specs=col_spec(rows, lwide),
        compiler_params=params(),
        cost_estimate=pl.CostEstimate(
            flops=4 * rows * HD * HD * local_heads,
            transcendentals=rows * local_heads,
            bytes_accessed=rows * width * (2 + 4 + 2) + local_heads * HD * HD * 4,
        ),
    )(
        lengths,
        shard_start,
        lin_query,
        state_a,
        state_c2,
        state_b,
        state_c1,
        lin_local,
        norm_gain.reshape(1, width),
    )
    return (lightning_out, attended)


def solution(mesh):
    placed = (
        P("ctx", "head"),
        P("ctx", "head"),
        P("ctx", "head"),
        P("head"),
        P(("ctx", "head"), None),
        P(("ctx", "head"), None),
        P(("ctx", "head"), None),
        P(),
    )
    return jax.shard_map(
        body,
        mesh=mesh,
        in_specs=placed,
        out_specs=(P("ctx", "head"), P("ctx", "head")),
        check_vma=False,
    )
```

```python
import math

import jax
import jax.numpy as jnp
import numpy as np
from jax import lax
from jax.experimental import pallas as pl
from jax.experimental.pallas import tpu as pltpu
from jax.sharding import PartitionSpec as P

HEADS = 64
HD = 128
KV_HEADS = 8
SPAN = 3

F32 = jnp.float32
BF16 = jnp.bfloat16


def document_index(doc_lengths, positions):
    doc_ends = jnp.cumsum(doc_lengths)
    counted = jnp.sum((positions[:, None] >= doc_ends[None, :]).astype(jnp.int32), axis=1)
    return jnp.where(positions < 0, -1, counted).astype(jnp.int32)


def from_behind(value, axis, steps):
    count = lax.axis_size(axis)
    pairs = [(source, source + steps) for source in range(0, count - steps)]
    if not pairs:
        return jnp.zeros_like(value)
    return lax.ppermute(value, axis, pairs)


def split_bf16(x):
    hi = x.astype(BF16)
    lo = (x - hi.astype(F32)).astype(BF16)
    return hi, lo


def dot_nt(a, b):
    return lax.dot_general(a, b, (((1,), (1,)), ((), ())), preferred_element_type=F32)


def head_cols(j):
    return slice(j * HD, (j + 1) * HD)


def doc_ends(len_ref, ndocs):
    ends = []
    total = jnp.int32(0)
    for i in range(ndocs):
        total = total + len_ref[i]
        ends.append(total)
    return ends


def doc_of(ends, pos):
    counted = jnp.zeros_like(pos)
    for e in ends:
        counted = counted + (pos >= e).astype(jnp.int32)
    return jnp.where(pos < 0, -1, counted)


def tail_kernel(hpb, ndocs, len_ref, start_ref, k_ref, v_ref, t_ref):
    rows = k_ref.shape[0]
    ends = doc_ends(len_ref, ndocs)
    start = start_ref[0]
    pos = start + lax.broadcasted_iota(jnp.int32, (rows, 1), 0)
    last = doc_of(ends, start + rows - 1)
    mask = (doc_of(ends, pos) == last).astype(BF16)
    for j in range(hpb):
        masked = v_ref[:, head_cols(j)] * mask
        t_ref[j] = lax.dot_general(
            k_ref[:, head_cols(j)], masked, (((0,), (0,)), ((), ())), preferred_element_type=F32
        )


def lin_local_kernel(hpb, ndocs, len_ref, start_ref, q_ref, k_ref, v_ref, lin_ref):
    rows = q_ref.shape[0]
    ends = doc_ends(len_ref, ndocs)
    start = start_ref[0]
    qpos = start + lax.broadcasted_iota(jnp.int32, (rows, 1), 0)
    kpos = start + lax.broadcasted_iota(jnp.int32, (1, rows), 1)
    visible = (doc_of(ends, qpos) == doc_of(ends, kpos)) & (kpos <= qpos)
    for j in range(hpb):
        scores = dot_nt(q_ref[:, head_cols(j)], k_ref[:, head_cols(j)])
        scores = jnp.where(visible, scores, 0.0)
        hi, lo = split_bf16(scores)
        v = v_ref[:, head_cols(j)]
        lin_ref[:, head_cols(j)] = jnp.dot(hi, v, preferred_element_type=F32) + jnp.dot(
            lo, v, preferred_element_type=F32
        )


def lin_finish_kernel(
    hpb, ndocs, len_ref, start_ref, q_ref, a_ref, c2_ref, b_ref, c1_ref, lin_ref, g_ref, o_ref
):
    rows = q_ref.shape[0]
    ends = doc_ends(len_ref, ndocs)
    start = start_ref[0]
    pos = start + lax.broadcasted_iota(jnp.int32, (rows, 1), 0)
    sees = (doc_of(ends, pos) == doc_of(ends, start - 1)).astype(F32)
    odd = lax.rem(start // rows, 2) == 1
    through_prev = (doc_of(ends, start - rows - 1) == doc_of(ends, start - 1)).astype(F32)
    for j in range(hpb):
        state = jnp.where(odd, a_ref[j] + through_prev * c2_ref[j], b_ref[j] + c1_ref[j])
        hi, lo = split_bf16(state)
        q = q_ref[:, head_cols(j)]
        carried = jnp.dot(q, hi, preferred_element_type=F32) + jnp.dot(
            q, lo, preferred_element_type=F32
        )
        lin = lin_ref[:, head_cols(j)] + carried * sees
        mean_sq = jnp.mean(lin * lin, axis=-1, keepdims=True)
        normed = lin * lax.rsqrt(mean_sq + 1e-06) * g_ref[:, head_cols(j)]
        o_ref[:, head_cols(j)] = normed.astype(o_ref.dtype)


def col_spec(rows, width=HD):
    return pl.BlockSpec((rows, width), lambda h: (0, h))


def full_spec(shape):
    return pl.BlockSpec(shape, lambda h: (0,) * len(shape))


def params():
    return pltpu.CompilerParams(dimension_semantics=("arbitrary",))


def soft_kernel(blocks, hpb, ndocs, len_ref, start_ref, q_ref, *rest):
    per_kind = 2 * blocks - 1
    o_ref = rest[2 * per_kind]
    s_ref, mx_ref, tot_ref, acc_ref = rest[2 * per_kind + 1 :]
    rows = q_ref.shape[0]
    odd = lax.rem(start_ref[0] // rows, 2) == 1

    def pick(refs):
        picked = [lambda: refs[0][...]]
        for m in range(1, blocks):
            picked.append(
                lambda m=m: jnp.where(odd, refs[2 * m - 1][...], refs[2 * m][...])
            )
        return picked

    key_refs = pick(rest[0:per_kind])
    value_refs = pick(rest[per_kind : 2 * per_kind])
    scale = 1.0 / math.sqrt(HD)
    ends = doc_ends(len_ref, ndocs)
    start = start_ref[0]
    qpos = start + lax.broadcasted_iota(jnp.int32, (rows, 1), 0)
    kpos = start + lax.broadcasted_iota(jnp.int32, (1, rows), 1)
    dq = doc_of(ends, qpos)
    first_doc = doc_of(ends, start)
    q = jnp.concatenate([q_ref[:, head_cols(j)] for j in range(hpb)], axis=0)

    def block_scores(m):
        shifted = kpos - m * rows
        visible = dq == doc_of(ends, shifted)
        if m == 0:
            visible = visible & (shifted <= qpos)
        s = dot_nt(q, key_refs[m]()).reshape(hpb, rows, rows) * scale
        return jnp.where(visible[None], s, -1e30)

    def needed(m):
        return doc_of(ends, start - (m - 1) * rows - 1) == first_doc

    s0 = block_scores(0)
    s_ref[0] = s0
    mx_ref[...] = jnp.max(s0, axis=-1, keepdims=True)
    for m in range(1, blocks):

        @pl.when(needed(m))
        def _():
            s = block_scores(m)
            s_ref[m] = s
            mx_ref[...] = jnp.maximum(mx_ref[...], jnp.max(s, axis=-1, keepdims=True))

    def weighted(m):
        w = jnp.exp(s_ref[m] - mx_ref[...])
        part = jnp.sum(w, axis=-1, keepdims=True)
        term = jnp.dot(
            w.reshape(hpb * rows, rows).astype(BF16),
            value_refs[m](),
            preferred_element_type=F32,
        ).reshape(hpb, rows, HD)
        return part, term

    part, term = weighted(0)
    tot_ref[...] = part
    acc_ref[...] = term
    for m in range(1, blocks):

        @pl.when(needed(m))
        def _():
            part, term = weighted(m)
            tot_ref[...] += part
            acc_ref[...] += term

    out = acc_ref[...] / tot_ref[...]
    for j in range(hpb):
        o_ref[:, head_cols(j)] = out[j].astype(o_ref.dtype)


def smem_spec():
    return pl.BlockSpec(memory_space=pltpu.SMEM)


def body(lin_query, lin_key, lin_value, norm_gain, soft_query, soft_key, soft_value, doc_lengths):
    rows, width = lin_query.shape
    local_heads = width // HD
    ndocs = doc_lengths.shape[0]
    lengths = doc_lengths.astype(jnp.int32)
    shard_start = (lax.axis_index("ctx") * rows).astype(jnp.int32).reshape(1)
    ends = jnp.cumsum(lengths)

    def doc_at(pos):
        return jnp.where(pos < 0, -1, jnp.sum((pos >= ends).astype(jnp.int32)))

    through_own = (doc_at(shard_start[0] - 1) == doc_at(shard_start[0] + rows - 1)).astype(F32)

    head_devices = lax.axis_size("head")
    group_size = HEADS // KV_HEADS
    per_device = HEADS // head_devices
    kv_local = max(1, per_device // group_size)
    kv_table = (
        np.arange(head_devices)[:, None] * per_device // group_size + np.arange(kv_local)[None, :]
    ).reshape(-1)
    short_rows = soft_key.shape[0]

    def spread(field):
        if np.array_equal(kv_table, np.arange(KV_HEADS)):
            return field.reshape(short_rows, head_devices, kv_local * HD)
        taken = jnp.take(field.reshape(short_rows, KV_HEADS, HD), kv_table, axis=1)
        return taken.reshape(short_rows, head_devices, kv_local * HD)

    kv_packed = jnp.concatenate([spread(soft_key), spread(soft_value)], axis=2)
    kv_packed = kv_packed.reshape(short_rows, head_devices * 2 * kv_local * HD)
    own_kv = lax.all_to_all(kv_packed, "head", split_axis=1, concat_axis=0, tiled=True)
    mixed = lax.all_to_all(soft_query, "head", split_axis=1, concat_axis=0, tiled=True)
    kv_width = own_kv.shape[1]

    n_ctx = lax.axis_size("ctx")
    even_to_odd = [(c, c + 1) for c in range(0, n_ctx - 1, 2)]
    odd_to_next = [(c, c + 1) for c in range(1, n_ctx - 1, 2)]
    even_to_even = [(c, c + 2) for c in range(0, n_ctx - 2, 2)]
    is_odd = lax.rem(lax.axis_index("ctx"), 2) == 1

    def send(value, pairs):
        if not pairs:
            return jnp.zeros_like(value)
        return lax.ppermute(value, "ctx", pairs)

    kv_a = send(own_kv, even_to_odd)
    kv_b = send(jnp.concatenate([own_kv, kv_a], axis=1), odd_to_next)
    kv_c1 = send(kv_b[:, :kv_width], even_to_even)
    kv_c2 = send(kv_b, even_to_odd)
    odd_src = [(own_kv, 0), (kv_a, 0), (kv_c2, 0), (kv_c2, 2 * kv_local)]
    even_src = [(own_kv, 0), (kv_b, 0), (kv_b, 2 * kv_local), (kv_c1, 0)]

    lhpb = min(local_heads, group_size)
    lsteps = local_heads // lhpb
    lwide = lhpb * HD
    tail = pl.pallas_call(
        lambda *refs: tail_kernel(lhpb, ndocs, *refs),
        out_shape=jax.ShapeDtypeStruct((local_heads, HD, HD), F32),
        grid=(lsteps,),
        in_specs=[smem_spec(), smem_spec(), col_spec(rows, lwide), col_spec(rows, lwide)],
        out_specs=pl.BlockSpec((lhpb, HD, HD), lambda h: (h, 0, 0)),
        compiler_params=params(),
        cost_estimate=pl.CostEstimate(
            flops=2 * rows * HD * HD * local_heads,
            transcendentals=0,
            bytes_accessed=2 * rows * width * 2 + local_heads * HD * HD * 4,
        ),
    )(lengths, shard_start, lin_key, lin_value)

    lin_local = pl.pallas_call(
        lambda *refs: lin_local_kernel(lhpb, ndocs, *refs),
        out_shape=jax.ShapeDtypeStruct((rows, width), F32),
        grid=(lsteps,),
        in_specs=[
            smem_spec(),
            smem_spec(),
            col_spec(rows, lwide),
            col_spec(rows, lwide),
            col_spec(rows, lwide),
        ],
        out_specs=col_spec(rows, lwide),
        compiler_params=params(),
        cost_estimate=pl.CostEstimate(
            flops=6 * rows * rows * HD * local_heads,
            transcendentals=0,
            bytes_accessed=3 * rows * width * 2 + rows * width * 4,
        ),
    )(lengths, shard_start, lin_query, lin_key, lin_value)

    def through(shard):
        first = shard * rows
        return (doc_at(first - 1) == doc_at(first + rows - 1)).astype(F32)

    here = lax.axis_index("ctx")
    state_a = send(tail, even_to_odd)
    state_v = tail + through_own * state_a
    state_b = send(state_v, odd_to_next)
    lin_local, mixed, state_b = lax.optimization_barrier((lin_local, mixed, state_b))
    state_c1 = send(through(here) * through(here + 1) * state_b, even_to_even)
    state_c2 = send(state_b, even_to_odd)

    blocks = SPAN + 1
    shpb = min(per_device, group_size)
    ssteps = per_device // shpb
    kv_index = lambda i: (i * shpb * kv_local) // per_device
    def kv_spec(offset, value):
        base = offset + (kv_local if value else 0)
        return pl.BlockSpec((rows, HD), lambda i: (0, base + kv_index(i)))

    kv_arrays, kv_specs = [], []
    for value in (False, True):
        for m in range(blocks):
            for source in ((odd_src[m],) if m == 0 else (odd_src[m], even_src[m])):
                kv_arrays.append(source[0])
                kv_specs.append(kv_spec(source[1], value))

    attended = pl.pallas_call(
        lambda *refs: soft_kernel(blocks, shpb, ndocs, *refs),
        out_shape=jax.ShapeDtypeStruct((rows, per_device * HD), BF16),
        grid=(ssteps,),
        in_specs=[smem_spec(), smem_spec(), col_spec(rows, shpb * HD)] + kv_specs,
        out_specs=col_spec(rows, shpb * HD),
        scratch_shapes=[
            pltpu.VMEM((blocks, shpb, rows, rows), F32),
            pltpu.VMEM((shpb, rows, 1), F32),
            pltpu.VMEM((shpb, rows, 1), F32),
            pltpu.VMEM((shpb, rows, HD), F32),
        ],
        compiler_params=pltpu.CompilerParams(
            dimension_semantics=("arbitrary",), vmem_limit_bytes=48 * 1024 * 1024
        ),
        cost_estimate=pl.CostEstimate(
            flops=4 * rows * rows * blocks * HD * per_device,
            transcendentals=rows * rows * blocks * per_device,
            bytes_accessed=rows * per_device * HD * 4 + 2 * blocks * rows * HD * 2 * per_device,
        ),
    )(lengths, shard_start, mixed, *kv_arrays)

    lightning_out = pl.pallas_call(
        lambda *refs: lin_finish_kernel(lhpb, ndocs, *refs),
        out_shape=jax.ShapeDtypeStruct((rows, width), BF16),
        grid=(lsteps,),
        in_specs=[
            smem_spec(),
            smem_spec(),
            col_spec(rows, lwide),
            pl.BlockSpec((lhpb, HD, HD), lambda h: (h, 0, 0)),
            pl.BlockSpec((lhpb, HD, HD), lambda h: (h, 0, 0)),
            pl.BlockSpec((lhpb, HD, HD), lambda h: (h, 0, 0)),
            pl.BlockSpec((lhpb, HD, HD), lambda h: (h, 0, 0)),
            col_spec(rows, lwide),
            pl.BlockSpec((1, lwide), lambda h: (0, h)),
        ],
        out_specs=col_spec(rows, lwide),
        compiler_params=params(),
        cost_estimate=pl.CostEstimate(
            flops=4 * rows * HD * HD * local_heads,
            transcendentals=rows * local_heads,
            bytes_accessed=rows * width * (2 + 4 + 2) + local_heads * HD * HD * 4,
        ),
    )(
        lengths,
        shard_start,
        lin_query,
        state_a,
        state_c2,
        state_b,
        state_c1,
        lin_local,
        norm_gain.reshape(1, width),
    )
    return (lightning_out, attended)


def solution(mesh):
    placed = (
        P("ctx", "head"),
        P("ctx", "head"),
        P("ctx", "head"),
        P("head"),
        P(("ctx", "head"), None),
        P(("ctx", "head"), None),
        P(("ctx", "head"), None),
        P(),
    )
    return jax.shard_map(
        body,
        mesh=mesh,
        in_specs=placed,
        out_specs=(P("ctx", "head"), P("ctx", "head")),
        check_vma=False,
    )
```

```python
import math

import jax
import jax.numpy as jnp
import numpy as np
from jax import lax
from jax.experimental import pallas as pl
from jax.experimental.pallas import tpu as pltpu
from jax.sharding import PartitionSpec as P

HEADS = 64
HD = 128
KV_HEADS = 8
SPAN = 3

F32 = jnp.float32
BF16 = jnp.bfloat16


def document_index(doc_lengths, positions):
    doc_ends = jnp.cumsum(doc_lengths)
    counted = jnp.sum((positions[:, None] >= doc_ends[None, :]).astype(jnp.int32), axis=1)
    return jnp.where(positions < 0, -1, counted).astype(jnp.int32)


def from_behind(value, axis, steps):
    count = lax.axis_size(axis)
    pairs = [(source, source + steps) for source in range(0, count - steps)]
    if not pairs:
        return jnp.zeros_like(value)
    return lax.ppermute(value, axis, pairs)


def split_bf16(x):
    hi = x.astype(BF16)
    lo = (x - hi.astype(F32)).astype(BF16)
    return hi, lo


def dot_nt(a, b):
    return lax.dot_general(a, b, (((1,), (1,)), ((), ())), preferred_element_type=F32)


def head_cols(j):
    return slice(j * HD, (j + 1) * HD)


def doc_ends(len_ref, ndocs):
    ends = []
    total = jnp.int32(0)
    for i in range(ndocs):
        total = total + len_ref[i]
        ends.append(total)
    return ends


def doc_of(ends, pos):
    counted = jnp.zeros_like(pos)
    for e in ends:
        counted = counted + (pos >= e).astype(jnp.int32)
    return jnp.where(pos < 0, -1, counted)


def tail_kernel(hpb, ndocs, len_ref, start_ref, k_ref, v_ref, t_ref):
    rows = k_ref.shape[0]
    ends = doc_ends(len_ref, ndocs)
    start = start_ref[0]
    pos = start + lax.broadcasted_iota(jnp.int32, (rows, 1), 0)
    last = doc_of(ends, start + rows - 1)
    mask = (doc_of(ends, pos) == last).astype(BF16)
    for j in range(hpb):
        masked = v_ref[:, head_cols(j)] * mask
        t_ref[j] = lax.dot_general(
            k_ref[:, head_cols(j)], masked, (((0,), (0,)), ((), ())), preferred_element_type=F32
        )


def lin_local_kernel(hpb, ndocs, len_ref, start_ref, q_ref, k_ref, v_ref, lin_ref):
    rows = q_ref.shape[0]
    ends = doc_ends(len_ref, ndocs)
    start = start_ref[0]
    qpos = start + lax.broadcasted_iota(jnp.int32, (rows, 1), 0)
    kpos = start + lax.broadcasted_iota(jnp.int32, (1, rows), 1)
    visible = (doc_of(ends, qpos) == doc_of(ends, kpos)) & (kpos <= qpos)
    for j in range(hpb):
        scores = dot_nt(q_ref[:, head_cols(j)], k_ref[:, head_cols(j)])
        scores = jnp.where(visible, scores, 0.0)
        hi, lo = split_bf16(scores)
        v = v_ref[:, head_cols(j)]
        lin_ref[:, head_cols(j)] = jnp.dot(hi, v, preferred_element_type=F32) + jnp.dot(
            lo, v, preferred_element_type=F32
        )


def lin_finish_kernel(
    hpb, ndocs, len_ref, start_ref, q_ref, a_ref, c2_ref, b_ref, c1_ref, lin_ref, g_ref, o_ref
):
    rows = q_ref.shape[0]
    ends = doc_ends(len_ref, ndocs)
    start = start_ref[0]
    pos = start + lax.broadcasted_iota(jnp.int32, (rows, 1), 0)
    sees = (doc_of(ends, pos) == doc_of(ends, start - 1)).astype(F32)
    odd = lax.rem(start // rows, 2) == 1
    through_prev = (doc_of(ends, start - rows - 1) == doc_of(ends, start - 1)).astype(F32)
    for j in range(hpb):
        state = jnp.where(odd, a_ref[j] + through_prev * c2_ref[j], b_ref[j] + c1_ref[j])
        hi, lo = split_bf16(state)
        q = q_ref[:, head_cols(j)]
        carried = jnp.dot(q, hi, preferred_element_type=F32) + jnp.dot(
            q, lo, preferred_element_type=F32
        )
        lin = lin_ref[:, head_cols(j)] + carried * sees
        mean_sq = jnp.mean(lin * lin, axis=-1, keepdims=True)
        normed = lin * lax.rsqrt(mean_sq + 1e-06) * g_ref[:, head_cols(j)]
        o_ref[:, head_cols(j)] = normed.astype(o_ref.dtype)


def col_spec(rows, width=HD):
    return pl.BlockSpec((rows, width), lambda h: (0, h))


def full_spec(shape):
    return pl.BlockSpec(shape, lambda h: (0,) * len(shape))


def params():
    return pltpu.CompilerParams(dimension_semantics=("arbitrary",))


def soft_kernel(blocks, hpb, ndocs, len_ref, start_ref, q_ref, *rest):
    per_kind = 2 * blocks - 1
    o_ref = rest[2 * per_kind]
    s_ref, mx_ref, tot_ref, acc_ref = rest[2 * per_kind + 1 :]
    rows = q_ref.shape[0]
    odd = lax.rem(start_ref[0] // rows, 2) == 1

    def pick(refs):
        picked = [lambda: refs[0][...]]
        for m in range(1, blocks):
            picked.append(
                lambda m=m: jnp.where(odd, refs[2 * m - 1][...], refs[2 * m][...])
            )
        return picked

    key_refs = pick(rest[0:per_kind])
    value_refs = pick(rest[per_kind : 2 * per_kind])
    scale = 1.0 / math.sqrt(HD)
    ends = doc_ends(len_ref, ndocs)
    start = start_ref[0]
    qpos = start + lax.broadcasted_iota(jnp.int32, (rows, 1), 0)
    kpos = start + lax.broadcasted_iota(jnp.int32, (1, rows), 1)
    dq = doc_of(ends, qpos)
    first_doc = doc_of(ends, start)
    q = jnp.concatenate([q_ref[:, head_cols(j)] for j in range(hpb)], axis=0)

    def block_scores(m):
        shifted = kpos - m * rows
        visible = dq == doc_of(ends, shifted)
        if m == 0:
            visible = visible & (shifted <= qpos)
        s = dot_nt(q, key_refs[m]()).reshape(hpb, rows, rows) * scale
        return jnp.where(visible[None], s, -1e30)

    def needed(m):
        return doc_of(ends, start - (m - 1) * rows - 1) == first_doc

    s0 = block_scores(0)
    s_ref[0] = s0
    mx_ref[...] = jnp.max(s0, axis=-1, keepdims=True)
    for m in range(1, blocks):

        @pl.when(needed(m))
        def _():
            s = block_scores(m)
            s_ref[m] = s
            mx_ref[...] = jnp.maximum(mx_ref[...], jnp.max(s, axis=-1, keepdims=True))

    def weighted(m):
        w = jnp.exp(s_ref[m] - mx_ref[...])
        part = jnp.sum(w, axis=-1, keepdims=True)
        term = jnp.dot(
            w.reshape(hpb * rows, rows).astype(BF16),
            value_refs[m](),
            preferred_element_type=F32,
        ).reshape(hpb, rows, HD)
        return part, term

    part, term = weighted(0)
    tot_ref[...] = part
    acc_ref[...] = term
    for m in range(1, blocks):

        @pl.when(needed(m))
        def _():
            part, term = weighted(m)
            tot_ref[...] += part
            acc_ref[...] += term

    out = acc_ref[...] / tot_ref[...]
    for j in range(hpb):
        o_ref[:, head_cols(j)] = out[j].astype(o_ref.dtype)


def smem_spec():
    return pl.BlockSpec(memory_space=pltpu.SMEM)


def body(lin_query, lin_key, lin_value, norm_gain, soft_query, soft_key, soft_value, doc_lengths):
    rows, width = lin_query.shape
    local_heads = width // HD
    ndocs = doc_lengths.shape[0]
    lengths = doc_lengths.astype(jnp.int32)
    shard_start = (lax.axis_index("ctx") * rows).astype(jnp.int32).reshape(1)
    ends = jnp.cumsum(lengths)

    def doc_at(pos):
        return jnp.where(pos < 0, -1, jnp.sum((pos >= ends).astype(jnp.int32)))

    through_own = (doc_at(shard_start[0] - 1) == doc_at(shard_start[0] + rows - 1)).astype(F32)

    head_devices = lax.axis_size("head")
    group_size = HEADS // KV_HEADS
    per_device = HEADS // head_devices
    kv_local = max(1, per_device // group_size)
    kv_table = (
        np.arange(head_devices)[:, None] * per_device // group_size + np.arange(kv_local)[None, :]
    ).reshape(-1)
    short_rows = soft_key.shape[0]

    def spread(field):
        if np.array_equal(kv_table, np.arange(KV_HEADS)):
            return field.reshape(short_rows, head_devices, kv_local * HD)
        taken = jnp.take(field.reshape(short_rows, KV_HEADS, HD), kv_table, axis=1)
        return taken.reshape(short_rows, head_devices, kv_local * HD)

    kv_packed = jnp.concatenate([spread(soft_key), spread(soft_value)], axis=2)
    kv_packed = kv_packed.reshape(short_rows, head_devices * 2 * kv_local * HD)
    own_kv = lax.all_to_all(kv_packed, "head", split_axis=1, concat_axis=0, tiled=True)
    mixed = lax.all_to_all(soft_query, "head", split_axis=1, concat_axis=0, tiled=True)
    kv_width = own_kv.shape[1]

    n_ctx = lax.axis_size("ctx")
    even_to_odd = [(c, c + 1) for c in range(0, n_ctx - 1, 2)]
    odd_to_next = [(c, c + 1) for c in range(1, n_ctx - 1, 2)]
    even_to_even = [(c, c + 2) for c in range(0, n_ctx - 2, 2)]
    is_odd = lax.rem(lax.axis_index("ctx"), 2) == 1

    def send(value, pairs):
        if not pairs:
            return jnp.zeros_like(value)
        return lax.ppermute(value, "ctx", pairs)

    kv_a = send(own_kv, even_to_odd)
    kv_b = send(jnp.concatenate([own_kv, kv_a], axis=1), odd_to_next)
    kv_c1 = send(kv_b[:, :kv_width], even_to_even)
    kv_c2 = send(kv_b, even_to_odd)
    odd_src = [(own_kv, 0), (kv_a, 0), (kv_c2, 0), (kv_c2, 2 * kv_local)]
    even_src = [(own_kv, 0), (kv_b, 0), (kv_b, 2 * kv_local), (kv_c1, 0)]

    lhpb = min(local_heads, group_size)
    lsteps = local_heads // lhpb
    lwide = lhpb * HD
    tail = pl.pallas_call(
        lambda *refs: tail_kernel(lhpb, ndocs, *refs),
        out_shape=jax.ShapeDtypeStruct((local_heads, HD, HD), F32),
        grid=(lsteps,),
        in_specs=[smem_spec(), smem_spec(), col_spec(rows, lwide), col_spec(rows, lwide)],
        out_specs=pl.BlockSpec((lhpb, HD, HD), lambda h: (h, 0, 0)),
        compiler_params=params(),
        cost_estimate=pl.CostEstimate(
            flops=2 * rows * HD * HD * local_heads,
            transcendentals=0,
            bytes_accessed=2 * rows * width * 2 + local_heads * HD * HD * 4,
        ),
    )(lengths, shard_start, lin_key, lin_value)

    lin_local = pl.pallas_call(
        lambda *refs: lin_local_kernel(lhpb, ndocs, *refs),
        out_shape=jax.ShapeDtypeStruct((rows, width), F32),
        grid=(lsteps,),
        in_specs=[
            smem_spec(),
            smem_spec(),
            col_spec(rows, lwide),
            col_spec(rows, lwide),
            col_spec(rows, lwide),
        ],
        out_specs=col_spec(rows, lwide),
        compiler_params=params(),
        cost_estimate=pl.CostEstimate(
            flops=6 * rows * rows * HD * local_heads,
            transcendentals=0,
            bytes_accessed=3 * rows * width * 2 + rows * width * 4,
        ),
    )(lengths, shard_start, lin_query, lin_key, lin_value)

    def through(shard):
        first = shard * rows
        return (doc_at(first - 1) == doc_at(first + rows - 1)).astype(F32)

    here = lax.axis_index("ctx")
    state_a = send(tail, even_to_odd)
    state_v = tail + through_own * state_a
    lin_local, state_v = lax.optimization_barrier((lin_local, state_v))
    state_b = send(state_v, odd_to_next)
    state_c1 = send(through(here) * through(here + 1) * state_b, even_to_even)
    state_c2 = send(state_b, even_to_odd)

    lightning_out = pl.pallas_call(
        lambda *refs: lin_finish_kernel(lhpb, ndocs, *refs),
        out_shape=jax.ShapeDtypeStruct((rows, width), BF16),
        grid=(lsteps,),
        in_specs=[
            smem_spec(),
            smem_spec(),
            col_spec(rows, lwide),
            pl.BlockSpec((lhpb, HD, HD), lambda h: (h, 0, 0)),
            pl.BlockSpec((lhpb, HD, HD), lambda h: (h, 0, 0)),
            pl.BlockSpec((lhpb, HD, HD), lambda h: (h, 0, 0)),
            pl.BlockSpec((lhpb, HD, HD), lambda h: (h, 0, 0)),
            col_spec(rows, lwide),
            pl.BlockSpec((1, lwide), lambda h: (0, h)),
        ],
        out_specs=col_spec(rows, lwide),
        compiler_params=params(),
        cost_estimate=pl.CostEstimate(
            flops=4 * rows * HD * HD * local_heads,
            transcendentals=rows * local_heads,
            bytes_accessed=rows * width * (2 + 4 + 2) + local_heads * HD * HD * 4,
        ),
    )(
        lengths,
        shard_start,
        lin_query,
        state_a,
        state_c2,
        state_b,
        state_c1,
        lin_local,
        norm_gain.reshape(1, width),
    )
    lightning_out, kv_c1, kv_c2 = lax.optimization_barrier((lightning_out, kv_c1, kv_c2))
    odd_src = [(own_kv, 0), (kv_a, 0), (kv_c2, 0), (kv_c2, 2 * kv_local)]
    even_src = [(own_kv, 0), (kv_b, 0), (kv_b, 2 * kv_local), (kv_c1, 0)]

    blocks = SPAN + 1
    shpb = min(per_device, group_size)
    ssteps = per_device // shpb
    kv_index = lambda i: (i * shpb * kv_local) // per_device
    def kv_spec(offset, value):
        base = offset + (kv_local if value else 0)
        return pl.BlockSpec((rows, HD), lambda i: (0, base + kv_index(i)))

    kv_arrays, kv_specs = [], []
    for value in (False, True):
        for m in range(blocks):
            for source in ((odd_src[m],) if m == 0 else (odd_src[m], even_src[m])):
                kv_arrays.append(source[0])
                kv_specs.append(kv_spec(source[1], value))

    attended = pl.pallas_call(
        lambda *refs: soft_kernel(blocks, shpb, ndocs, *refs),
        out_shape=jax.ShapeDtypeStruct((rows, per_device * HD), BF16),
        grid=(ssteps,),
        in_specs=[smem_spec(), smem_spec(), col_spec(rows, shpb * HD)] + kv_specs,
        out_specs=col_spec(rows, shpb * HD),
        scratch_shapes=[
            pltpu.VMEM((blocks, shpb, rows, rows), F32),
            pltpu.VMEM((shpb, rows, 1), F32),
            pltpu.VMEM((shpb, rows, 1), F32),
            pltpu.VMEM((shpb, rows, HD), F32),
        ],
        compiler_params=pltpu.CompilerParams(
            dimension_semantics=("arbitrary",), vmem_limit_bytes=48 * 1024 * 1024
        ),
        cost_estimate=pl.CostEstimate(
            flops=4 * rows * rows * blocks * HD * per_device,
            transcendentals=rows * rows * blocks * per_device,
            bytes_accessed=rows * per_device * HD * 4 + 2 * blocks * rows * HD * 2 * per_device,
        ),
    )(lengths, shard_start, mixed, *kv_arrays)

    return (lightning_out, attended)


def solution(mesh):
    placed = (
        P("ctx", "head"),
        P("ctx", "head"),
        P("ctx", "head"),
        P("head"),
        P(("ctx", "head"), None),
        P(("ctx", "head"), None),
        P(("ctx", "head"), None),
        P(),
    )
    return jax.shard_map(
        body,
        mesh=mesh,
        in_specs=placed,
        out_specs=(P("ctx", "head"), P("ctx", "head")),
        check_vma=False,
    )
```

```python
import math

import jax
import jax.numpy as jnp
import numpy as np
from jax import lax
from jax.experimental import pallas as pl
from jax.experimental.pallas import tpu as pltpu
from jax.sharding import PartitionSpec as P

HEADS = 64
HD = 128
KV_HEADS = 8
SPAN = 3

F32 = jnp.float32
BF16 = jnp.bfloat16


def document_index(doc_lengths, positions):
    doc_ends = jnp.cumsum(doc_lengths)
    counted = jnp.sum((positions[:, None] >= doc_ends[None, :]).astype(jnp.int32), axis=1)
    return jnp.where(positions < 0, -1, counted).astype(jnp.int32)


def from_behind(value, axis, steps):
    count = lax.axis_size(axis)
    pairs = [(source, source + steps) for source in range(0, count - steps)]
    if not pairs:
        return jnp.zeros_like(value)
    return lax.ppermute(value, axis, pairs)


def split_bf16(x):
    hi = x.astype(BF16)
    lo = (x - hi.astype(F32)).astype(BF16)
    return hi, lo


def split_kept(x):
    rounded = lax.reduce_precision(x, exponent_bits=8, mantissa_bits=7)
    return rounded.astype(BF16), (x - rounded).astype(BF16)


def dot_nt(a, b):
    return lax.dot_general(a, b, (((1,), (1,)), ((), ())), preferred_element_type=F32)


def head_cols(j):
    return slice(j * HD, (j + 1) * HD)


def doc_ends(len_ref, ndocs):
    ends = []
    total = jnp.int32(0)
    for i in range(ndocs):
        total = total + len_ref[i]
        ends.append(total)
    return ends


def doc_of(ends, pos):
    counted = jnp.zeros_like(pos)
    for e in ends:
        counted = counted + (pos >= e).astype(jnp.int32)
    return jnp.where(pos < 0, -1, counted)


def tail_kernel(hpb, ndocs, len_ref, start_ref, k_ref, v_ref, t_ref):
    rows = k_ref.shape[0]
    ends = doc_ends(len_ref, ndocs)
    start = start_ref[0]
    pos = start + lax.broadcasted_iota(jnp.int32, (rows, 1), 0)
    last = doc_of(ends, start + rows - 1)
    mask = (doc_of(ends, pos) == last).astype(BF16)
    for j in range(hpb):
        masked = v_ref[:, head_cols(j)] * mask
        t_ref[j] = lax.dot_general(
            k_ref[:, head_cols(j)], masked, (((0,), (0,)), ((), ())), preferred_element_type=F32
        )


def lin_local_kernel(hpb, ndocs, len_ref, start_ref, q_ref, k_ref, v_ref, lin_ref):
    rows = q_ref.shape[0]
    ends = doc_ends(len_ref, ndocs)
    start = start_ref[0]
    qpos = start + lax.broadcasted_iota(jnp.int32, (rows, 1), 0)
    kpos = start + lax.broadcasted_iota(jnp.int32, (1, rows), 1)
    visible = (doc_of(ends, qpos) == doc_of(ends, kpos)) & (kpos <= qpos)
    for j in range(hpb):
        scores = dot_nt(q_ref[:, head_cols(j)], k_ref[:, head_cols(j)])
        scores = jnp.where(visible, scores, 0.0)
        hi, lo = split_bf16(scores)
        v = v_ref[:, head_cols(j)]
        lin_ref[:, head_cols(j)] = jnp.dot(hi, v, preferred_element_type=F32) + jnp.dot(
            lo, v, preferred_element_type=F32
        )


def lin_finish_kernel(
    hpb, ndocs, len_ref, start_ref, q_ref, a_ref, *rest
):
    bh_ref, bl_ref, c1h_ref, c1l_ref, c2h_ref, c2l_ref, lin_ref, g_ref, o_ref = rest
    rows = q_ref.shape[0]
    ends = doc_ends(len_ref, ndocs)
    start = start_ref[0]
    pos = start + lax.broadcasted_iota(jnp.int32, (rows, 1), 0)
    sees = (doc_of(ends, pos) == doc_of(ends, start - 1)).astype(F32)
    odd = lax.rem(start // rows, 2) == 1
    through_prev = (doc_of(ends, start - rows - 1) == doc_of(ends, start - 1)).astype(F32)
    through_prev2 = (
        doc_of(ends, start - 2 * rows - 1) == doc_of(ends, start - rows - 1)
    ).astype(F32)
    for j in range(hpb):
        wide = lambda h_ref, l_ref: h_ref[j].astype(F32) + l_ref[j].astype(F32)
        on_odd = a_ref[j] + through_prev * wide(c2h_ref, c2l_ref)
        on_even = wide(bh_ref, bl_ref) + through_prev * through_prev2 * wide(c1h_ref, c1l_ref)
        state = jnp.where(odd, on_odd, on_even)
        hi, lo = split_bf16(state)
        q = q_ref[:, head_cols(j)]
        carried = jnp.dot(q, hi, preferred_element_type=F32) + jnp.dot(
            q, lo, preferred_element_type=F32
        )
        lin = lin_ref[:, head_cols(j)] + carried * sees
        mean_sq = jnp.mean(lin * lin, axis=-1, keepdims=True)
        normed = lin * lax.rsqrt(mean_sq + 1e-06) * g_ref[:, head_cols(j)]
        o_ref[:, head_cols(j)] = normed.astype(o_ref.dtype)


def col_spec(rows, width=HD):
    return pl.BlockSpec((rows, width), lambda h: (0, h))


def full_spec(shape):
    return pl.BlockSpec(shape, lambda h: (0,) * len(shape))


def params():
    return pltpu.CompilerParams(dimension_semantics=("arbitrary",))


def soft_kernel(blocks, hpb, ndocs, len_ref, start_ref, q_ref, *rest):
    per_kind = 2 * blocks - 1
    o_ref = rest[2 * per_kind]
    s_ref, mx_ref, tot_ref, acc_ref = rest[2 * per_kind + 1 :]
    rows = q_ref.shape[0]
    odd = lax.rem(start_ref[0] // rows, 2) == 1

    def pick(refs):
        picked = [lambda: refs[0][...]]
        for m in range(1, blocks):
            picked.append(
                lambda m=m: jnp.where(odd, refs[2 * m - 1][...], refs[2 * m][...]).reshape(rows, HD)
            )
        return picked

    key_refs = pick(rest[0:per_kind])
    value_refs = pick(rest[per_kind : 2 * per_kind])
    scale = 1.0 / math.sqrt(HD)
    ends = doc_ends(len_ref, ndocs)
    start = start_ref[0]
    qpos = start + lax.broadcasted_iota(jnp.int32, (rows, 1), 0)
    kpos = start + lax.broadcasted_iota(jnp.int32, (1, rows), 1)
    dq = doc_of(ends, qpos)
    first_doc = doc_of(ends, start)
    q = jnp.concatenate([q_ref[:, head_cols(j)] for j in range(hpb)], axis=0)

    def block_scores(m):
        shifted = kpos - m * rows
        visible = dq == doc_of(ends, shifted)
        if m == 0:
            visible = visible & (shifted <= qpos)
        s = dot_nt(q, key_refs[m]()).reshape(hpb, rows, rows) * scale
        return jnp.where(visible[None], s, -1e30)

    def needed(m):
        return doc_of(ends, start - (m - 1) * rows - 1) == first_doc

    s0 = block_scores(0)
    s_ref[0] = s0
    mx_ref[...] = jnp.max(s0, axis=-1, keepdims=True)
    for m in range(1, blocks):

        @pl.when(needed(m))
        def _():
            s = block_scores(m)
            s_ref[m] = s
            mx_ref[...] = jnp.maximum(mx_ref[...], jnp.max(s, axis=-1, keepdims=True))

    def weighted(m):
        w = jnp.exp(s_ref[m] - mx_ref[...])
        part = jnp.sum(w, axis=-1, keepdims=True)
        term = jnp.dot(
            w.reshape(hpb * rows, rows).astype(BF16),
            value_refs[m](),
            preferred_element_type=F32,
        ).reshape(hpb, rows, HD)
        return part, term

    part, term = weighted(0)
    tot_ref[...] = part
    acc_ref[...] = term
    for m in range(1, blocks):

        @pl.when(needed(m))
        def _():
            part, term = weighted(m)
            tot_ref[...] += part
            acc_ref[...] += term

    out = acc_ref[...] / tot_ref[...]
    for j in range(hpb):
        o_ref[:, head_cols(j)] = out[j].astype(o_ref.dtype)


def smem_spec():
    return pl.BlockSpec(memory_space=pltpu.SMEM)


def body(lin_query, lin_key, lin_value, norm_gain, soft_query, soft_key, soft_value, doc_lengths):
    rows, width = lin_query.shape
    local_heads = width // HD
    ndocs = doc_lengths.shape[0]
    lengths = doc_lengths.astype(jnp.int32)
    shard_start = (lax.axis_index("ctx") * rows).astype(jnp.int32).reshape(1)
    ends = jnp.cumsum(lengths)

    def doc_at(pos):
        return jnp.where(pos < 0, -1, jnp.sum((pos >= ends).astype(jnp.int32)))

    through_own = (doc_at(shard_start[0] - 1) == doc_at(shard_start[0] + rows - 1)).astype(F32)

    head_devices = lax.axis_size("head")
    group_size = HEADS // KV_HEADS
    per_device = HEADS // head_devices
    kv_local = max(1, per_device // group_size)
    kv_table = (
        np.arange(head_devices)[:, None] * per_device // group_size + np.arange(kv_local)[None, :]
    ).reshape(-1)
    short_rows = soft_key.shape[0]

    def spread(field):
        if np.array_equal(kv_table, np.arange(KV_HEADS)):
            return field.reshape(short_rows, head_devices, kv_local * HD)
        taken = jnp.take(field.reshape(short_rows, KV_HEADS, HD), kv_table, axis=1)
        return taken.reshape(short_rows, head_devices, kv_local * HD)

    packed = jnp.concatenate(
        [
            soft_query.reshape(short_rows, head_devices, per_device * HD),
            spread(soft_key),
            spread(soft_value),
        ],
        axis=2,
    )
    packed = packed.reshape(short_rows, head_devices * packed.shape[2])
    mixed = lax.all_to_all(packed, "head", split_axis=1, concat_axis=0, tiled=True)
    own_kv = mixed[:, per_device * HD :]
    kv_width = own_kv.shape[1]
    kv_planes = own_kv.reshape(rows, kv_width // HD, HD).transpose(1, 0, 2)
    kv_planes = kv_planes.reshape(kv_width * rows // (HD * HD), HD, HD)

    n_ctx = lax.axis_size("ctx")
    even_to_odd = [(c, c + 1) for c in range(0, n_ctx - 1, 2)]
    odd_to_next = [(c, c + 1) for c in range(1, n_ctx - 1, 2)]
    even_to_even = [(c, c + 2) for c in range(0, n_ctx - 2, 2)]
    is_odd = lax.rem(lax.axis_index("ctx"), 2) == 1

    def send(value, pairs):
        if not pairs:
            return jnp.zeros_like(value)
        return lax.ppermute(value, "ctx", pairs)

    kv_a = send(kv_planes, even_to_odd)

    lhpb = min(local_heads, group_size)
    lsteps = local_heads // lhpb
    lwide = lhpb * HD
    tail = pl.pallas_call(
        lambda *refs: tail_kernel(lhpb, ndocs, *refs),
        out_shape=jax.ShapeDtypeStruct((local_heads, HD, HD), F32),
        grid=(lsteps,),
        in_specs=[smem_spec(), smem_spec(), col_spec(rows, lwide), col_spec(rows, lwide)],
        out_specs=pl.BlockSpec((lhpb, HD, HD), lambda h: (h, 0, 0)),
        compiler_params=params(),
        cost_estimate=pl.CostEstimate(
            flops=2 * rows * HD * HD * local_heads,
            transcendentals=0,
            bytes_accessed=2 * rows * width * 2 + local_heads * HD * HD * 4,
        ),
    )(lengths, shard_start, lin_key, lin_value)

    lin_local = pl.pallas_call(
        lambda *refs: lin_local_kernel(lhpb, ndocs, *refs),
        out_shape=jax.ShapeDtypeStruct((rows, width), F32),
        grid=(lsteps,),
        in_specs=[
            smem_spec(),
            smem_spec(),
            col_spec(rows, lwide),
            col_spec(rows, lwide),
            col_spec(rows, lwide),
        ],
        out_specs=col_spec(rows, lwide),
        compiler_params=params(),
        cost_estimate=pl.CostEstimate(
            flops=6 * rows * rows * HD * local_heads,
            transcendentals=0,
            bytes_accessed=3 * rows * width * 2 + rows * width * 4,
        ),
    )(lengths, shard_start, lin_query, lin_key, lin_value)

    def through(shard):
        first = shard * rows
        return (doc_at(first - 1) == doc_at(first + rows - 1)).astype(F32)

    state_a = send(tail, even_to_odd)
    v_hi, v_lo = split_kept(tail + through_own * state_a)
    recv_b = send(jnp.concatenate([v_hi, v_lo, kv_planes, kv_a], axis=0), odd_to_next)
    lin_local, recv_b = lax.optimization_barrier((lin_local, recv_b))
    one_shard = 2 * local_heads + kv_planes.shape[0]
    recv_c1 = send(recv_b[:one_shard], even_to_even)
    recv_c2 = send(recv_b, even_to_odd)
    as_rows = lambda a: a.reshape(a.shape[0] * HD // rows, rows, HD)
    kv_a_rows, b_rows, c1_rows, c2_rows = (as_rows(a) for a in (kv_a, recv_b, recv_c1, recv_c2))
    first_kv = local_heads
    second_kv = local_heads + 2 * kv_local
    odd_src = [(own_kv, 0), (kv_a_rows, 0), (c2_rows, first_kv), (c2_rows, second_kv)]
    even_src = [(own_kv, 0), (b_rows, first_kv), (b_rows, second_kv), (c1_rows, first_kv)]

    blocks = SPAN + 1
    shpb = min(per_device, group_size)
    ssteps = per_device // shpb
    kv_index = lambda i: (i * shpb * kv_local) // per_device
    def kv_spec(array, offset, value):
        base = offset + (kv_local if value else 0)
        if array.ndim == 2:
            return pl.BlockSpec((rows, HD), lambda i: (0, base + kv_index(i)))
        return pl.BlockSpec((1, rows, HD), lambda i: (base + kv_index(i), 0, 0))

    kv_arrays, kv_specs = [], []
    for value in (False, True):
        for m in range(blocks):
            for source in ((odd_src[m],) if m == 0 else (odd_src[m], even_src[m])):
                kv_arrays.append(source[0])
                kv_specs.append(kv_spec(source[0], source[1], value))

    attended = pl.pallas_call(
        lambda *refs: soft_kernel(blocks, shpb, ndocs, *refs),
        out_shape=jax.ShapeDtypeStruct((rows, per_device * HD), BF16),
        grid=(ssteps,),
        in_specs=[smem_spec(), smem_spec(), col_spec(rows, shpb * HD)] + kv_specs,
        out_specs=col_spec(rows, shpb * HD),
        scratch_shapes=[
            pltpu.VMEM((blocks, shpb, rows, rows), F32),
            pltpu.VMEM((shpb, rows, 1), F32),
            pltpu.VMEM((shpb, rows, 1), F32),
            pltpu.VMEM((shpb, rows, HD), F32),
        ],
        compiler_params=pltpu.CompilerParams(
            dimension_semantics=("arbitrary",), vmem_limit_bytes=48 * 1024 * 1024
        ),
        cost_estimate=pl.CostEstimate(
            flops=4 * rows * rows * blocks * HD * per_device,
            transcendentals=rows * rows * blocks * per_device,
            bytes_accessed=rows * per_device * HD * 4 + 2 * blocks * rows * HD * 2 * per_device,
        ),
    )(lengths, shard_start, mixed, *kv_arrays)

    lightning_out = pl.pallas_call(
        lambda *refs: lin_finish_kernel(lhpb, ndocs, *refs),
        out_shape=jax.ShapeDtypeStruct((rows, width), BF16),
        grid=(lsteps,),
        in_specs=[
            smem_spec(),
            smem_spec(),
            col_spec(rows, lwide),
            pl.BlockSpec((lhpb, HD, HD), lambda h: (h, 0, 0)),
        ]
        + [
            pl.BlockSpec((lhpb, HD, HD), lambda h, half=half: (half * lsteps + h, 0, 0))
            for _ in range(3)
            for half in (0, 1)
        ]
        + [
            col_spec(rows, lwide),
            pl.BlockSpec((1, lwide), lambda h: (0, h)),
        ],
        out_specs=col_spec(rows, lwide),
        compiler_params=params(),
        cost_estimate=pl.CostEstimate(
            flops=4 * rows * HD * HD * local_heads,
            transcendentals=rows * local_heads,
            bytes_accessed=rows * width * (2 + 4 + 2) + local_heads * HD * HD * 4,
        ),
    )(
        lengths,
        shard_start,
        lin_query,
        state_a,
        recv_b,
        recv_b,
        recv_c1,
        recv_c1,
        recv_c2,
        recv_c2,
        lin_local,
        norm_gain.reshape(1, width),
    )
    return (lightning_out, attended)


def solution(mesh):
    placed = (
        P("ctx", "head"),
        P("ctx", "head"),
        P("ctx", "head"),
        P("head"),
        P(("ctx", "head"), None),
        P(("ctx", "head"), None),
        P(("ctx", "head"), None),
        P(),
    )
    return jax.shard_map(
        body,
        mesh=mesh,
        in_specs=placed,
        out_specs=(P("ctx", "head"), P("ctx", "head")),
        check_vma=False,
    )
```

```python
import math

import jax
import jax.numpy as jnp
import numpy as np
from jax import lax
from jax.experimental import pallas as pl
from jax.experimental.pallas import tpu as pltpu
from jax.sharding import PartitionSpec as P

HEADS = 64
HD = 128
KV_HEADS = 8
SPAN = 3

F32 = jnp.float32
BF16 = jnp.bfloat16


def document_index(doc_lengths, positions):
    doc_ends = jnp.cumsum(doc_lengths)
    counted = jnp.sum((positions[:, None] >= doc_ends[None, :]).astype(jnp.int32), axis=1)
    return jnp.where(positions < 0, -1, counted).astype(jnp.int32)


def from_behind(value, axis, steps):
    count = lax.axis_size(axis)
    pairs = [(source, source + steps) for source in range(0, count - steps)]
    if not pairs:
        return jnp.zeros_like(value)
    return lax.ppermute(value, axis, pairs)


def split_bf16(x):
    hi = x.astype(BF16)
    lo = (x - hi.astype(F32)).astype(BF16)
    return hi, lo


def dot_nt(a, b):
    return lax.dot_general(a, b, (((1,), (1,)), ((), ())), preferred_element_type=F32)


def head_cols(j):
    return slice(j * HD, (j + 1) * HD)


def doc_ends(len_ref, ndocs):
    ends = []
    total = jnp.int32(0)
    for i in range(ndocs):
        total = total + len_ref[i]
        ends.append(total)
    return ends


def doc_of(ends, pos):
    counted = jnp.zeros_like(pos)
    for e in ends:
        counted = counted + (pos >= e).astype(jnp.int32)
    return jnp.where(pos < 0, -1, counted)


def tail_kernel(hpb, ndocs, len_ref, start_ref, k_ref, v_ref, t_ref):
    rows = k_ref.shape[0]
    ends = doc_ends(len_ref, ndocs)
    start = start_ref[0]
    pos = start + lax.broadcasted_iota(jnp.int32, (rows, 1), 0)
    last = doc_of(ends, start + rows - 1)
    mask = (doc_of(ends, pos) == last).astype(BF16)
    for j in range(hpb):
        masked = v_ref[:, head_cols(j)] * mask
        t_ref[j] = lax.dot_general(
            k_ref[:, head_cols(j)], masked, (((0,), (0,)), ((), ())), preferred_element_type=F32
        )


def lin_local_kernel(hpb, ndocs, len_ref, start_ref, q_ref, k_ref, v_ref, lin_ref):
    rows = q_ref.shape[0]
    ends = doc_ends(len_ref, ndocs)
    start = start_ref[0]
    qpos = start + lax.broadcasted_iota(jnp.int32, (rows, 1), 0)
    kpos = start + lax.broadcasted_iota(jnp.int32, (1, rows), 1)
    visible = (doc_of(ends, qpos) == doc_of(ends, kpos)) & (kpos <= qpos)
    for j in range(hpb):
        scores = dot_nt(q_ref[:, head_cols(j)], k_ref[:, head_cols(j)])
        scores = jnp.where(visible, scores, 0.0)
        hi, lo = split_bf16(scores)
        v = v_ref[:, head_cols(j)]
        lin_ref[:, head_cols(j)] = jnp.dot(hi, v, preferred_element_type=F32) + jnp.dot(
            lo, v, preferred_element_type=F32
        )


def lin_finish_kernel(
    hpb, ndocs, len_ref, start_ref, q_ref, a_ref, c2_ref, b_ref, c1_ref, lin_ref, g_ref, o_ref
):
    rows = q_ref.shape[0]
    ends = doc_ends(len_ref, ndocs)
    start = start_ref[0]
    pos = start + lax.broadcasted_iota(jnp.int32, (rows, 1), 0)
    sees = (doc_of(ends, pos) == doc_of(ends, start - 1)).astype(F32)
    odd = lax.rem(start // rows, 2) == 1
    through_prev = (doc_of(ends, start - rows - 1) == doc_of(ends, start - 1)).astype(F32)
    for j in range(hpb):
        state = jnp.where(odd, a_ref[j] + through_prev * c2_ref[j], b_ref[j] + c1_ref[j])
        hi, lo = split_bf16(state)
        q = q_ref[:, head_cols(j)]
        carried = jnp.dot(q, hi, preferred_element_type=F32) + jnp.dot(
            q, lo, preferred_element_type=F32
        )
        lin = lin_ref[:, head_cols(j)] + carried * sees
        mean_sq = jnp.mean(lin * lin, axis=-1, keepdims=True)
        normed = lin * lax.rsqrt(mean_sq + 1e-06) * g_ref[:, head_cols(j)]
        o_ref[:, head_cols(j)] = normed.astype(o_ref.dtype)


def col_spec(rows, width=HD):
    return pl.BlockSpec((rows, width), lambda h: (0, h))


def full_spec(shape):
    return pl.BlockSpec(shape, lambda h: (0,) * len(shape))


def params():
    return pltpu.CompilerParams(dimension_semantics=("arbitrary",))


def soft_kernel(blocks, hpb, ndocs, len_ref, start_ref, q_ref, *rest):
    per_kind = 2 * blocks - 1
    o_ref = rest[2 * per_kind]
    s_ref, mx_ref, tot_ref, acc_ref = rest[2 * per_kind + 1 :]
    rows = q_ref.shape[0]
    odd = lax.rem(start_ref[0] // rows, 2) == 1

    def pick(refs):
        picked = [lambda: refs[0][...]]
        for m in range(1, blocks):
            picked.append(
                lambda m=m: jnp.where(odd, refs[2 * m - 1][...], refs[2 * m][...])
            )
        return picked

    key_refs = pick(rest[0:per_kind])
    value_refs = pick(rest[per_kind : 2 * per_kind])
    scale = 1.0 / math.sqrt(HD)
    ends = doc_ends(len_ref, ndocs)
    start = start_ref[0]
    qpos = start + lax.broadcasted_iota(jnp.int32, (rows, 1), 0)
    kpos = start + lax.broadcasted_iota(jnp.int32, (1, rows), 1)
    dq = doc_of(ends, qpos)
    first_doc = doc_of(ends, start)
    q = jnp.concatenate([q_ref[:, head_cols(j)] for j in range(hpb)], axis=0)

    def block_scores(m):
        shifted = kpos - m * rows
        visible = dq == doc_of(ends, shifted)
        if m == 0:
            visible = visible & (shifted <= qpos)
        s = dot_nt(q, key_refs[m]()).reshape(hpb, rows, rows) * scale
        return jnp.where(visible[None], s, -1e30)

    def needed(m):
        return doc_of(ends, start - (m - 1) * rows - 1) == first_doc

    s0 = block_scores(0)
    s_ref[0] = s0
    mx_ref[...] = jnp.max(s0, axis=-1, keepdims=True)
    for m in range(1, blocks):

        @pl.when(needed(m))
        def _():
            s = block_scores(m)
            s_ref[m] = s
            mx_ref[...] = jnp.maximum(mx_ref[...], jnp.max(s, axis=-1, keepdims=True))

    def weighted(m):
        w = jnp.exp(s_ref[m] - mx_ref[...])
        part = jnp.sum(w, axis=-1, keepdims=True)
        term = jnp.dot(
            w.reshape(hpb * rows, rows).astype(BF16),
            value_refs[m](),
            preferred_element_type=F32,
        ).reshape(hpb, rows, HD)
        return part, term

    part, term = weighted(0)
    tot_ref[...] = part
    acc_ref[...] = term
    for m in range(1, blocks):

        @pl.when(needed(m))
        def _():
            part, term = weighted(m)
            tot_ref[...] += part
            acc_ref[...] += term

    out = acc_ref[...] / tot_ref[...]
    for j in range(hpb):
        o_ref[:, head_cols(j)] = out[j].astype(o_ref.dtype)


def smem_spec():
    return pl.BlockSpec(memory_space=pltpu.SMEM)


def body(lin_query, lin_key, lin_value, norm_gain, soft_query, soft_key, soft_value, doc_lengths):
    rows, width = lin_query.shape
    local_heads = width // HD
    ndocs = doc_lengths.shape[0]
    lengths = doc_lengths.astype(jnp.int32)
    shard_start = (lax.axis_index("ctx") * rows).astype(jnp.int32).reshape(1)
    ends = jnp.cumsum(lengths)

    def doc_at(pos):
        return jnp.where(pos < 0, -1, jnp.sum((pos >= ends).astype(jnp.int32)))

    through_own = (doc_at(shard_start[0] - 1) == doc_at(shard_start[0] + rows - 1)).astype(F32)

    head_devices = lax.axis_size("head")
    group_size = HEADS // KV_HEADS
    per_device = HEADS // head_devices
    kv_local = max(1, per_device // group_size)
    kv_table = (
        np.arange(head_devices)[:, None] * per_device // group_size + np.arange(kv_local)[None, :]
    ).reshape(-1)
    short_rows = soft_key.shape[0]

    def spread(field):
        if np.array_equal(kv_table, np.arange(KV_HEADS)):
            return field.reshape(short_rows, head_devices, kv_local * HD)
        taken = jnp.take(field.reshape(short_rows, KV_HEADS, HD), kv_table, axis=1)
        return taken.reshape(short_rows, head_devices, kv_local * HD)

    packed = jnp.concatenate(
        [
            soft_query.reshape(short_rows, head_devices, per_device * HD),
            spread(soft_key),
            spread(soft_value),
        ],
        axis=2,
    )
    packed = packed.reshape(short_rows, head_devices * packed.shape[2])
    mixed = lax.all_to_all(packed, "head", split_axis=1, concat_axis=0, tiled=True)
    own_kv = mixed[:, per_device * HD :]
    kv_width = own_kv.shape[1]

    n_ctx = lax.axis_size("ctx")
    even_to_odd = [(c, c + 1) for c in range(0, n_ctx - 1, 2)]
    odd_to_next = [(c, c + 1) for c in range(1, n_ctx - 1, 2)]
    even_to_even = [(c, c + 2) for c in range(0, n_ctx - 2, 2)]
    is_odd = lax.rem(lax.axis_index("ctx"), 2) == 1

    def send(value, pairs):
        if not pairs:
            return jnp.zeros_like(value)
        return lax.ppermute(value, "ctx", pairs)

    kv_a = send(own_kv, even_to_odd)
    kv_b = send(jnp.concatenate([own_kv, kv_a], axis=1), odd_to_next)
    kv_c1 = send(kv_b[:, :kv_width], even_to_even)
    kv_c2 = send(kv_b, even_to_odd)
    odd_src = [(mixed, per_device), (kv_a, 0), (kv_c2, 0), (kv_c2, 2 * kv_local)]
    even_src = [(mixed, per_device), (kv_b, 0), (kv_b, 2 * kv_local), (kv_c1, 0)]

    lhpb = min(local_heads, group_size)
    lsteps = local_heads // lhpb
    lwide = lhpb * HD
    tail = pl.pallas_call(
        lambda *refs: tail_kernel(lhpb, ndocs, *refs),
        out_shape=jax.ShapeDtypeStruct((local_heads, HD, HD), F32),
        grid=(lsteps,),
        in_specs=[smem_spec(), smem_spec(), col_spec(rows, lwide), col_spec(rows, lwide)],
        out_specs=pl.BlockSpec((lhpb, HD, HD), lambda h: (h, 0, 0)),
        compiler_params=params(),
        cost_estimate=pl.CostEstimate(
            flops=2 * rows * HD * HD * local_heads,
            transcendentals=0,
            bytes_accessed=2 * rows * width * 2 + local_heads * HD * HD * 4,
        ),
    )(lengths, shard_start, lin_key, lin_value)

    lin_local = pl.pallas_call(
        lambda *refs: lin_local_kernel(lhpb, ndocs, *refs),
        out_shape=jax.ShapeDtypeStruct((rows, width), F32),
        grid=(lsteps,),
        in_specs=[
            smem_spec(),
            smem_spec(),
            col_spec(rows, lwide),
            col_spec(rows, lwide),
            col_spec(rows, lwide),
        ],
        out_specs=col_spec(rows, lwide),
        compiler_params=params(),
        cost_estimate=pl.CostEstimate(
            flops=6 * rows * rows * HD * local_heads,
            transcendentals=0,
            bytes_accessed=3 * rows * width * 2 + rows * width * 4,
        ),
    )(lengths, shard_start, lin_query, lin_key, lin_value)

    def through(shard):
        first = shard * rows
        return (doc_at(first - 1) == doc_at(first + rows - 1)).astype(F32)

    here = lax.axis_index("ctx")
    state_a = send(tail, even_to_odd)
    state_v = tail + through_own * state_a
    lin_local, state_v = lax.optimization_barrier((lin_local, state_v))
    state_b = send(state_v, odd_to_next)
    state_c1 = send(through(here) * through(here + 1) * state_b, even_to_even)
    state_c2 = send(state_b, even_to_odd)

    blocks = SPAN + 1
    shpb = min(per_device, group_size)
    ssteps = per_device // shpb
    kv_index = lambda i: (i * shpb * kv_local) // per_device
    def kv_spec(offset, value):
        base = offset + (kv_local if value else 0)
        return pl.BlockSpec((rows, HD), lambda i: (0, base + kv_index(i)))

    kv_arrays, kv_specs = [], []
    for value in (False, True):
        for m in range(blocks):
            for source in ((odd_src[m],) if m == 0 else (odd_src[m], even_src[m])):
                kv_arrays.append(source[0])
                kv_specs.append(kv_spec(source[1], value))

    attended = pl.pallas_call(
        lambda *refs: soft_kernel(blocks, shpb, ndocs, *refs),
        out_shape=jax.ShapeDtypeStruct((rows, per_device * HD), BF16),
        grid=(ssteps,),
        in_specs=[smem_spec(), smem_spec(), col_spec(rows, shpb * HD)] + kv_specs,
        out_specs=col_spec(rows, shpb * HD),
        scratch_shapes=[
            pltpu.VMEM((blocks, shpb, rows, rows), F32),
            pltpu.VMEM((shpb, rows, 1), F32),
            pltpu.VMEM((shpb, rows, 1), F32),
            pltpu.VMEM((shpb, rows, HD), F32),
        ],
        compiler_params=pltpu.CompilerParams(
            dimension_semantics=("arbitrary",), vmem_limit_bytes=48 * 1024 * 1024
        ),
        cost_estimate=pl.CostEstimate(
            flops=4 * rows * rows * blocks * HD * per_device,
            transcendentals=rows * rows * blocks * per_device,
            bytes_accessed=rows * per_device * HD * 4 + 2 * blocks * rows * HD * 2 * per_device,
        ),
    )(lengths, shard_start, mixed, *kv_arrays)

    lightning_out = pl.pallas_call(
        lambda *refs: lin_finish_kernel(lhpb, ndocs, *refs),
        out_shape=jax.ShapeDtypeStruct((rows, width), BF16),
        grid=(lsteps,),
        in_specs=[
            smem_spec(),
            smem_spec(),
            col_spec(rows, lwide),
            pl.BlockSpec((lhpb, HD, HD), lambda h: (h, 0, 0)),
            pl.BlockSpec((lhpb, HD, HD), lambda h: (h, 0, 0)),
            pl.BlockSpec((lhpb, HD, HD), lambda h: (h, 0, 0)),
            pl.BlockSpec((lhpb, HD, HD), lambda h: (h, 0, 0)),
            col_spec(rows, lwide),
            pl.BlockSpec((1, lwide), lambda h: (0, h)),
        ],
        out_specs=col_spec(rows, lwide),
        compiler_params=params(),
        cost_estimate=pl.CostEstimate(
            flops=4 * rows * HD * HD * local_heads,
            transcendentals=rows * local_heads,
            bytes_accessed=rows * width * (2 + 4 + 2) + local_heads * HD * HD * 4,
        ),
    )(
        lengths,
        shard_start,
        lin_query,
        state_a,
        state_c2,
        state_b,
        state_c1,
        lin_local,
        norm_gain.reshape(1, width),
    )
    return (lightning_out, attended)


def solution(mesh):
    placed = (
        P("ctx", "head"),
        P("ctx", "head"),
        P("ctx", "head"),
        P("head"),
        P(("ctx", "head"), None),
        P(("ctx", "head"), None),
        P(("ctx", "head"), None),
        P(),
    )
    return jax.shard_map(
        body,
        mesh=mesh,
        in_specs=placed,
        out_specs=(P("ctx", "head"), P("ctx", "head")),
        check_vma=False,
    )
```

```python
import math

import jax
import jax.numpy as jnp
import numpy as np
from jax import lax
from jax.experimental import pallas as pl
from jax.experimental.pallas import tpu as pltpu
from jax.sharding import PartitionSpec as P

HEADS = 64
HD = 128
KV_HEADS = 8
SPAN = 3

F32 = jnp.float32
BF16 = jnp.bfloat16


def document_index(doc_lengths, positions):
    doc_ends = jnp.cumsum(doc_lengths)
    counted = jnp.sum((positions[:, None] >= doc_ends[None, :]).astype(jnp.int32), axis=1)
    return jnp.where(positions < 0, -1, counted).astype(jnp.int32)


def from_behind(value, axis, steps):
    count = lax.axis_size(axis)
    pairs = [(source, source + steps) for source in range(0, count - steps)]
    if not pairs:
        return jnp.zeros_like(value)
    return lax.ppermute(value, axis, pairs)


def split_bf16(x):
    hi = x.astype(BF16)
    lo = (x - hi.astype(F32)).astype(BF16)
    return hi, lo


def dot_nt(a, b):
    return lax.dot_general(a, b, (((1,), (1,)), ((), ())), preferred_element_type=F32)


def head_cols(j):
    return slice(j * HD, (j + 1) * HD)


def doc_ends(len_ref, ndocs):
    ends = []
    total = jnp.int32(0)
    for i in range(ndocs):
        total = total + len_ref[i]
        ends.append(total)
    return ends


def doc_of(ends, pos):
    counted = jnp.zeros_like(pos)
    for e in ends:
        counted = counted + (pos >= e).astype(jnp.int32)
    return jnp.where(pos < 0, -1, counted)


def tail_kernel(hpb, ndocs, len_ref, start_ref, k_ref, v_ref, t_ref):
    rows = k_ref.shape[0]
    ends = doc_ends(len_ref, ndocs)
    start = start_ref[0]
    pos = start + lax.broadcasted_iota(jnp.int32, (rows, 1), 0)
    last = doc_of(ends, start + rows - 1)
    mask = (doc_of(ends, pos) == last).astype(BF16)
    for j in range(hpb):
        masked = v_ref[:, head_cols(j)] * mask
        t_ref[j] = lax.dot_general(
            k_ref[:, head_cols(j)], masked, (((0,), (0,)), ((), ())), preferred_element_type=F32
        )


def lin_local_kernel(hpb, ndocs, len_ref, start_ref, q_ref, k_ref, v_ref, lin_ref):
    rows = q_ref.shape[0]
    ends = doc_ends(len_ref, ndocs)
    start = start_ref[0]
    qpos = start + lax.broadcasted_iota(jnp.int32, (rows, 1), 0)
    kpos = start + lax.broadcasted_iota(jnp.int32, (1, rows), 1)
    visible = (doc_of(ends, qpos) == doc_of(ends, kpos)) & (kpos <= qpos)
    for j in range(hpb):
        scores = dot_nt(q_ref[:, head_cols(j)], k_ref[:, head_cols(j)])
        scores = jnp.where(visible, scores, 0.0)
        hi, lo = split_bf16(scores)
        v = v_ref[:, head_cols(j)]
        lin_ref[:, head_cols(j)] = jnp.dot(hi, v, preferred_element_type=F32) + jnp.dot(
            lo, v, preferred_element_type=F32
        )


def lin_finish_kernel(
    hpb, ndocs, len_ref, start_ref, q_ref, a_ref, c2_ref, b_ref, c1_ref, lin_ref, g_ref, o_ref
):
    rows = q_ref.shape[0]
    ends = doc_ends(len_ref, ndocs)
    start = start_ref[0]
    pos = start + lax.broadcasted_iota(jnp.int32, (rows, 1), 0)
    sees = (doc_of(ends, pos) == doc_of(ends, start - 1)).astype(F32)
    odd = lax.rem(start // rows, 2) == 1
    through_prev = (doc_of(ends, start - rows - 1) == doc_of(ends, start - 1)).astype(F32)
    for j in range(hpb):
        state = jnp.where(odd, a_ref[j] + through_prev * c2_ref[j], b_ref[j] + c1_ref[j])
        hi, lo = split_bf16(state)
        q = q_ref[:, head_cols(j)]
        carried = jnp.dot(q, hi, preferred_element_type=F32) + jnp.dot(
            q, lo, preferred_element_type=F32
        )
        lin = lin_ref[:, head_cols(j)] + carried * sees
        mean_sq = jnp.mean(lin * lin, axis=-1, keepdims=True)
        normed = lin * lax.rsqrt(mean_sq + 1e-06) * g_ref[:, head_cols(j)]
        o_ref[:, head_cols(j)] = normed.astype(o_ref.dtype)


def col_spec(rows, width=HD):
    return pl.BlockSpec((rows, width), lambda h: (0, h))


def full_spec(shape):
    return pl.BlockSpec(shape, lambda h: (0,) * len(shape))


def params():
    return pltpu.CompilerParams(dimension_semantics=("arbitrary",))


def soft_kernel(blocks, hpb, ndocs, len_ref, start_ref, q_ref, *rest):
    per_kind = 2 * blocks - 1
    o_ref = rest[2 * per_kind]
    s_ref, mx_ref, tot_ref, acc_ref = rest[2 * per_kind + 1 :]
    rows = q_ref.shape[0]
    odd = lax.rem(start_ref[0] // rows, 2) == 1

    def pick(refs):
        picked = [lambda: refs[0][...]]
        for m in range(1, blocks):
            picked.append(
                lambda m=m: jnp.where(odd, refs[2 * m - 1][...], refs[2 * m][...])
            )
        return picked

    key_refs = pick(rest[0:per_kind])
    value_refs = pick(rest[per_kind : 2 * per_kind])
    scale = 1.0 / math.sqrt(HD)
    ends = doc_ends(len_ref, ndocs)
    start = start_ref[0]
    qpos = start + lax.broadcasted_iota(jnp.int32, (rows, 1), 0)
    kpos = start + lax.broadcasted_iota(jnp.int32, (1, rows), 1)
    dq = doc_of(ends, qpos)
    first_doc = doc_of(ends, start)
    q = jnp.concatenate([q_ref[:, head_cols(j)] for j in range(hpb)], axis=0)

    def block_scores(m):
        shifted = kpos - m * rows
        visible = dq == doc_of(ends, shifted)
        if m == 0:
            visible = visible & (shifted <= qpos)
        s = dot_nt(q, key_refs[m]()).reshape(hpb, rows, rows) * scale
        return jnp.where(visible[None], s, -1e30)

    def needed(m):
        return doc_of(ends, start - (m - 1) * rows - 1) == first_doc

    s0 = block_scores(0)
    s_ref[0] = s0
    mx_ref[...] = jnp.max(s0, axis=-1, keepdims=True)
    for m in range(1, blocks):

        @pl.when(needed(m))
        def _():
            s = block_scores(m)
            s_ref[m] = s
            mx_ref[...] = jnp.maximum(mx_ref[...], jnp.max(s, axis=-1, keepdims=True))

    def weighted(m):
        w = jnp.exp(s_ref[m] - mx_ref[...])
        part = jnp.sum(w, axis=-1, keepdims=True)
        term = jnp.dot(
            w.reshape(hpb * rows, rows).astype(BF16),
            value_refs[m](),
            preferred_element_type=F32,
        ).reshape(hpb, rows, HD)
        return part, term

    part, term = weighted(0)
    tot_ref[...] = part
    acc_ref[...] = term
    for m in range(1, blocks):

        @pl.when(needed(m))
        def _():
            part, term = weighted(m)
            tot_ref[...] += part
            acc_ref[...] += term

    out = acc_ref[...] / tot_ref[...]
    for j in range(hpb):
        o_ref[:, head_cols(j)] = out[j].astype(o_ref.dtype)


def smem_spec():
    return pl.BlockSpec(memory_space=pltpu.SMEM)


def body(lin_query, lin_key, lin_value, norm_gain, soft_query, soft_key, soft_value, doc_lengths):
    rows, width = lin_query.shape
    local_heads = width // HD
    ndocs = doc_lengths.shape[0]
    lengths = doc_lengths.astype(jnp.int32)
    shard_start = (lax.axis_index("ctx") * rows).astype(jnp.int32).reshape(1)
    ends = jnp.cumsum(lengths)

    def doc_at(pos):
        return jnp.where(pos < 0, -1, jnp.sum((pos >= ends).astype(jnp.int32)))

    through_own = (doc_at(shard_start[0] - 1) == doc_at(shard_start[0] + rows - 1)).astype(F32)

    head_devices = lax.axis_size("head")
    group_size = HEADS // KV_HEADS
    per_device = HEADS // head_devices
    kv_local = max(1, per_device // group_size)
    kv_table = (
        np.arange(head_devices)[:, None] * per_device // group_size + np.arange(kv_local)[None, :]
    ).reshape(-1)
    short_rows = soft_key.shape[0]

    def spread(field):
        if np.array_equal(kv_table, np.arange(KV_HEADS)):
            return field.reshape(short_rows, head_devices, kv_local * HD)
        taken = jnp.take(field.reshape(short_rows, KV_HEADS, HD), kv_table, axis=1)
        return taken.reshape(short_rows, head_devices, kv_local * HD)

    kv_packed = jnp.concatenate([spread(soft_key), spread(soft_value)], axis=2)
    kv_packed = kv_packed.reshape(short_rows, head_devices * 2 * kv_local * HD)
    own_kv = lax.all_to_all(kv_packed, "head", split_axis=1, concat_axis=0, tiled=True)
    mixed = lax.all_to_all(soft_query, "head", split_axis=1, concat_axis=0, tiled=True)
    kv_width = own_kv.shape[1]

    n_ctx = lax.axis_size("ctx")
    even_to_odd = [(c, c + 1) for c in range(0, n_ctx - 1, 2)]
    odd_to_next = [(c, c + 1) for c in range(1, n_ctx - 1, 2)]
    even_to_even = [(c, c + 2) for c in range(0, n_ctx - 2, 2)]
    is_odd = lax.rem(lax.axis_index("ctx"), 2) == 1

    def send(value, pairs):
        if not pairs:
            return jnp.zeros_like(value)
        return lax.ppermute(value, "ctx", pairs)

    kv_a = send(own_kv, even_to_odd)
    kv_b = send(jnp.concatenate([own_kv, kv_a], axis=1), odd_to_next)
    mixed, kv_b = lax.optimization_barrier((mixed, kv_b))
    kv_c1 = send(kv_b[:, :kv_width], even_to_even)
    kv_c2 = send(kv_b, even_to_odd)
    odd_src = [(own_kv, 0), (kv_a, 0), (kv_c2, 0), (kv_c2, 2 * kv_local)]
    even_src = [(own_kv, 0), (kv_b, 0), (kv_b, 2 * kv_local), (kv_c1, 0)]

    lhpb = min(local_heads, group_size)
    lsteps = local_heads // lhpb
    lwide = lhpb * HD
    tail = pl.pallas_call(
        lambda *refs: tail_kernel(lhpb, ndocs, *refs),
        out_shape=jax.ShapeDtypeStruct((local_heads, HD, HD), F32),
        grid=(lsteps,),
        in_specs=[smem_spec(), smem_spec(), col_spec(rows, lwide), col_spec(rows, lwide)],
        out_specs=pl.BlockSpec((lhpb, HD, HD), lambda h: (h, 0, 0)),
        compiler_params=params(),
        cost_estimate=pl.CostEstimate(
            flops=2 * rows * HD * HD * local_heads,
            transcendentals=0,
            bytes_accessed=2 * rows * width * 2 + local_heads * HD * HD * 4,
        ),
    )(lengths, shard_start, lin_key, lin_value)

    lin_local = pl.pallas_call(
        lambda *refs: lin_local_kernel(lhpb, ndocs, *refs),
        out_shape=jax.ShapeDtypeStruct((rows, width), F32),
        grid=(lsteps,),
        in_specs=[
            smem_spec(),
            smem_spec(),
            col_spec(rows, lwide),
            col_spec(rows, lwide),
            col_spec(rows, lwide),
        ],
        out_specs=col_spec(rows, lwide),
        compiler_params=params(),
        cost_estimate=pl.CostEstimate(
            flops=6 * rows * rows * HD * local_heads,
            transcendentals=0,
            bytes_accessed=3 * rows * width * 2 + rows * width * 4,
        ),
    )(lengths, shard_start, lin_query, lin_key, lin_value)

    def through(shard):
        first = shard * rows
        return (doc_at(first - 1) == doc_at(first + rows - 1)).astype(F32)

    here = lax.axis_index("ctx")
    state_a = send(tail, even_to_odd)
    state_v = tail + through_own * state_a
    lin_local, state_v = lax.optimization_barrier((lin_local, state_v))
    state_b = send(state_v, odd_to_next)
    state_c1 = send(through(here) * through(here + 1) * state_b, even_to_even)
    state_c2 = send(state_b, even_to_odd)

    blocks = SPAN + 1
    shpb = min(per_device, group_size)
    ssteps = per_device // shpb
    kv_index = lambda i: (i * shpb * kv_local) // per_device
    def kv_spec(offset, value):
        base = offset + (kv_local if value else 0)
        return pl.BlockSpec((rows, HD), lambda i: (0, base + kv_index(i)))

    kv_arrays, kv_specs = [], []
    for value in (False, True):
        for m in range(blocks):
            for source in ((odd_src[m],) if m == 0 else (odd_src[m], even_src[m])):
                kv_arrays.append(source[0])
                kv_specs.append(kv_spec(source[1], value))

    attended = pl.pallas_call(
        lambda *refs: soft_kernel(blocks, shpb, ndocs, *refs),
        out_shape=jax.ShapeDtypeStruct((rows, per_device * HD), BF16),
        grid=(ssteps,),
        in_specs=[smem_spec(), smem_spec(), col_spec(rows, shpb * HD)] + kv_specs,
        out_specs=col_spec(rows, shpb * HD),
        scratch_shapes=[
            pltpu.VMEM((blocks, shpb, rows, rows), F32),
            pltpu.VMEM((shpb, rows, 1), F32),
            pltpu.VMEM((shpb, rows, 1), F32),
            pltpu.VMEM((shpb, rows, HD), F32),
        ],
        compiler_params=pltpu.CompilerParams(
            dimension_semantics=("arbitrary",), vmem_limit_bytes=48 * 1024 * 1024
        ),
        cost_estimate=pl.CostEstimate(
            flops=4 * rows * rows * blocks * HD * per_device,
            transcendentals=rows * rows * blocks * per_device,
            bytes_accessed=rows * per_device * HD * 4 + 2 * blocks * rows * HD * 2 * per_device,
        ),
    )(lengths, shard_start, mixed, *kv_arrays)

    lightning_out = pl.pallas_call(
        lambda *refs: lin_finish_kernel(lhpb, ndocs, *refs),
        out_shape=jax.ShapeDtypeStruct((rows, width), BF16),
        grid=(lsteps,),
        in_specs=[
            smem_spec(),
            smem_spec(),
            col_spec(rows, lwide),
            pl.BlockSpec((lhpb, HD, HD), lambda h: (h, 0, 0)),
            pl.BlockSpec((lhpb, HD, HD), lambda h: (h, 0, 0)),
            pl.BlockSpec((lhpb, HD, HD), lambda h: (h, 0, 0)),
            pl.BlockSpec((lhpb, HD, HD), lambda h: (h, 0, 0)),
            col_spec(rows, lwide),
            pl.BlockSpec((1, lwide), lambda h: (0, h)),
        ],
        out_specs=col_spec(rows, lwide),
        compiler_params=params(),
        cost_estimate=pl.CostEstimate(
            flops=4 * rows * HD * HD * local_heads,
            transcendentals=rows * local_heads,
            bytes_accessed=rows * width * (2 + 4 + 2) + local_heads * HD * HD * 4,
        ),
    )(
        lengths,
        shard_start,
        lin_query,
        state_a,
        state_c2,
        state_b,
        state_c1,
        lin_local,
        norm_gain.reshape(1, width),
    )
    return (lightning_out, attended)


def solution(mesh):
    placed = (
        P("ctx", "head"),
        P("ctx", "head"),
        P("ctx", "head"),
        P("head"),
        P(("ctx", "head"), None),
        P(("ctx", "head"), None),
        P(("ctx", "head"), None),
        P(),
    )
    return jax.shard_map(
        body,
        mesh=mesh,
        in_specs=placed,
        out_specs=(P("ctx", "head"), P("ctx", "head")),
        check_vma=False,
    )
```

```python
import math

import jax
import jax.numpy as jnp
import numpy as np
from jax import lax
from jax.experimental import pallas as pl
from jax.experimental.pallas import tpu as pltpu
from jax.sharding import PartitionSpec as P

HEADS = 64
HD = 128
KV_HEADS = 8
SPAN = 3

F32 = jnp.float32
BF16 = jnp.bfloat16


def document_index(doc_lengths, positions):
    doc_ends = jnp.cumsum(doc_lengths)
    counted = jnp.sum((positions[:, None] >= doc_ends[None, :]).astype(jnp.int32), axis=1)
    return jnp.where(positions < 0, -1, counted).astype(jnp.int32)


def from_behind(value, axis, steps):
    count = lax.axis_size(axis)
    pairs = [(source, source + steps) for source in range(0, count - steps)]
    if not pairs:
        return jnp.zeros_like(value)
    return lax.ppermute(value, axis, pairs)


def split_bf16(x):
    hi = x.astype(BF16)
    lo = (x - hi.astype(F32)).astype(BF16)
    return hi, lo


def dot_nt(a, b):
    return lax.dot_general(a, b, (((1,), (1,)), ((), ())), preferred_element_type=F32)


def head_cols(j):
    return slice(j * HD, (j + 1) * HD)


def doc_ends(len_ref, ndocs):
    ends = []
    total = jnp.int32(0)
    for i in range(ndocs):
        total = total + len_ref[i]
        ends.append(total)
    return ends


def doc_of(ends, pos):
    counted = jnp.zeros_like(pos)
    for e in ends:
        counted = counted + (pos >= e).astype(jnp.int32)
    return jnp.where(pos < 0, -1, counted)


def tail_kernel(hpb, ndocs, len_ref, start_ref, k_ref, v_ref, t_ref):
    rows = k_ref.shape[0]
    ends = doc_ends(len_ref, ndocs)
    start = start_ref[0]
    pos = start + lax.broadcasted_iota(jnp.int32, (rows, 1), 0)
    last = doc_of(ends, start + rows - 1)
    mask = (doc_of(ends, pos) == last).astype(BF16)
    for j in range(hpb):
        masked = v_ref[:, head_cols(j)] * mask
        t_ref[j] = lax.dot_general(
            k_ref[:, head_cols(j)], masked, (((0,), (0,)), ((), ())), preferred_element_type=F32
        )


def lin_local_kernel(hpb, ndocs, len_ref, start_ref, q_ref, k_ref, v_ref, lin_ref):
    rows = q_ref.shape[0]
    ends = doc_ends(len_ref, ndocs)
    start = start_ref[0]
    qpos = start + lax.broadcasted_iota(jnp.int32, (rows, 1), 0)
    kpos = start + lax.broadcasted_iota(jnp.int32, (1, rows), 1)
    visible = (doc_of(ends, qpos) == doc_of(ends, kpos)) & (kpos <= qpos)
    for j in range(hpb):
        scores = dot_nt(q_ref[:, head_cols(j)], k_ref[:, head_cols(j)])
        scores = jnp.where(visible, scores, 0.0)
        hi, lo = split_bf16(scores)
        v = v_ref[:, head_cols(j)]
        lin_ref[:, head_cols(j)] = jnp.dot(hi, v, preferred_element_type=F32) + jnp.dot(
            lo, v, preferred_element_type=F32
        )


def lin_finish_kernel(
    hpb, ndocs, len_ref, start_ref, q_ref, a_ref, c2_ref, b_ref, c1_ref, lin_ref, g_ref, o_ref
):
    rows = q_ref.shape[0]
    ends = doc_ends(len_ref, ndocs)
    start = start_ref[0]
    pos = start + lax.broadcasted_iota(jnp.int32, (rows, 1), 0)
    sees = (doc_of(ends, pos) == doc_of(ends, start - 1)).astype(F32)
    odd = lax.rem(start // rows, 2) == 1
    through_prev = (doc_of(ends, start - rows - 1) == doc_of(ends, start - 1)).astype(F32)
    for j in range(hpb):
        state = jnp.where(odd, a_ref[j] + through_prev * c2_ref[j], b_ref[j] + c1_ref[j])
        hi, lo = split_bf16(state)
        q = q_ref[:, head_cols(j)]
        carried = jnp.dot(q, hi, preferred_element_type=F32) + jnp.dot(
            q, lo, preferred_element_type=F32
        )
        lin = lin_ref[:, head_cols(j)] + carried * sees
        mean_sq = jnp.mean(lin * lin, axis=-1, keepdims=True)
        normed = lin * lax.rsqrt(mean_sq + 1e-06) * g_ref[:, head_cols(j)]
        o_ref[:, head_cols(j)] = normed.astype(o_ref.dtype)


def col_spec(rows, width=HD):
    return pl.BlockSpec((rows, width), lambda h: (0, h))


def full_spec(shape):
    return pl.BlockSpec(shape, lambda h: (0,) * len(shape))


def params():
    return pltpu.CompilerParams(dimension_semantics=("arbitrary",))


def soft_kernel(blocks, hpb, ndocs, len_ref, start_ref, q_ref, *rest):
    per_kind = 2 * blocks - 1
    o_ref = rest[2 * per_kind]
    s_ref, mx_ref, tot_ref, acc_ref = rest[2 * per_kind + 1 :]
    rows = q_ref.shape[0]
    odd = lax.rem(start_ref[0] // rows, 2) == 1

    def pick(refs):
        picked = [lambda: refs[0][...]]
        for m in range(1, blocks):
            picked.append(
                lambda m=m: jnp.where(odd, refs[2 * m - 1][...], refs[2 * m][...])
            )
        return picked

    key_refs = pick(rest[0:per_kind])
    value_refs = pick(rest[per_kind : 2 * per_kind])
    scale = 1.0 / math.sqrt(HD)
    ends = doc_ends(len_ref, ndocs)
    start = start_ref[0]
    qpos = start + lax.broadcasted_iota(jnp.int32, (rows, 1), 0)
    kpos = start + lax.broadcasted_iota(jnp.int32, (1, rows), 1)
    dq = doc_of(ends, qpos)
    first_doc = doc_of(ends, start)
    q = jnp.concatenate([q_ref[:, head_cols(j)] for j in range(hpb)], axis=0)

    def block_scores(m):
        shifted = kpos - m * rows
        visible = dq == doc_of(ends, shifted)
        if m == 0:
            visible = visible & (shifted <= qpos)
        s = dot_nt(q, key_refs[m]()).reshape(hpb, rows, rows) * scale
        return jnp.where(visible[None], s, -1e30)

    def needed(m):
        return doc_of(ends, start - (m - 1) * rows - 1) == first_doc

    s0 = block_scores(0)
    s_ref[0] = s0
    mx_ref[...] = jnp.max(s0, axis=-1, keepdims=True)
    for m in range(1, blocks):

        @pl.when(needed(m))
        def _():
            s = block_scores(m)
            s_ref[m] = s
            mx_ref[...] = jnp.maximum(mx_ref[...], jnp.max(s, axis=-1, keepdims=True))

    def weighted(m):
        w = jnp.exp(s_ref[m] - mx_ref[...])
        part = jnp.sum(w, axis=-1, keepdims=True)
        term = jnp.dot(
            w.reshape(hpb * rows, rows).astype(BF16),
            value_refs[m](),
            preferred_element_type=F32,
        ).reshape(hpb, rows, HD)
        return part, term

    part, term = weighted(0)
    tot_ref[...] = part
    acc_ref[...] = term
    for m in range(1, blocks):

        @pl.when(needed(m))
        def _():
            part, term = weighted(m)
            tot_ref[...] += part
            acc_ref[...] += term

    out = acc_ref[...] / tot_ref[...]
    for j in range(hpb):
        o_ref[:, head_cols(j)] = out[j].astype(o_ref.dtype)


def smem_spec():
    return pl.BlockSpec(memory_space=pltpu.SMEM)


def body(lin_query, lin_key, lin_value, norm_gain, soft_query, soft_key, soft_value, doc_lengths):
    rows, width = lin_query.shape
    local_heads = width // HD
    ndocs = doc_lengths.shape[0]
    lengths = doc_lengths.astype(jnp.int32)
    shard_start = (lax.axis_index("ctx") * rows).astype(jnp.int32).reshape(1)
    ends = jnp.cumsum(lengths)

    def doc_at(pos):
        return jnp.where(pos < 0, -1, jnp.sum((pos >= ends).astype(jnp.int32)))

    through_own = (doc_at(shard_start[0] - 1) == doc_at(shard_start[0] + rows - 1)).astype(F32)

    head_devices = lax.axis_size("head")
    group_size = HEADS // KV_HEADS
    per_device = HEADS // head_devices
    kv_local = max(1, per_device // group_size)
    kv_table = (
        np.arange(head_devices)[:, None] * per_device // group_size + np.arange(kv_local)[None, :]
    ).reshape(-1)
    short_rows = soft_key.shape[0]

    def spread(field):
        if np.array_equal(kv_table, np.arange(KV_HEADS)):
            return field.reshape(short_rows, head_devices, kv_local * HD)
        taken = jnp.take(field.reshape(short_rows, KV_HEADS, HD), kv_table, axis=1)
        return taken.reshape(short_rows, head_devices, kv_local * HD)

    packed = jnp.concatenate(
        [
            soft_query.reshape(short_rows, head_devices, per_device * HD),
            spread(soft_key),
            spread(soft_value),
        ],
        axis=2,
    )
    packed = packed.reshape(short_rows, head_devices * packed.shape[2])
    mixed = lax.all_to_all(packed, "head", split_axis=1, concat_axis=0, tiled=True)

    n_ctx = lax.axis_size("ctx")
    even_to_odd = [(c, c + 1) for c in range(0, n_ctx - 1, 2)]
    odd_to_next = [(c, c + 1) for c in range(1, n_ctx - 1, 2)]
    even_to_even = [(c, c + 2) for c in range(0, n_ctx - 2, 2)]
    is_odd = lax.rem(lax.axis_index("ctx"), 2) == 1

    def send(value, pairs):
        if not pairs:
            return jnp.zeros_like(value)
        return lax.ppermute(value, "ctx", pairs)

    raw = jnp.concatenate([soft_key, soft_value], axis=1)
    raw_width = raw.shape[1]
    raw_a = send(raw, even_to_odd)
    raw_b = send(jnp.concatenate([raw, raw_a], axis=1), odd_to_next)
    raw_c1 = send(raw_b[:, :raw_width], even_to_even)
    raw_c2 = send(raw_b, even_to_odd)
    older_raw = [
        jnp.where(is_odd, raw_a, raw_b[:, :raw_width]),
        jnp.where(is_odd, raw_c2[:, :raw_width], raw_b[:, raw_width:]),
        jnp.where(is_odd, raw_c2[:, raw_width:], raw_c1),
    ]
    older_pieces = []
    for shard in older_raw:
        older_pieces.append(spread(shard[:, : KV_HEADS * HD]))
        older_pieces.append(spread(shard[:, KV_HEADS * HD :]))
    older_packed = jnp.concatenate(older_pieces, axis=2)
    older_packed = older_packed.reshape(short_rows, head_devices * older_packed.shape[2])
    older = lax.all_to_all(older_packed, "head", split_axis=1, concat_axis=0, tiled=True)
    odd_src = [(mixed, per_device)] + [(older, 2 * kv_local * m) for m in range(SPAN)]
    even_src = odd_src

    lhpb = min(local_heads, group_size)
    lsteps = local_heads // lhpb
    lwide = lhpb * HD
    tail = pl.pallas_call(
        lambda *refs: tail_kernel(lhpb, ndocs, *refs),
        out_shape=jax.ShapeDtypeStruct((local_heads, HD, HD), F32),
        grid=(lsteps,),
        in_specs=[smem_spec(), smem_spec(), col_spec(rows, lwide), col_spec(rows, lwide)],
        out_specs=pl.BlockSpec((lhpb, HD, HD), lambda h: (h, 0, 0)),
        compiler_params=params(),
        cost_estimate=pl.CostEstimate(
            flops=2 * rows * HD * HD * local_heads,
            transcendentals=0,
            bytes_accessed=2 * rows * width * 2 + local_heads * HD * HD * 4,
        ),
    )(lengths, shard_start, lin_key, lin_value)

    lin_local = pl.pallas_call(
        lambda *refs: lin_local_kernel(lhpb, ndocs, *refs),
        out_shape=jax.ShapeDtypeStruct((rows, width), F32),
        grid=(lsteps,),
        in_specs=[
            smem_spec(),
            smem_spec(),
            col_spec(rows, lwide),
            col_spec(rows, lwide),
            col_spec(rows, lwide),
        ],
        out_specs=col_spec(rows, lwide),
        compiler_params=params(),
        cost_estimate=pl.CostEstimate(
            flops=6 * rows * rows * HD * local_heads,
            transcendentals=0,
            bytes_accessed=3 * rows * width * 2 + rows * width * 4,
        ),
    )(lengths, shard_start, lin_query, lin_key, lin_value)

    def through(shard):
        first = shard * rows
        return (doc_at(first - 1) == doc_at(first + rows - 1)).astype(F32)

    here = lax.axis_index("ctx")
    state_a = send(tail, even_to_odd)
    state_v = tail + through_own * state_a
    lin_local, state_v = lax.optimization_barrier((lin_local, state_v))
    state_b = send(state_v, odd_to_next)
    state_c1 = send(through(here) * through(here + 1) * state_b, even_to_even)
    state_c2 = send(state_b, even_to_odd)

    blocks = SPAN + 1
    shpb = min(per_device, group_size)
    ssteps = per_device // shpb
    kv_index = lambda i: (i * shpb * kv_local) // per_device
    def kv_spec(offset, value):
        base = offset + (kv_local if value else 0)
        return pl.BlockSpec((rows, HD), lambda i: (0, base + kv_index(i)))

    kv_arrays, kv_specs = [], []
    for value in (False, True):
        for m in range(blocks):
            for source in ((odd_src[m],) if m == 0 else (odd_src[m], even_src[m])):
                kv_arrays.append(source[0])
                kv_specs.append(kv_spec(source[1], value))

    attended = pl.pallas_call(
        lambda *refs: soft_kernel(blocks, shpb, ndocs, *refs),
        out_shape=jax.ShapeDtypeStruct((rows, per_device * HD), BF16),
        grid=(ssteps,),
        in_specs=[smem_spec(), smem_spec(), col_spec(rows, shpb * HD)] + kv_specs,
        out_specs=col_spec(rows, shpb * HD),
        scratch_shapes=[
            pltpu.VMEM((blocks, shpb, rows, rows), F32),
            pltpu.VMEM((shpb, rows, 1), F32),
            pltpu.VMEM((shpb, rows, 1), F32),
            pltpu.VMEM((shpb, rows, HD), F32),
        ],
        compiler_params=pltpu.CompilerParams(
            dimension_semantics=("arbitrary",), vmem_limit_bytes=48 * 1024 * 1024
        ),
        cost_estimate=pl.CostEstimate(
            flops=4 * rows * rows * blocks * HD * per_device,
            transcendentals=rows * rows * blocks * per_device,
            bytes_accessed=rows * per_device * HD * 4 + 2 * blocks * rows * HD * 2 * per_device,
        ),
    )(lengths, shard_start, mixed, *kv_arrays)

    lightning_out = pl.pallas_call(
        lambda *refs: lin_finish_kernel(lhpb, ndocs, *refs),
        out_shape=jax.ShapeDtypeStruct((rows, width), BF16),
        grid=(lsteps,),
        in_specs=[
            smem_spec(),
            smem_spec(),
            col_spec(rows, lwide),
            pl.BlockSpec((lhpb, HD, HD), lambda h: (h, 0, 0)),
            pl.BlockSpec((lhpb, HD, HD), lambda h: (h, 0, 0)),
            pl.BlockSpec((lhpb, HD, HD), lambda h: (h, 0, 0)),
            pl.BlockSpec((lhpb, HD, HD), lambda h: (h, 0, 0)),
            col_spec(rows, lwide),
            pl.BlockSpec((1, lwide), lambda h: (0, h)),
        ],
        out_specs=col_spec(rows, lwide),
        compiler_params=params(),
        cost_estimate=pl.CostEstimate(
            flops=4 * rows * HD * HD * local_heads,
            transcendentals=rows * local_heads,
            bytes_accessed=rows * width * (2 + 4 + 2) + local_heads * HD * HD * 4,
        ),
    )(
        lengths,
        shard_start,
        lin_query,
        state_a,
        state_c2,
        state_b,
        state_c1,
        lin_local,
        norm_gain.reshape(1, width),
    )
    return (lightning_out, attended)


def solution(mesh):
    placed = (
        P("ctx", "head"),
        P("ctx", "head"),
        P("ctx", "head"),
        P("head"),
        P(("ctx", "head"), None),
        P(("ctx", "head"), None),
        P(("ctx", "head"), None),
        P(),
    )
    return jax.shard_map(
        body,
        mesh=mesh,
        in_specs=placed,
        out_specs=(P("ctx", "head"), P("ctx", "head")),
        check_vma=False,
    )
```

```python
import math

import jax
import jax.numpy as jnp
import numpy as np
from jax import lax
from jax.experimental import pallas as pl
from jax.experimental.pallas import tpu as pltpu
from jax.sharding import PartitionSpec as P

HEADS = 64
HD = 128
KV_HEADS = 8
SPAN = 3

F32 = jnp.float32
BF16 = jnp.bfloat16


def document_index(doc_lengths, positions):
    doc_ends = jnp.cumsum(doc_lengths)
    counted = jnp.sum((positions[:, None] >= doc_ends[None, :]).astype(jnp.int32), axis=1)
    return jnp.where(positions < 0, -1, counted).astype(jnp.int32)


def from_behind(value, axis, steps):
    count = lax.axis_size(axis)
    pairs = [(source, source + steps) for source in range(0, count - steps)]
    if not pairs:
        return jnp.zeros_like(value)
    return lax.ppermute(value, axis, pairs)


def split_bf16(x):
    hi = x.astype(BF16)
    lo = (x - hi.astype(F32)).astype(BF16)
    return hi, lo


def dot_nt(a, b):
    return lax.dot_general(a, b, (((1,), (1,)), ((), ())), preferred_element_type=F32)


def head_cols(j):
    return slice(j * HD, (j + 1) * HD)


def doc_ends(len_ref, ndocs):
    ends = []
    total = jnp.int32(0)
    for i in range(ndocs):
        total = total + len_ref[i]
        ends.append(total)
    return ends


def doc_of(ends, pos):
    counted = jnp.zeros_like(pos)
    for e in ends:
        counted = counted + (pos >= e).astype(jnp.int32)
    return jnp.where(pos < 0, -1, counted)


def tail_kernel(hpb, ndocs, len_ref, start_ref, k_ref, v_ref, t_ref):
    rows = k_ref.shape[0]
    ends = doc_ends(len_ref, ndocs)
    start = start_ref[0]
    pos = start + lax.broadcasted_iota(jnp.int32, (rows, 1), 0)
    last = doc_of(ends, start + rows - 1)
    mask = (doc_of(ends, pos) == last).astype(BF16)
    for j in range(hpb):
        masked = v_ref[:, head_cols(j)] * mask
        t_ref[j] = lax.dot_general(
            k_ref[:, head_cols(j)], masked, (((0,), (0,)), ((), ())), preferred_element_type=F32
        )


def lin_local_kernel(hpb, ndocs, len_ref, start_ref, q_ref, k_ref, v_ref, lin_ref):
    rows = q_ref.shape[0]
    ends = doc_ends(len_ref, ndocs)
    start = start_ref[0]
    qpos = start + lax.broadcasted_iota(jnp.int32, (rows, 1), 0)
    kpos = start + lax.broadcasted_iota(jnp.int32, (1, rows), 1)
    visible = (doc_of(ends, qpos) == doc_of(ends, kpos)) & (kpos <= qpos)
    for j in range(hpb):
        scores = dot_nt(q_ref[:, head_cols(j)], k_ref[:, head_cols(j)])
        scores = jnp.where(visible, scores, 0.0)
        hi, lo = split_bf16(scores)
        v = v_ref[:, head_cols(j)]
        lin_ref[:, head_cols(j)] = jnp.dot(hi, v, preferred_element_type=F32) + jnp.dot(
            lo, v, preferred_element_type=F32
        )


def lin_finish_kernel(
    hpb, ndocs, len_ref, start_ref, q_ref, a_ref, c2_ref, b_ref, c1_ref, lin_ref, g_ref, o_ref
):
    rows = q_ref.shape[0]
    ends = doc_ends(len_ref, ndocs)
    start = start_ref[0]
    pos = start + lax.broadcasted_iota(jnp.int32, (rows, 1), 0)
    sees = (doc_of(ends, pos) == doc_of(ends, start - 1)).astype(F32)
    odd = lax.rem(start // rows, 2) == 1
    through_prev = (doc_of(ends, start - rows - 1) == doc_of(ends, start - 1)).astype(F32)
    through_prev2 = (
        doc_of(ends, start - 2 * rows - 1) == doc_of(ends, start - rows - 1)
    ).astype(F32)
    for j in range(hpb):
        on_even = b_ref[j] + through_prev * through_prev2 * c1_ref[j]
        state = jnp.where(odd, a_ref[j] + through_prev * c2_ref[j], on_even)
        hi, lo = split_bf16(state)
        q = q_ref[:, head_cols(j)]
        carried = jnp.dot(q, hi, preferred_element_type=F32) + jnp.dot(
            q, lo, preferred_element_type=F32
        )
        lin = lin_ref[:, head_cols(j)] + carried * sees
        mean_sq = jnp.mean(lin * lin, axis=-1, keepdims=True)
        normed = lin * lax.rsqrt(mean_sq + 1e-06) * g_ref[:, head_cols(j)]
        o_ref[:, head_cols(j)] = normed.astype(o_ref.dtype)


def col_spec(rows, width=HD):
    return pl.BlockSpec((rows, width), lambda h: (0, h))


def full_spec(shape):
    return pl.BlockSpec(shape, lambda h: (0,) * len(shape))


def params():
    return pltpu.CompilerParams(dimension_semantics=("arbitrary",))


def soft_kernel(blocks, hpb, ndocs, len_ref, start_ref, q_ref, *rest):
    per_kind = 2 * blocks - 1
    o_ref = rest[2 * per_kind]
    s_ref, mx_ref, tot_ref, acc_ref = rest[2 * per_kind + 1 :]
    rows = q_ref.shape[0]
    odd = lax.rem(start_ref[0] // rows, 2) == 1

    def pick(refs):
        picked = [lambda: refs[0][...]]
        for m in range(1, blocks):
            picked.append(
                lambda m=m: jnp.where(odd, refs[2 * m - 1][...], refs[2 * m][...])
            )
        return picked

    key_refs = pick(rest[0:per_kind])
    value_refs = pick(rest[per_kind : 2 * per_kind])
    scale = 1.0 / math.sqrt(HD)
    ends = doc_ends(len_ref, ndocs)
    start = start_ref[0]
    qpos = start + lax.broadcasted_iota(jnp.int32, (rows, 1), 0)
    kpos = start + lax.broadcasted_iota(jnp.int32, (1, rows), 1)
    dq = doc_of(ends, qpos)
    first_doc = doc_of(ends, start)
    q = jnp.concatenate([q_ref[:, head_cols(j)] for j in range(hpb)], axis=0)

    def block_scores(m):
        shifted = kpos - m * rows
        visible = dq == doc_of(ends, shifted)
        if m == 0:
            visible = visible & (shifted <= qpos)
        s = dot_nt(q, key_refs[m]()).reshape(hpb, rows, rows) * scale
        return jnp.where(visible[None], s, -1e30)

    def needed(m):
        return doc_of(ends, start - (m - 1) * rows - 1) == first_doc

    s0 = block_scores(0)
    s_ref[0] = s0
    mx_ref[...] = jnp.max(s0, axis=-1, keepdims=True)
    for m in range(1, blocks):

        @pl.when(needed(m))
        def _():
            s = block_scores(m)
            s_ref[m] = s
            mx_ref[...] = jnp.maximum(mx_ref[...], jnp.max(s, axis=-1, keepdims=True))

    def weighted(m):
        w = jnp.exp(s_ref[m] - mx_ref[...])
        part = jnp.sum(w, axis=-1, keepdims=True)
        term = jnp.dot(
            w.reshape(hpb * rows, rows).astype(BF16),
            value_refs[m](),
            preferred_element_type=F32,
        ).reshape(hpb, rows, HD)
        return part, term

    part, term = weighted(0)
    tot_ref[...] = part
    acc_ref[...] = term
    for m in range(1, blocks):

        @pl.when(needed(m))
        def _():
            part, term = weighted(m)
            tot_ref[...] += part
            acc_ref[...] += term

    out = acc_ref[...] / tot_ref[...]
    for j in range(hpb):
        o_ref[:, head_cols(j)] = out[j].astype(o_ref.dtype)


def smem_spec():
    return pl.BlockSpec(memory_space=pltpu.SMEM)


def body(lin_query, lin_key, lin_value, norm_gain, soft_query, soft_key, soft_value, doc_lengths):
    rows, width = lin_query.shape
    local_heads = width // HD
    ndocs = doc_lengths.shape[0]
    lengths = doc_lengths.astype(jnp.int32)
    shard_start = (lax.axis_index("ctx") * rows).astype(jnp.int32).reshape(1)
    ends = jnp.cumsum(lengths)

    def doc_at(pos):
        return jnp.where(pos < 0, -1, jnp.sum((pos >= ends).astype(jnp.int32)))

    through_own = (doc_at(shard_start[0] - 1) == doc_at(shard_start[0] + rows - 1)).astype(F32)

    head_devices = lax.axis_size("head")
    group_size = HEADS // KV_HEADS
    per_device = HEADS // head_devices
    kv_local = max(1, per_device // group_size)
    kv_table = (
        np.arange(head_devices)[:, None] * per_device // group_size + np.arange(kv_local)[None, :]
    ).reshape(-1)
    short_rows = soft_key.shape[0]

    def spread(field):
        if np.array_equal(kv_table, np.arange(KV_HEADS)):
            return field.reshape(short_rows, head_devices, kv_local * HD)
        taken = jnp.take(field.reshape(short_rows, KV_HEADS, HD), kv_table, axis=1)
        return taken.reshape(short_rows, head_devices, kv_local * HD)

    kv_packed = jnp.concatenate([spread(soft_key), spread(soft_value)], axis=2)
    kv_packed = kv_packed.reshape(short_rows, head_devices * 2 * kv_local * HD)
    own_kv = lax.all_to_all(kv_packed, "head", split_axis=1, concat_axis=0, tiled=True)
    mixed = lax.all_to_all(soft_query, "head", split_axis=1, concat_axis=0, tiled=True)
    kv_width = own_kv.shape[1]

    n_ctx = lax.axis_size("ctx")
    even_to_odd = [(c, c + 1) for c in range(0, n_ctx - 1, 2)]
    odd_to_next = [(c, c + 1) for c in range(1, n_ctx - 1, 2)]
    even_to_even = [(c, c + 2) for c in range(0, n_ctx - 2, 2)]
    is_odd = lax.rem(lax.axis_index("ctx"), 2) == 1

    def send(value, pairs):
        if not pairs:
            return jnp.zeros_like(value)
        return lax.ppermute(value, "ctx", pairs)

    kv_a = send(own_kv, even_to_odd)
    kv_b = send(jnp.concatenate([own_kv, kv_a], axis=1), odd_to_next)
    kv_c1 = send(kv_b[:, :kv_width], even_to_even)
    kv_c2 = send(kv_b, even_to_odd)
    odd_src = [(own_kv, 0), (kv_a, 0), (kv_c2, 0), (kv_c2, 2 * kv_local)]
    even_src = [(own_kv, 0), (kv_b, 0), (kv_b, 2 * kv_local), (kv_c1, 0)]

    lhpb = min(local_heads, group_size)
    lsteps = local_heads // lhpb
    lwide = lhpb * HD
    tail = pl.pallas_call(
        lambda *refs: tail_kernel(lhpb, ndocs, *refs),
        out_shape=jax.ShapeDtypeStruct((local_heads, HD, HD), F32),
        grid=(lsteps,),
        in_specs=[smem_spec(), smem_spec(), col_spec(rows, lwide), col_spec(rows, lwide)],
        out_specs=pl.BlockSpec((lhpb, HD, HD), lambda h: (h, 0, 0)),
        compiler_params=params(),
        cost_estimate=pl.CostEstimate(
            flops=2 * rows * HD * HD * local_heads,
            transcendentals=0,
            bytes_accessed=2 * rows * width * 2 + local_heads * HD * HD * 4,
        ),
    )(lengths, shard_start, lin_key, lin_value)

    lin_local = pl.pallas_call(
        lambda *refs: lin_local_kernel(lhpb, ndocs, *refs),
        out_shape=jax.ShapeDtypeStruct((rows, width), F32),
        grid=(lsteps,),
        in_specs=[
            smem_spec(),
            smem_spec(),
            col_spec(rows, lwide),
            col_spec(rows, lwide),
            col_spec(rows, lwide),
        ],
        out_specs=col_spec(rows, lwide),
        compiler_params=params(),
        cost_estimate=pl.CostEstimate(
            flops=6 * rows * rows * HD * local_heads,
            transcendentals=0,
            bytes_accessed=3 * rows * width * 2 + rows * width * 4,
        ),
    )(lengths, shard_start, lin_query, lin_key, lin_value)

    def through(shard):
        first = shard * rows
        return (doc_at(first - 1) == doc_at(first + rows - 1)).astype(F32)

    here = lax.axis_index("ctx")
    state_a = send(tail, even_to_odd)
    state_v = tail + through_own * state_a
    lin_local, state_v = lax.optimization_barrier((lin_local, state_v))
    state_b = send(state_v, odd_to_next)
    state_c1 = send(state_b, even_to_even)
    state_c2 = send(state_b, even_to_odd)

    blocks = SPAN + 1
    shpb = min(per_device, group_size)
    ssteps = per_device // shpb
    kv_index = lambda i: (i * shpb * kv_local) // per_device
    def kv_spec(offset, value):
        base = offset + (kv_local if value else 0)
        return pl.BlockSpec((rows, HD), lambda i: (0, base + kv_index(i)))

    kv_arrays, kv_specs = [], []
    for value in (False, True):
        for m in range(blocks):
            for source in ((odd_src[m],) if m == 0 else (odd_src[m], even_src[m])):
                kv_arrays.append(source[0])
                kv_specs.append(kv_spec(source[1], value))

    attended = pl.pallas_call(
        lambda *refs: soft_kernel(blocks, shpb, ndocs, *refs),
        out_shape=jax.ShapeDtypeStruct((rows, per_device * HD), BF16),
        grid=(ssteps,),
        in_specs=[smem_spec(), smem_spec(), col_spec(rows, shpb * HD)] + kv_specs,
        out_specs=col_spec(rows, shpb * HD),
        scratch_shapes=[
            pltpu.VMEM((blocks, shpb, rows, rows), F32),
            pltpu.VMEM((shpb, rows, 1), F32),
            pltpu.VMEM((shpb, rows, 1), F32),
            pltpu.VMEM((shpb, rows, HD), F32),
        ],
        compiler_params=pltpu.CompilerParams(
            dimension_semantics=("arbitrary",), vmem_limit_bytes=48 * 1024 * 1024
        ),
        cost_estimate=pl.CostEstimate(
            flops=4 * rows * rows * blocks * HD * per_device,
            transcendentals=rows * rows * blocks * per_device,
            bytes_accessed=rows * per_device * HD * 4 + 2 * blocks * rows * HD * 2 * per_device,
        ),
    )(lengths, shard_start, mixed, *kv_arrays)

    lightning_out = pl.pallas_call(
        lambda *refs: lin_finish_kernel(lhpb, ndocs, *refs),
        out_shape=jax.ShapeDtypeStruct((rows, width), BF16),
        grid=(lsteps,),
        in_specs=[
            smem_spec(),
            smem_spec(),
            col_spec(rows, lwide),
            pl.BlockSpec((lhpb, HD, HD), lambda h: (h, 0, 0)),
            pl.BlockSpec((lhpb, HD, HD), lambda h: (h, 0, 0)),
            pl.BlockSpec((lhpb, HD, HD), lambda h: (h, 0, 0)),
            pl.BlockSpec((lhpb, HD, HD), lambda h: (h, 0, 0)),
            col_spec(rows, lwide),
            pl.BlockSpec((1, lwide), lambda h: (0, h)),
        ],
        out_specs=col_spec(rows, lwide),
        compiler_params=params(),
        cost_estimate=pl.CostEstimate(
            flops=4 * rows * HD * HD * local_heads,
            transcendentals=rows * local_heads,
            bytes_accessed=rows * width * (2 + 4 + 2) + local_heads * HD * HD * 4,
        ),
    )(
        lengths,
        shard_start,
        lin_query,
        state_a,
        state_c2,
        state_b,
        state_c1,
        lin_local,
        norm_gain.reshape(1, width),
    )
    return (lightning_out, attended)


def solution(mesh):
    placed = (
        P("ctx", "head"),
        P("ctx", "head"),
        P("ctx", "head"),
        P("head"),
        P(("ctx", "head"), None),
        P(("ctx", "head"), None),
        P(("ctx", "head"), None),
        P(),
    )
    return jax.shard_map(
        body,
        mesh=mesh,
        in_specs=placed,
        out_specs=(P("ctx", "head"), P("ctx", "head")),
        check_vma=False,
    )
```

```python
import math

import jax
import jax.numpy as jnp
import numpy as np
from jax import lax
from jax.experimental import pallas as pl
from jax.experimental.pallas import tpu as pltpu
from jax.sharding import PartitionSpec as P

HEADS = 64
HD = 128
KV_HEADS = 8
SPAN = 3

F32 = jnp.float32
BF16 = jnp.bfloat16


def document_index(doc_lengths, positions):
    doc_ends = jnp.cumsum(doc_lengths)
    counted = jnp.sum((positions[:, None] >= doc_ends[None, :]).astype(jnp.int32), axis=1)
    return jnp.where(positions < 0, -1, counted).astype(jnp.int32)


def from_behind(value, axis, steps):
    count = lax.axis_size(axis)
    pairs = [(source, source + steps) for source in range(0, count - steps)]
    if not pairs:
        return jnp.zeros_like(value)
    return lax.ppermute(value, axis, pairs)


def split_bf16(x):
    hi = x.astype(BF16)
    lo = (x - hi.astype(F32)).astype(BF16)
    return hi, lo


def dot_nt(a, b):
    return lax.dot_general(a, b, (((1,), (1,)), ((), ())), preferred_element_type=F32)


def head_cols(j):
    return slice(j * HD, (j + 1) * HD)


def doc_ends(len_ref, ndocs):
    ends = []
    total = jnp.int32(0)
    for i in range(ndocs):
        total = total + len_ref[i]
        ends.append(total)
    return ends


def doc_of(ends, pos):
    counted = jnp.zeros_like(pos)
    for e in ends:
        counted = counted + (pos >= e).astype(jnp.int32)
    return jnp.where(pos < 0, -1, counted)


def tail_kernel(hpb, ndocs, len_ref, start_ref, k_ref, v_ref, t_ref):
    rows = k_ref.shape[0]
    ends = doc_ends(len_ref, ndocs)
    start = start_ref[0]
    pos = start + lax.broadcasted_iota(jnp.int32, (rows, 1), 0)
    last = doc_of(ends, start + rows - 1)
    mask = (doc_of(ends, pos) == last).astype(BF16)
    for j in range(hpb):
        masked = v_ref[:, head_cols(j)] * mask
        t_ref[j] = lax.dot_general(
            k_ref[:, head_cols(j)], masked, (((0,), (0,)), ((), ())), preferred_element_type=F32
        )


def lin_local_kernel(hpb, ndocs, len_ref, start_ref, q_ref, k_ref, v_ref, lin_ref):
    rows = q_ref.shape[0]
    ends = doc_ends(len_ref, ndocs)
    start = start_ref[0]
    qpos = start + lax.broadcasted_iota(jnp.int32, (rows, 1), 0)
    kpos = start + lax.broadcasted_iota(jnp.int32, (1, rows), 1)
    visible = (doc_of(ends, qpos) == doc_of(ends, kpos)) & (kpos <= qpos)
    for j in range(hpb):
        scores = dot_nt(q_ref[:, head_cols(j)], k_ref[:, head_cols(j)])
        scores = jnp.where(visible, scores, 0.0)
        hi, lo = split_bf16(scores)
        v = v_ref[:, head_cols(j)]
        lin_ref[:, head_cols(j)] = jnp.dot(hi, v, preferred_element_type=F32) + jnp.dot(
            lo, v, preferred_element_type=F32
        )


def lin_finish_kernel(
    hpb, ndocs, len_ref, start_ref, q_ref, a_ref, c2_ref, b_ref, c1_ref, lin_ref, g_ref, o_ref
):
    rows = q_ref.shape[0]
    ends = doc_ends(len_ref, ndocs)
    start = start_ref[0]
    pos = start + lax.broadcasted_iota(jnp.int32, (rows, 1), 0)
    sees = (doc_of(ends, pos) == doc_of(ends, start - 1)).astype(F32)
    odd = lax.rem(start // rows, 2) == 1
    through_prev = (doc_of(ends, start - rows - 1) == doc_of(ends, start - 1)).astype(F32)
    through_prev2 = (
        doc_of(ends, start - 2 * rows - 1) == doc_of(ends, start - rows - 1)
    ).astype(F32)
    for j in range(hpb):
        on_even = b_ref[j] + through_prev * through_prev2 * c1_ref[j]
        state = jnp.where(odd, a_ref[j] + through_prev * c2_ref[j], on_even)
        hi, lo = split_bf16(state)
        q = q_ref[:, head_cols(j)]
        carried = jnp.dot(q, hi, preferred_element_type=F32) + jnp.dot(
            q, lo, preferred_element_type=F32
        )
        lin = lin_ref[:, head_cols(j)] + carried * sees
        mean_sq = jnp.mean(lin * lin, axis=-1, keepdims=True)
        normed = lin * lax.rsqrt(mean_sq + 1e-06) * g_ref[:, head_cols(j)]
        o_ref[:, head_cols(j)] = normed.astype(o_ref.dtype)


def col_spec(rows, width=HD):
    return pl.BlockSpec((rows, width), lambda h: (0, h))


def full_spec(shape):
    return pl.BlockSpec(shape, lambda h: (0,) * len(shape))


def params():
    return pltpu.CompilerParams(dimension_semantics=("arbitrary",))


def soft_kernel(blocks, hpb, ndocs, len_ref, start_ref, q_ref, *rest):
    per_kind = 2 * blocks - 1
    o_ref = rest[2 * per_kind]
    s_ref, mx_ref, tot_ref, acc_ref = rest[2 * per_kind + 1 :]
    rows = q_ref.shape[0]
    odd = lax.rem(start_ref[0] // rows, 2) == 1

    def pick(refs):
        picked = [lambda: refs[0][...]]
        for m in range(1, blocks):
            picked.append(
                lambda m=m: jnp.where(odd, refs[2 * m - 1][...], refs[2 * m][...])
            )
        return picked

    key_refs = pick(rest[0:per_kind])
    value_refs = pick(rest[per_kind : 2 * per_kind])
    scale = 1.0 / math.sqrt(HD)
    ends = doc_ends(len_ref, ndocs)
    start = start_ref[0]
    qpos = start + lax.broadcasted_iota(jnp.int32, (rows, 1), 0)
    kpos = start + lax.broadcasted_iota(jnp.int32, (1, rows), 1)
    dq = doc_of(ends, qpos)
    first_doc = doc_of(ends, start)
    q = jnp.concatenate([q_ref[:, head_cols(j)] for j in range(hpb)], axis=0)

    def block_scores(m):
        shifted = kpos - m * rows
        visible = dq == doc_of(ends, shifted)
        if m == 0:
            visible = visible & (shifted <= qpos)
        s = dot_nt(q, key_refs[m]()).reshape(hpb, rows, rows) * scale
        return jnp.where(visible[None], s, -1e30)

    def needed(m):
        return doc_of(ends, start - (m - 1) * rows - 1) == first_doc

    s0 = block_scores(0)
    s_ref[0] = s0
    mx_ref[...] = jnp.max(s0, axis=-1, keepdims=True)
    for m in range(1, blocks):

        @pl.when(needed(m))
        def _():
            s = block_scores(m)
            s_ref[m] = s
            mx_ref[...] = jnp.maximum(mx_ref[...], jnp.max(s, axis=-1, keepdims=True))

    def weighted(m):
        w = jnp.exp(s_ref[m] - mx_ref[...])
        part = jnp.sum(w, axis=-1, keepdims=True)
        term = jnp.dot(
            w.reshape(hpb * rows, rows).astype(BF16),
            value_refs[m](),
            preferred_element_type=F32,
        ).reshape(hpb, rows, HD)
        return part, term

    part, term = weighted(0)
    tot_ref[...] = part
    acc_ref[...] = term
    for m in range(1, blocks):

        @pl.when(needed(m))
        def _():
            part, term = weighted(m)
            tot_ref[...] += part
            acc_ref[...] += term

    out = acc_ref[...] / tot_ref[...]
    for j in range(hpb):
        o_ref[:, head_cols(j)] = out[j].astype(o_ref.dtype)


def smem_spec():
    return pl.BlockSpec(memory_space=pltpu.SMEM)


def body(lin_query, lin_key, lin_value, norm_gain, soft_query, soft_key, soft_value, doc_lengths):
    rows, width = lin_query.shape
    local_heads = width // HD
    ndocs = doc_lengths.shape[0]
    lengths = doc_lengths.astype(jnp.int32)
    shard_start = (lax.axis_index("ctx") * rows).astype(jnp.int32).reshape(1)
    ends = jnp.cumsum(lengths)

    def doc_at(pos):
        return jnp.where(pos < 0, -1, jnp.sum((pos >= ends).astype(jnp.int32)))

    through_own = (doc_at(shard_start[0] - 1) == doc_at(shard_start[0] + rows - 1)).astype(F32)

    head_devices = lax.axis_size("head")
    group_size = HEADS // KV_HEADS
    per_device = HEADS // head_devices
    kv_local = max(1, per_device // group_size)
    kv_table = (
        np.arange(head_devices)[:, None] * per_device // group_size + np.arange(kv_local)[None, :]
    ).reshape(-1)
    short_rows = soft_key.shape[0]

    def spread(field):
        if np.array_equal(kv_table, np.arange(KV_HEADS)):
            return field.reshape(short_rows, head_devices, kv_local * HD)
        taken = jnp.take(field.reshape(short_rows, KV_HEADS, HD), kv_table, axis=1)
        return taken.reshape(short_rows, head_devices, kv_local * HD)

    kv_packed = jnp.concatenate([spread(soft_key), spread(soft_value)], axis=2)
    kv_packed = kv_packed.reshape(short_rows, head_devices * 2 * kv_local * HD)
    own_kv = lax.all_to_all(kv_packed, "head", split_axis=1, concat_axis=0, tiled=True)
    mixed = lax.all_to_all(soft_query, "head", split_axis=1, concat_axis=0, tiled=True)
    kv_width = own_kv.shape[1]

    n_ctx = lax.axis_size("ctx")
    even_to_odd = [(c, c + 1) for c in range(0, n_ctx - 1, 2)]
    odd_to_next = [(c, c + 1) for c in range(1, n_ctx - 1, 2)]
    even_to_even = [(c, c + 2) for c in range(0, n_ctx - 2, 2)]
    is_odd = lax.rem(lax.axis_index("ctx"), 2) == 1

    def send(value, pairs):
        if not pairs:
            return jnp.zeros_like(value)
        return lax.ppermute(value, "ctx", pairs)

    kv_a = send(own_kv, even_to_odd)
    kv_b = send(jnp.concatenate([own_kv, kv_a], axis=1), odd_to_next)
    kv_c1 = send(kv_b[:, :kv_width], even_to_even)
    kv_c2 = send(kv_b, even_to_odd)
    odd_src = [(own_kv, 0), (kv_a, 0), (kv_c2, 0), (kv_c2, 2 * kv_local)]
    even_src = [(own_kv, 0), (kv_b, 0), (kv_b, 2 * kv_local), (kv_c1, 0)]

    lhpb = min(local_heads, group_size)
    lsteps = local_heads // lhpb
    lwide = lhpb * HD
    tail = pl.pallas_call(
        lambda *refs: tail_kernel(lhpb, ndocs, *refs),
        out_shape=jax.ShapeDtypeStruct((local_heads, HD, HD), F32),
        grid=(lsteps,),
        in_specs=[smem_spec(), smem_spec(), col_spec(rows, lwide), col_spec(rows, lwide)],
        out_specs=pl.BlockSpec((lhpb, HD, HD), lambda h: (h, 0, 0)),
        compiler_params=params(),
        cost_estimate=pl.CostEstimate(
            flops=2 * rows * HD * HD * local_heads,
            transcendentals=0,
            bytes_accessed=2 * rows * width * 2 + local_heads * HD * HD * 4,
        ),
    )(lengths, shard_start, lin_key, lin_value)

    lin_local = pl.pallas_call(
        lambda *refs: lin_local_kernel(lhpb, ndocs, *refs),
        out_shape=jax.ShapeDtypeStruct((rows, width), F32),
        grid=(lsteps,),
        in_specs=[
            smem_spec(),
            smem_spec(),
            col_spec(rows, lwide),
            col_spec(rows, lwide),
            col_spec(rows, lwide),
        ],
        out_specs=col_spec(rows, lwide),
        compiler_params=params(),
        cost_estimate=pl.CostEstimate(
            flops=6 * rows * rows * HD * local_heads,
            transcendentals=0,
            bytes_accessed=3 * rows * width * 2 + rows * width * 4,
        ),
    )(lengths, shard_start, lin_query, lin_key, lin_value)

    def through(shard):
        first = shard * rows
        return (doc_at(first - 1) == doc_at(first + rows - 1)).astype(F32)

    here = lax.axis_index("ctx")
    state_a = send(tail, even_to_odd)
    state_v = tail + through_own * state_a
    state_b = send(state_v, odd_to_next)
    lin_local, state_b = lax.optimization_barrier((lin_local, state_b))
    state_c1 = send(state_b, even_to_even)
    state_c2 = send(state_b, even_to_odd)

    blocks = SPAN + 1
    shpb = min(per_device, group_size)
    ssteps = per_device // shpb
    kv_index = lambda i: (i * shpb * kv_local) // per_device
    def kv_spec(offset, value):
        base = offset + (kv_local if value else 0)
        return pl.BlockSpec((rows, HD), lambda i: (0, base + kv_index(i)))

    kv_arrays, kv_specs = [], []
    for value in (False, True):
        for m in range(blocks):
            for source in ((odd_src[m],) if m == 0 else (odd_src[m], even_src[m])):
                kv_arrays.append(source[0])
                kv_specs.append(kv_spec(source[1], value))

    attended = pl.pallas_call(
        lambda *refs: soft_kernel(blocks, shpb, ndocs, *refs),
        out_shape=jax.ShapeDtypeStruct((rows, per_device * HD), BF16),
        grid=(ssteps,),
        in_specs=[smem_spec(), smem_spec(), col_spec(rows, shpb * HD)] + kv_specs,
        out_specs=col_spec(rows, shpb * HD),
        scratch_shapes=[
            pltpu.VMEM((blocks, shpb, rows, rows), F32),
            pltpu.VMEM((shpb, rows, 1), F32),
            pltpu.VMEM((shpb, rows, 1), F32),
            pltpu.VMEM((shpb, rows, HD), F32),
        ],
        compiler_params=pltpu.CompilerParams(
            dimension_semantics=("arbitrary",), vmem_limit_bytes=48 * 1024 * 1024
        ),
        cost_estimate=pl.CostEstimate(
            flops=4 * rows * rows * blocks * HD * per_device,
            transcendentals=rows * rows * blocks * per_device,
            bytes_accessed=rows * per_device * HD * 4 + 2 * blocks * rows * HD * 2 * per_device,
        ),
    )(lengths, shard_start, mixed, *kv_arrays)

    lightning_out = pl.pallas_call(
        lambda *refs: lin_finish_kernel(lhpb, ndocs, *refs),
        out_shape=jax.ShapeDtypeStruct((rows, width), BF16),
        grid=(lsteps,),
        in_specs=[
            smem_spec(),
            smem_spec(),
            col_spec(rows, lwide),
            pl.BlockSpec((lhpb, HD, HD), lambda h: (h, 0, 0)),
            pl.BlockSpec((lhpb, HD, HD), lambda h: (h, 0, 0)),
            pl.BlockSpec((lhpb, HD, HD), lambda h: (h, 0, 0)),
            pl.BlockSpec((lhpb, HD, HD), lambda h: (h, 0, 0)),
            col_spec(rows, lwide),
            pl.BlockSpec((1, lwide), lambda h: (0, h)),
        ],
        out_specs=col_spec(rows, lwide),
        compiler_params=params(),
        cost_estimate=pl.CostEstimate(
            flops=4 * rows * HD * HD * local_heads,
            transcendentals=rows * local_heads,
            bytes_accessed=rows * width * (2 + 4 + 2) + local_heads * HD * HD * 4,
        ),
    )(
        lengths,
        shard_start,
        lin_query,
        state_a,
        state_c2,
        state_b,
        state_c1,
        lin_local,
        norm_gain.reshape(1, width),
    )
    return (lightning_out, attended)


def solution(mesh):
    placed = (
        P("ctx", "head"),
        P("ctx", "head"),
        P("ctx", "head"),
        P("head"),
        P(("ctx", "head"), None),
        P(("ctx", "head"), None),
        P(("ctx", "head"), None),
        P(),
    )
    return jax.shard_map(
        body,
        mesh=mesh,
        in_specs=placed,
        out_specs=(P("ctx", "head"), P("ctx", "head")),
        check_vma=False,
    )
```
